256 devices in a mesh: dp: 32 (over x, y, core), head: 8 (over z).
Axes of the slice: x: 4, y: 4, z: 8, core: 2. Of those that a mesh axis runs over, the one named last changes fastest.
Arguments:
- hidden: bfloat16 [16384, 2048], P('dp'), may hold values from -9 to 9
- parents: int32 [256, 64], P('dp'), may hold values from -1 to 62, as said below
- owner_slot: int32 [256], replicated, may hold values from 0 to 255, as said below
- slot_lengths: int32 [256], P('dp'), may hold values from 65 to 496, as said below
- accepted_path: int32 [256, 16], P('dp'), may hold values from 0 to 63, as said below
- accepted_count: int32 [256], P('dp'), may hold values from 1 to 16, as said below
- cache_keys: bfloat16 [256, 512, 2048], P('dp', None, 'head'), may hold values from -82 to 82
- cache_values: bfloat16 [256, 512, 2048], P('dp', None, 'head'), may hold values from -5 to 5
- w_query: bfloat16 [2048, 2048], P(None, 'head'), may hold values from -0.125 to 0.125
- b_query: float32 [2048], P('head'), may hold values from -3 to 3
- w_key: bfloat16 [2048, 2048], P(None, 'head'), may hold values from -0.25 to 0.25
- w_value: bfloat16 [2048, 2048], P(None, 'head'), may hold values from -0.125 to 0.125
- b_value: float32 [2048], P('head'), may hold values from -3 to 3
- w_out: bfloat16 [2048, 2048], P('head'), may hold values from -0.5 to 0.5
- b_out: float32 [2048], replicated, may hold values from -3 to 3
- first_gain: float32 [2048], replicated, may hold values from 0.48 to 2.25
- first_shift: float32 [2048], replicated, may hold values from -2 to 2
- w_up: bfloat16 [2048, 4096], P(None, 'head'), may hold values from -0.125 to 0.125
- b_up: float32 [4096], P('head'), may hold values from -3 to 3
- w_down: bfloat16 [4096, 2048], P('head'), may hold values from -0.09375 to 0.09375
- b_down: float32 [2048], replicated, may hold values from -3 to 3
- second_gain: float32 [2048], replicated, may hold values from 0.5 to 1.5
- second_shift: float32 [2048], replicated, may hold values from -2 to 2
Outputs:
- layer_out: bfloat16 [16384, 2048], P('dp', 'head')
- new_keys: bfloat16 [256, 16, 2048], P('dp', None, 'head')
- new_values: bfloat16 [256, 16, 2048], P('dp', None, 'head')
The draws below stay inside these ranges and needn't reach their ends.
Inputs may be any that keep to these rules, and one draw needn't show every extreme that they name: owner_slot is a permutation of the 256 slots; slot s lies on dp index s // 8. Of the 8 requests of one dp index, at most 2 have their slots on one dp index, and on every dp index some 2 do. `slot_lengths`: some slot is filled to exactly 496 positions. parents[r, 0] = -1 and 0 <= parents[r, i] < i for i >= 1. For k < accepted_count[r], accepted_path[r, k] is the node at depth k on the way from the root to some node of request r's tree (so entry 0 is node 0); later entries are arbitrary node indices. `accepted_count`: some request has the full 16 entries.
All inputs are finite; a program needn't handle non-finite values.
Results may differ from the reference program's by a relative error of at most 0.018.
Values may be sent and summed in bfloat16 or wider, within the bound.
No kernel may reach another device: no remote copies, remote signals or barrier semaphores. Data moves between devices by JAX's collectives and lax.ppermute only.
A program may use at most 64 MiB of HBM per device.

```python
import math
import jax
import jax.numpy as jnp
from jax import lax

D = 2048
HEADS = 16
HD = 128
FF = 4096
REQ_DEV = 8
DRAFT = 64
PATH = 16
CAP = 512
REQS = 256
TOKENS = 16384
N_HEAD = 8


def tree_draw(key):
    key_parent = jax.random.fold_in(key, 101)
    key_target = jax.random.fold_in(key, 102)
    key_count = jax.random.fold_in(key, 103)
    key_fullest = jax.random.fold_in(key, 104)
    key_filler = jax.random.fold_in(key, 105)
    nodes = jnp.arange(DRAFT, dtype=jnp.int32)
    lowest = jnp.maximum(nodes - 3, 0)
    spans = jnp.maximum(nodes - lowest, 1)
    picks = jax.random.randint(key_parent, (REQS, DRAFT), 0, 3, dtype=jnp.int32)
    parent = lowest[None, :] + picks % spans[None, :]
    parent = jnp.where(nodes[None, :] == 0, -1, parent).astype(jnp.int32)

    def deepen(index, depth):
        above = jnp.maximum(parent[:, index], 0)
        level = jnp.take_along_axis(depth, above[:, None], 1)[:, 0] + 1
        return depth.at[:, index].set(level)
    depth = lax.fori_loop(1, DRAFT, deepen, jnp.zeros((REQS, DRAFT), jnp.int32))
    target = jax.random.randint(key_target, (REQS,), DRAFT - 8, DRAFT, dtype=jnp.int32)
    levels = jnp.arange(PATH, dtype=jnp.int32)[None, :]

    def climb(step, node_at):
        node_depth = jnp.take_along_axis(depth, node_at, 1)
        upward = jnp.take_along_axis(parent, node_at, 1)
        return jnp.where(node_depth > levels, upward, node_at)
    chain = lax.fori_loop(0, DRAFT, climb, jnp.broadcast_to(target[:, None], (REQS, PATH)).astype(jnp.int32))
    counted = jax.random.randint(key_count, (REQS,), 1, PATH + 1, dtype=jnp.int32)
    fullest = jax.random.randint(key_fullest, (), 0, REQS, dtype=jnp.int32)
    counted = jnp.where(jnp.arange(REQS, dtype=jnp.int32) == fullest, PATH, counted).astype(jnp.int32)
    filler = jax.random.randint(key_filler, (REQS, PATH), 0, DRAFT, dtype=jnp.int32)
    paths = jnp.where(levels < counted[:, None], chain, filler).astype(jnp.int32)
    return (parent, paths, counted)


def draw_parents(key, part):
    return tree_draw(key)[0]


def draw_accepted_path(key, part):
    return tree_draw(key)[1]


def draw_accepted_count(key, part):
    return tree_draw(key)[2]


def draw_owner_slot(key, part):
    shards = REQS // REQ_DEV
    key_base = jax.random.fold_in(key, 201)
    key_shift = jax.random.fold_in(key, 202)
    key_slot = jax.random.fold_in(key, 203)
    key_order = jax.random.fold_in(key, 204)
    key_anchor = jax.random.fold_in(key, 205)
    base = jax.random.permutation(key_base, shards).astype(jnp.int32)
    anchor = jax.random.randint(key_anchor, (), 0, shards, dtype=jnp.int32)
    opposite = (anchor + shards // 2) % shards
    spots = jnp.arange(shards, dtype=jnp.int32)
    holder = jnp.sum(jnp.where(base == opposite, spots, 0)).astype(jnp.int32)
    moved = base[anchor]
    base = jnp.where(spots == holder, moved, base)
    base = jnp.where(spots == anchor, opposite, base).astype(jnp.int32)
    extra = (jax.random.permutation(key_shift, shards - 1).astype(jnp.int32) + 1)[:REQ_DEV - 2]
    shifts = jnp.concatenate([jnp.zeros((2,), jnp.int32), extra])
    senders = jnp.arange(shards, dtype=jnp.int32)[:, None]
    classes = jnp.arange(REQ_DEV, dtype=jnp.int32)[None, :]
    target = base[(senders + shifts[None, :]) % shards]
    slot_score = jax.random.randint(key_slot, (shards, REQ_DEV), 0, 1 << 20, dtype=jnp.int32) * REQ_DEV + classes
    within = jnp.argsort(slot_score, axis=1).astype(jnp.int32)
    slots = target * REQ_DEV + within[target, classes]
    order_score = jax.random.randint(key_order, (shards, REQ_DEV), 0, 1 << 20, dtype=jnp.int32) * REQ_DEV + classes
    placing = jnp.argsort(order_score, axis=1).astype(jnp.int32)
    owners = jnp.zeros((shards, REQ_DEV), jnp.int32).at[senders, placing].set(slots)
    return owners.reshape(REQS)


def draw_slot_lengths(key, part):
    key_kind = jax.random.fold_in(key, 301)
    key_long = jax.random.fold_in(key, 302)
    key_short = jax.random.fold_in(key, 303)
    key_fullest = jax.random.fold_in(key, 304)
    longish = jax.random.randint(key_kind, (REQS,), 0, 20, dtype=jnp.int32) < 7
    long_length = CAP - PATH - jax.random.randint(key_long, (REQS,), 0, CAP // 8, dtype=jnp.int32)
    short_length = CAP // 4 - jax.random.randint(key_short, (REQS,), 0, CAP // 8, dtype=jnp.int32)
    lengths = jnp.where(longish, long_length, short_length)
    fullest = jax.random.randint(key_fullest, (), 0, REQS, dtype=jnp.int32)
    return jnp.where(jnp.arange(REQS, dtype=jnp.int32) == fullest, CAP - PATH, lengths).astype(jnp.int32)


def draw_hidden(key, part):
    key_values = jax.random.fold_in(key, 401)
    key_rough = jax.random.fold_in(key, 402)
    column = jnp.arange(D, dtype=jnp.float32) / D
    rough = jax.random.uniform(key_rough, (D,), jnp.float32, 0.8, 1.25)
    scaling = 0.6 * jnp.power(3.0, column) * rough
    values = jnp.clip(jax.random.normal(key_values, (TOKENS, D), jnp.float32), -4.0, 4.0)
    return (values * scaling[None, :]).astype(jnp.bfloat16)


def draw_cache_keys(key, part):
    key_values = jax.random.fold_in(key, 501)
    shape = (REQS, CAP, HEADS * HD)
    return jnp.clip(jax.random.normal(key_values, shape, jnp.float32), -4.0, 4.0).astype(jnp.bfloat16)


def draw_first_gain(key, part):
    column = jnp.arange(D, dtype=jnp.float32) / D
    rough = jax.random.uniform(jax.random.fold_in(key, 601), (D,), jnp.float32, 0.8, 1.25)
    return 0.6 * jnp.power(3.0, column) * rough


def steps_of(own_key, shape, cuts, least, largest):
    factor_of, own = 1.0, jax.random.fold_in(own_key, 6)
    for dim, shards_of in cuts:
        draws = jnp.exp(jax.random.uniform(jax.random.fold_in(own, dim), (shards_of,), jnp.float32, least / len(cuts), largest / len(cuts)))
        factor_of = factor_of * jnp.repeat(draws, shape[dim] // shards_of).reshape([-1 if axis == dim else 1 for axis in range(len(shape))])
    return factor_of


def normal_values(own_key, extent, scale, most, cuts=(), kind=jnp.bfloat16):
    result = jax.random.normal(own_key, extent, jnp.float32) * scale
    if len(cuts) > 0:
        result = steps_of(own_key, extent, cuts, -0.22, 0.18) * result
    return jnp.clip(result, min=-most, max=most).astype(kind)


def setup_inputs(seed: int = 0) -> dict:
    key_list = jax.random.split(jax.random.key(seed), 24)
    hidden = draw_hidden(jax.random.fold_in(key_list[23], 71), 0)
    parents = draw_parents(jax.random.fold_in(key_list[23], 71), 0)
    owner_slot = draw_owner_slot(jax.random.fold_in(key_list[23], 71), 0)
    slot_lengths = draw_slot_lengths(jax.random.fold_in(key_list[23], 71), 0)
    accepted_path = draw_accepted_path(jax.random.fold_in(key_list[23], 71), 0)
    accepted_count = draw_accepted_count(jax.random.fold_in(key_list[23], 71), 0)
    cache_keys = draw_cache_keys(jax.random.fold_in(key_list[23], 71), 0)
    cache_values = normal_values(key_list[7], (REQS, CAP, HEADS * HD), 1.0, 5.0, ((0, 32), (2, 8)))
    w_query = normal_values(key_list[8], (D, HEADS * HD), D ** -0.5, 0.125, ((1, 8),))
    b_query = normal_values(key_list[9], (HEADS * HD,), 0.5, 3.0, ((0, 8),), jnp.float32)
    w_key = normal_values(key_list[10], (D, HEADS * HD), (D // 4) ** -0.5, 0.25, ((1, 8),))
    w_value = normal_values(key_list[11], (D, HEADS * HD), D ** -0.5, 0.125, ((1, 8),))
    b_value = normal_values(key_list[12], (HEADS * HD,), 0.5, 3.0, ((0, 8),), jnp.float32)
    w_out = normal_values(key_list[13], (HEADS * HD, D), (HEADS * HD // 16) ** -0.5, 0.5, ((0, 8),))
    b_out = normal_values(key_list[14], (D,), 0.5, 3.0, (), jnp.float32)
    first_gain = draw_first_gain(jax.random.fold_in(key_list[23], 71), 0)
    first_shift = normal_values(key_list[16], (D,), 0.3, 2.0, (), jnp.float32)
    w_up = normal_values(key_list[17], (D, FF), D ** -0.5, 0.125, ((1, 8),))
    b_up = normal_values(key_list[18], (FF,), 0.5, 3.0, ((0, 8),), jnp.float32)
    w_down = normal_values(key_list[19], (FF, D), FF ** -0.5, 0.09375, ((0, 8),))
    b_down = normal_values(key_list[20], (D,), 0.5, 3.0, (), jnp.float32)
    second_gain = jnp.clip(1.0 + 0.1 * jax.random.normal(key_list[21], (D,), jnp.float32), 0.5, 1.5)
    second_shift = normal_values(key_list[22], (D,), 0.3, 2.0, (), jnp.float32)
    return {"hidden": hidden, "parents": parents, "owner_slot": owner_slot, "slot_lengths": slot_lengths, "accepted_path": accepted_path, "accepted_count": accepted_count, "cache_keys": cache_keys, "cache_values": cache_values, "w_query": w_query, "b_query": b_query, "w_key": w_key, "w_value": w_value, "b_value": b_value, "w_out": w_out, "b_out": b_out, "first_gain": first_gain, "first_shift": first_shift, "w_up": w_up, "b_up": b_up, "w_down": w_down, "b_down": b_down, "second_gain": second_gain, "second_shift": second_shift}


EPSILON = 1e-05

def ancestry(parent_row, draft):
    nodes = jnp.arange(draft, dtype=jnp.int32)
    reach = (parent_row[:, None] == nodes[None, :]).astype(jnp.float32) + jnp.eye(draft, dtype=jnp.float32)
    for turn in range(max(1, draft.bit_length())):
        reach = jnp.minimum(jnp.dot(reach, reach, precision=lax.Precision.HIGHEST), 1.0)
    return reach > 0.5

def normalize(mixed, gain, shift):
    center = lax.optimization_barrier(jnp.mean(mixed, axis=-1, keepdims=True))
    square = lax.optimization_barrier(jnp.mean(mixed * mixed, axis=-1, keepdims=True))
    return (mixed - center) * lax.rsqrt(square - center * center + EPSILON) * gain + shift

def reference(hidden, parents, owner_slot, slot_lengths, accepted_path, accepted_count, cache_keys, cache_values, w_query, b_query, w_key, w_value, b_value, w_out, b_out, first_gain, first_shift, w_up, b_up, w_down, b_down, second_gain, second_shift):
    requests = owner_slot.shape[0]
    draft = parents.shape[1]
    all_width = w_query.shape[1]
    heads = all_width // HD
    tokens = hidden.shape[0]
    scale = 1.0 / math.sqrt(HD)
    highest = lax.Precision.HIGHEST
    queries = (jnp.dot(hidden, w_query, preferred_element_type=jnp.float32) + b_query).astype(jnp.bfloat16)
    key_rows = jnp.dot(hidden, w_key, preferred_element_type=jnp.float32).astype(jnp.bfloat16)
    value_rows = (jnp.dot(hidden, w_value, preferred_element_type=jnp.float32) + b_value).astype(jnp.bfloat16)

    def verify(request):
        slot_index = owner_slot[request]
        length = slot_lengths[slot_index]
        query_block = lax.dynamic_slice_in_dim(queries, request * draft, draft, 0).reshape(draft, heads, HD).astype(jnp.float32)
        keys_slot = cache_keys[slot_index].reshape(CAP, heads, HD).astype(jnp.float32)
        values_slot = cache_values[slot_index].reshape(CAP, heads, HD).astype(jnp.float32)
        scores = jnp.einsum('qhd,khd->hqk', query_block, keys_slot, precision=highest) * scale
        living = jnp.arange(CAP, dtype=jnp.int32) < length
        scores = jnp.where(living[None, None, :], scores, -jnp.inf)
        cache_top = lax.optimization_barrier(jnp.max(scores, axis=2, keepdims=True))
        cache_exp = jnp.exp(scores - cache_top)
        cache_total = lax.optimization_barrier(jnp.sum(cache_exp, axis=2, keepdims=True))
        cache_probs = lax.optimization_barrier(cache_exp.astype(jnp.bfloat16)).astype(jnp.float32)
        cache_mix = jnp.einsum('hqk,khd->qhd', cache_probs, values_slot, precision=highest)
        cache_part = (cache_mix / jnp.transpose(cache_total, (1, 0, 2))).astype(jnp.bfloat16)
        cache_part = lax.optimization_barrier(cache_part).astype(jnp.float32)
        cache_lse = jnp.transpose((cache_top + jnp.log(cache_total))[..., 0])[..., None]
        lineage = ancestry(parents[request], draft)
        tree_keys = lax.dynamic_slice_in_dim(key_rows, request * draft, draft, 0).reshape(draft, heads, HD).astype(jnp.float32)
        tree_values = lax.dynamic_slice_in_dim(value_rows, request * draft, draft, 0).reshape(draft, heads, HD).astype(jnp.float32)
        tree_scores = jnp.einsum('qhd,khd->hqk', query_block, tree_keys, precision=highest) * scale
        tree_scores = jnp.where(lineage[None], tree_scores, -jnp.inf)
        tree_top = lax.optimization_barrier(jnp.max(tree_scores, axis=2, keepdims=True))
        tree_exp = jnp.exp(tree_scores - tree_top)
        tree_total = lax.optimization_barrier(jnp.sum(tree_exp, axis=2, keepdims=True))
        tree_probs = lax.optimization_barrier(tree_exp.astype(jnp.bfloat16)).astype(jnp.float32)
        tree_part = jnp.einsum('hqk,khd->qhd', tree_probs, tree_values, precision=highest) / jnp.transpose(tree_total, (1, 0, 2))
        tree_lse = jnp.transpose((tree_top + jnp.log(tree_total))[..., 0])[..., None]
        larger = jnp.maximum(cache_lse, tree_lse)
        cache_share = jnp.exp(cache_lse - larger)
        tree_share = jnp.exp(tree_lse - larger)
        attended = (cache_share * cache_part + tree_share * tree_part) / (cache_share + tree_share)
        return attended.astype(jnp.bfloat16).reshape(draft, all_width)
    attended = lax.map(verify, jnp.arange(requests, dtype=jnp.int32)).reshape(tokens, all_width)
    group = all_width // N_HEAD
    attention_sum = jnp.zeros((tokens, D), jnp.float32)
    for group_index in range(N_HEAD):
        term = jnp.dot(attended[:, group_index * group:(group_index + 1) * group], w_out[group_index * group:(group_index + 1) * group], preferred_element_type=jnp.float32)
        attention_sum = attention_sum + lax.optimization_barrier(term.astype(jnp.bfloat16)).astype(jnp.float32)
    first_normed = normalize(attention_sum + b_out + hidden.astype(jnp.float32), first_gain, first_shift).astype(jnp.bfloat16)
    inner = jax.nn.gelu(jnp.dot(first_normed, w_up, preferred_element_type=jnp.float32) + b_up, approximate=True).astype(jnp.bfloat16)
    units = inner.shape[1] // N_HEAD
    down_sum = jnp.zeros((tokens, D), jnp.float32)
    for group_index in range(N_HEAD):
        term = jnp.dot(inner[:, group_index * units:(group_index + 1) * units], w_down[group_index * units:(group_index + 1) * units], preferred_element_type=jnp.float32)
        down_sum = down_sum + lax.optimization_barrier(term.astype(jnp.bfloat16)).astype(jnp.float32)
    layer_out = normalize(down_sum + b_down + first_normed.astype(jnp.float32), second_gain, second_shift).astype(jnp.bfloat16)
    levels = jnp.arange(accepted_path.shape[1], dtype=jnp.int32)
    chosen = jnp.arange(requests, dtype=jnp.int32)[:, None] * draft + accepted_path
    usable = (levels[None, :] < accepted_count[:, None])[..., None]
    picked_keys = jnp.where(usable, key_rows[chosen], jnp.zeros((), jnp.bfloat16))
    picked_values = jnp.where(usable, value_rows[chosen], jnp.zeros((), jnp.bfloat16))
    new_keys = jnp.zeros_like(picked_keys).at[owner_slot].set(picked_keys)
    new_values = jnp.zeros_like(picked_values).at[owner_slot].set(picked_values)
    return (layer_out, new_keys, new_values)
```

```python
import math

import jax
import jax.numpy as jnp
from jax import lax
from jax.sharding import PartitionSpec as P

HD = 128
PEER_MOST = 2


EPSILON = 1e-05


def ancestry(parent_row, draft):
    nodes = jnp.arange(draft, dtype=jnp.int32)
    reach = (parent_row[:, None] == nodes[None, :]).astype(jnp.float32) + jnp.eye(
        draft, dtype=jnp.float32
    )
    for turn in range(max(1, draft.bit_length())):
        reach = jnp.minimum(jnp.dot(reach, reach, precision=lax.Precision.HIGHEST), 1.0)
    return reach > 0.5


def normalize(mixed, gain, shift):
    center = jnp.mean(mixed, axis=-1, keepdims=True)
    square = jnp.mean(mixed * mixed, axis=-1, keepdims=True)
    return (mixed - center) * lax.rsqrt(square - center * center + EPSILON) * gain + shift


def normalize_shared(mixed, sums, gain, shift, model_width):
    center = (sums[0] / model_width)[:, None]
    square = (sums[1] / model_width)[:, None]
    return (mixed - center) * lax.rsqrt(square - center * center + EPSILON) * gain + shift


def split_three(values):
    high = values.astype(jnp.bfloat16)
    rest = values - high.astype(jnp.float32)
    middle = rest.astype(jnp.bfloat16)
    low = (rest - middle.astype(jnp.float32)).astype(jnp.bfloat16)
    return jnp.stack([high, middle, low], axis=1)


def join_three(pieces):
    wide = pieces.astype(jnp.float32)
    return wide[:, 0] + (wide[:, 1] + wide[:, 2])


def local(
    hidden,
    parents,
    owner_slot,
    slot_lengths,
    accepted_path,
    accepted_count,
    cache_keys,
    cache_values,
    w_query,
    b_query,
    w_key,
    w_value,
    b_value,
    w_out,
    b_out,
    first_gain,
    first_shift,
    w_up,
    b_up,
    w_down,
    b_down,
    second_gain,
    second_shift,
):
    requests = parents.shape[0]
    draft = parents.shape[1]
    tokens = hidden.shape[0]
    model_width = hidden.shape[1]
    width = w_query.shape[1]
    local_heads = width // HD
    capacity = cache_keys.shape[1]
    block = min(capacity, 256)
    shards = lax.axis_size("dp")
    myself = lax.axis_index("dp")
    scale = 1.0 / math.sqrt(HD)
    queries = (jnp.dot(hidden, w_query, preferred_element_type=jnp.float32) + b_query).astype(
        jnp.bfloat16
    )
    key_rows = jnp.dot(hidden, w_key, preferred_element_type=jnp.float32).astype(jnp.bfloat16)
    value_rows = (jnp.dot(hidden, w_value, preferred_element_type=jnp.float32) + b_value).astype(
        jnp.bfloat16
    )
    local_ids = jnp.arange(requests, dtype=jnp.int32)
    levels = jnp.arange(accepted_path.shape[1], dtype=jnp.int32)
    chosen = local_ids[:, None] * draft + accepted_path
    usable = (levels[None, :] < accepted_count[:, None])[..., None]
    kept_keys = jnp.where(usable, key_rows[chosen], jnp.zeros((), jnp.bfloat16))
    kept_values = jnp.where(usable, value_rows[chosen], jnp.zeros((), jnp.bfloat16))
    tree_queries = queries.reshape(requests, draft, local_heads, HD)
    tree_keys = key_rows.reshape(requests, draft, local_heads, HD)
    tree_values = value_rows.reshape(requests, draft, local_heads, HD)
    lineage = jax.vmap(lambda parent_row: ancestry(parent_row, draft))(parents)
    tree_scores = (
        jnp.einsum("rqhd,rkhd->rhqk", tree_queries, tree_keys, preferred_element_type=jnp.float32)
        * scale
    )
    tree_scores = jnp.where(lineage[:, None], tree_scores, -jnp.inf)
    tree_top = jnp.max(tree_scores, axis=3, keepdims=True)
    tree_exp = jnp.exp(tree_scores - tree_top)
    tree_total = jnp.sum(tree_exp, axis=3, keepdims=True)
    tree_probs = tree_exp.astype(jnp.bfloat16)
    tree_part = jnp.einsum(
        "rhqk,rkhd->rqhd", tree_probs, tree_values, preferred_element_type=jnp.float32
    ) / jnp.transpose(tree_total, (0, 2, 1, 3))
    tree_lse = jnp.transpose((tree_top + jnp.log(tree_total))[..., 0], (0, 2, 1))[..., None]
    my_owner = lax.dynamic_slice_in_dim(owner_slot, myself * requests, requests)
    target = my_owner // requests
    earlier = local_ids[None, :] < local_ids[:, None]
    same_target = target[None, :] == target[:, None]
    rank = jnp.sum((earlier & same_target).astype(jnp.int32), axis=1)
    my_slots = myself * requests + local_ids
    every_id = jnp.arange(owner_slot.shape[0], dtype=jnp.int32)
    source_request = jnp.sum(
        jnp.where(owner_slot[None, :] == my_slots[:, None], every_id[None, :], 0), axis=1
    )
    source = source_request // requests
    source_local = source_request % requests
    source_targets = owner_slot.reshape(shards, requests)[source] // requests
    source_rank = jnp.sum(
        ((local_ids[None, :] < source_local[:, None]) & (source_targets == myself)).astype(
            jnp.int32
        ),
        axis=1,
    )

    shaped_queries = queries.reshape(requests, draft, width)
    slots_total = shards * PEER_MOST
    send_index = target * PEER_MOST + rank
    receive_index = source * PEER_MOST + source_rank
    slot_ids = jnp.arange(slots_total, dtype=jnp.int32)

    def spread(values, index):
        match = index[None, :] == slot_ids[:, None]
        filled = jnp.any(match, axis=1)
        pick = jnp.sum(jnp.where(match, local_ids[None, :], 0), axis=1)
        taken = values[pick]
        shape = (slots_total,) + (1,) * (values.ndim - 1)
        return jnp.where(filled.reshape(shape), taken, jnp.zeros((), values.dtype))

    arrived = (
        lax.all_to_all(
            spread(shaped_queries, send_index), "dp", split_axis=0, concat_axis=0, tiled=True
        ),
        lax.all_to_all(
            spread(kept_keys, send_index), "dp", split_axis=0, concat_axis=0, tiled=True
        ),
        lax.all_to_all(
            spread(kept_values, send_index), "dp", split_axis=0, concat_axis=0, tiled=True
        ),
    )
    owned_queries = arrived[0][receive_index].reshape(requests, draft, local_heads, HD)
    new_keys = arrived[1][receive_index]
    new_values = arrived[2][receive_index]
    slot_keys = cache_keys.reshape(requests, capacity, local_heads, HD)
    slot_values = cache_values.reshape(requests, capacity, local_heads, HD)
    scores = (
        jnp.einsum(
            "sqhd,skhd->shqk", owned_queries, slot_keys, preferred_element_type=jnp.float32
        )
        * scale
    )
    living = jnp.arange(capacity, dtype=jnp.int32)[None, :] < slot_lengths[:, None]
    scores = jnp.where(living[:, None, None, :], scores, -jnp.inf)
    cache_top = jnp.max(scores, axis=3, keepdims=True)
    cache_exp = jnp.exp(scores - cache_top)
    cache_total = jnp.sum(cache_exp, axis=3, keepdims=True)
    cache_probs = cache_exp.astype(jnp.bfloat16)
    gathered = jnp.einsum(
        "shqk,skhd->sqhd", cache_probs, slot_values, preferred_element_type=jnp.float32
    )
    owned_part = (
        (gathered / jnp.transpose(cache_total, (0, 2, 1, 3)))
        .astype(jnp.bfloat16)
        .reshape(requests, draft, width)
    )
    owned_lse = (cache_top + jnp.log(cache_total))[..., 0]
    lse_flat = split_three(owned_lse).reshape(requests, -1)
    lse_rows = -(-lse_flat.shape[1] // width)
    lse_flat = jnp.pad(lse_flat, ((0, 0), (0, lse_rows * width - lse_flat.shape[1])))
    back = jnp.concatenate(
        [owned_part, lse_flat.reshape(requests, lse_rows, width)], axis=1
    )
    returned = lax.all_to_all(
        spread(back, receive_index), "dp", split_axis=0, concat_axis=0, tiled=True
    )[send_index]
    cache_part = returned[:, :draft]
    lse_back = returned[:, draft:].reshape(requests, -1)[:, : 3 * local_heads * draft]
    cache_lse = join_three(lse_back.reshape(requests, 3, local_heads, draft))
    cache_weight = jnp.transpose(cache_lse, (0, 2, 1))[..., None]
    larger = jnp.maximum(cache_weight, tree_lse)
    cache_share = jnp.exp(cache_weight - larger)
    tree_share = jnp.exp(tree_lse - larger)
    blended = (
        cache_share * cache_part.astype(jnp.float32).reshape(requests, draft, local_heads, HD)
        + tree_share * tree_part
    ) / (cache_share + tree_share)
    attended = blended.astype(jnp.bfloat16).reshape(tokens, width)
    attention_term = jnp.dot(attended, w_out, preferred_element_type=jnp.float32)
    feature = model_width // lax.axis_size("head")
    offset = lax.axis_index("head") * feature

    def columns(values):
        return lax.dynamic_slice_in_dim(values, offset, feature, values.ndim - 1)

    attention_sum = lax.psum(attention_term.astype(jnp.bfloat16), "head").astype(jnp.float32)
    first_normed = normalize(
        attention_sum + b_out + hidden.astype(jnp.float32), first_gain, first_shift
    ).astype(jnp.bfloat16)
    inner = jax.nn.gelu(
        jnp.dot(first_normed, w_up, preferred_element_type=jnp.float32) + b_up, approximate=True
    ).astype(jnp.bfloat16)
    down_share = lax.psum_scatter(
        jnp.dot(inner, w_down, preferred_element_type=jnp.float32).astype(jnp.bfloat16),
        "head",
        scatter_dimension=1,
        tiled=True,
    ).astype(jnp.float32)
    second_mixed = down_share + columns(b_down) + columns(first_normed).astype(jnp.float32)
    second_sums = lax.psum(
        jnp.stack([jnp.sum(second_mixed, axis=1), jnp.sum(second_mixed * second_mixed, axis=1)]),
        "head",
    )
    layer_out = normalize_shared(
        second_mixed, second_sums, columns(second_gain), columns(second_shift), model_width
    ).astype(jnp.bfloat16)
    return (layer_out, new_keys, new_values)


def solution(mesh):
    placed = (
        P("dp", None),
        P("dp", None),
        P(),
        P("dp"),
        P("dp", None),
        P("dp"),
        P("dp", None, "head"),
        P("dp", None, "head"),
        P(None, "head"),
        P("head"),
        P(None, "head"),
        P(None, "head"),
        P("head"),
        P("head", None),
        P(),
        P(),
        P(),
        P(None, "head"),
        P("head"),
        P("head", None),
        P(),
        P(),
        P(),
    )
    return jax.shard_map(
        local,
        mesh=mesh,
        in_specs=placed,
        out_specs=(P("dp", "head"), P("dp", None, "head"), P("dp", None, "head")),
        check_vma=False,
    )
```

```python
import math

import jax
import jax.numpy as jnp
from jax import lax
from jax.sharding import PartitionSpec as P

HD = 128
PEER_MOST = 2


EPSILON = 1e-05


def ancestry(parent_row, draft):
    nodes = jnp.arange(draft, dtype=jnp.int32)
    reach = (parent_row[:, None] == nodes[None, :]).astype(jnp.float32) + jnp.eye(
        draft, dtype=jnp.float32
    )
    for turn in range(max(1, draft.bit_length())):
        reach = jnp.minimum(jnp.dot(reach, reach, precision=lax.Precision.HIGHEST), 1.0)
    return reach > 0.5


def normalize(mixed, gain, shift):
    center = jnp.mean(mixed, axis=-1, keepdims=True)
    square = jnp.mean(mixed * mixed, axis=-1, keepdims=True)
    return (mixed - center) * lax.rsqrt(square - center * center + EPSILON) * gain + shift


def normalize_shared(mixed, sums, gain, shift, model_width):
    center = (sums[0] / model_width)[:, None]
    square = (sums[1] / model_width)[:, None]
    return (mixed - center) * lax.rsqrt(square - center * center + EPSILON) * gain + shift


def split_three(values):
    high = values.astype(jnp.bfloat16)
    rest = values - high.astype(jnp.float32)
    middle = rest.astype(jnp.bfloat16)
    low = (rest - middle.astype(jnp.float32)).astype(jnp.bfloat16)
    return jnp.stack([high, middle, low], axis=1)


def join_three(pieces):
    wide = pieces.astype(jnp.float32)
    return wide[:, 0] + (wide[:, 1] + wide[:, 2])


CHUNKS = 2


def local(
    hidden,
    parents,
    owner_slot,
    slot_lengths,
    accepted_path,
    accepted_count,
    cache_keys,
    cache_values,
    w_query,
    b_query,
    w_key,
    w_value,
    b_value,
    w_out,
    b_out,
    first_gain,
    first_shift,
    w_up,
    b_up,
    w_down,
    b_down,
    second_gain,
    second_shift,
):
    requests = parents.shape[0]
    draft = parents.shape[1]
    model_width = hidden.shape[1]
    width = w_query.shape[1]
    local_heads = width // HD
    capacity = cache_keys.shape[1]
    shards = lax.axis_size("dp")
    myself = lax.axis_index("dp")
    scale = 1.0 / math.sqrt(HD)
    rows = draft // CHUNKS
    queries = (jnp.dot(hidden, w_query, preferred_element_type=jnp.float32) + b_query).astype(
        jnp.bfloat16
    )
    key_rows = jnp.dot(hidden, w_key, preferred_element_type=jnp.float32).astype(jnp.bfloat16)
    value_rows = (jnp.dot(hidden, w_value, preferred_element_type=jnp.float32) + b_value).astype(
        jnp.bfloat16
    )
    local_ids = jnp.arange(requests, dtype=jnp.int32)
    levels = jnp.arange(accepted_path.shape[1], dtype=jnp.int32)
    chosen = local_ids[:, None] * draft + accepted_path
    usable = (levels[None, :] < accepted_count[:, None])[..., None]
    kept_keys = jnp.where(usable, key_rows[chosen], jnp.zeros((), jnp.bfloat16))
    kept_values = jnp.where(usable, value_rows[chosen], jnp.zeros((), jnp.bfloat16))
    tree_queries = queries.reshape(requests, draft, local_heads, HD)
    tree_keys = key_rows.reshape(requests, draft, local_heads, HD)
    tree_values = value_rows.reshape(requests, draft, local_heads, HD)
    lineage = jax.vmap(lambda parent_row: ancestry(parent_row, draft))(parents)
    tree_scores = (
        jnp.einsum("rqhd,rkhd->rhqk", tree_queries, tree_keys, preferred_element_type=jnp.float32)
        * scale
    )
    tree_scores = jnp.where(lineage[:, None], tree_scores, -jnp.inf)
    tree_top = jnp.max(tree_scores, axis=3, keepdims=True)
    tree_exp = jnp.exp(tree_scores - tree_top)
    tree_total = jnp.sum(tree_exp, axis=3, keepdims=True)
    tree_probs = tree_exp.astype(jnp.bfloat16)
    tree_part = jnp.einsum(
        "rhqk,rkhd->rqhd", tree_probs, tree_values, preferred_element_type=jnp.float32
    ) / jnp.transpose(tree_total, (0, 2, 1, 3))
    tree_lse = jnp.transpose((tree_top + jnp.log(tree_total))[..., 0], (0, 2, 1))[..., None]
    my_owner = lax.dynamic_slice_in_dim(owner_slot, myself * requests, requests)
    target = my_owner // requests
    earlier = local_ids[None, :] < local_ids[:, None]
    same_target = target[None, :] == target[:, None]
    rank = jnp.sum((earlier & same_target).astype(jnp.int32), axis=1)
    my_slots = myself * requests + local_ids
    every_id = jnp.arange(owner_slot.shape[0], dtype=jnp.int32)
    source_request = jnp.sum(
        jnp.where(owner_slot[None, :] == my_slots[:, None], every_id[None, :], 0), axis=1
    )
    source = source_request // requests
    source_local = source_request % requests
    source_targets = owner_slot.reshape(shards, requests)[source] // requests
    source_rank = jnp.sum(
        ((local_ids[None, :] < source_local[:, None]) & (source_targets == myself)).astype(
            jnp.int32
        ),
        axis=1,
    )
    slots_total = shards * PEER_MOST
    send_index = target * PEER_MOST + rank
    receive_index = source * PEER_MOST + source_rank
    slot_ids = jnp.arange(slots_total, dtype=jnp.int32)

    def spread(values, index):
        match = index[None, :] == slot_ids[:, None]
        filled = jnp.any(match, axis=1)
        pick = jnp.sum(jnp.where(match, local_ids[None, :], 0), axis=1)
        taken = values[pick]
        shape = (slots_total,) + (1,) * (values.ndim - 1)
        return jnp.where(filled.reshape(shape), taken, jnp.zeros((), values.dtype))

    def exchange(values, there, back):
        moved = lax.all_to_all(spread(values, there), "dp", split_axis=0, concat_axis=0, tiled=True)
        return moved[back]

    slot_keys = cache_keys.reshape(requests, capacity, local_heads, HD)
    slot_values = cache_values.reshape(requests, capacity, local_heads, HD)
    living = jnp.arange(capacity, dtype=jnp.int32)[None, :] < slot_lengths[:, None]
    shaped_queries = queries.reshape(requests, draft, width)
    shaped_hidden = hidden.reshape(requests, draft, model_width)
    feature = model_width // lax.axis_size("head")
    offset = lax.axis_index("head") * feature

    def columns(values):
        return lax.dynamic_slice_in_dim(values, offset, feature, values.ndim - 1)

    paths = kept_keys.shape[1]
    kept = exchange(jnp.concatenate([kept_keys, kept_values], axis=1), send_index, receive_index)
    new_keys = kept[:, :paths]
    new_values = kept[:, paths:]
    attention_terms = []
    attention_sums = []
    for chunk in range(CHUNKS):
        low = chunk * rows
        sent = shaped_queries[:, low : low + rows]
        if chunk > 0:
            sent, attention_terms[-1] = lax.optimization_barrier((sent, attention_terms[-1]))
            attention_sums.append(lax.psum(attention_terms[-1].astype(jnp.bfloat16), "head"))
        arrived = exchange(sent, send_index, receive_index)
        owned_queries = arrived[:, :rows].reshape(requests, rows, local_heads, HD)
        scores = (
            jnp.einsum(
                "sqhd,skhd->shqk", owned_queries, slot_keys, preferred_element_type=jnp.float32
            )
            * scale
        )
        scores = jnp.where(living[:, None, None, :], scores, -jnp.inf)
        cache_top = jnp.max(scores, axis=3, keepdims=True)
        cache_exp = jnp.exp(scores - cache_top)
        cache_total = jnp.sum(cache_exp, axis=3, keepdims=True)
        cache_probs = cache_exp.astype(jnp.bfloat16)
        gathered = jnp.einsum(
            "shqk,skhd->sqhd", cache_probs, slot_values, preferred_element_type=jnp.float32
        )
        owned_part = (
            (gathered / jnp.transpose(cache_total, (0, 2, 1, 3)))
            .astype(jnp.bfloat16)
            .reshape(requests, rows, width)
        )
        owned_lse = (cache_top + jnp.log(cache_total))[..., 0]
        lse_flat = split_three(owned_lse).reshape(requests, -1)
        lse_rows = -(-lse_flat.shape[1] // width)
        lse_flat = jnp.pad(lse_flat, ((0, 0), (0, lse_rows * width - lse_flat.shape[1])))
        back = jnp.concatenate([owned_part, lse_flat.reshape(requests, lse_rows, width)], axis=1)
        returned = exchange(back, receive_index, send_index)
        cache_part = returned[:, :rows]
        lse_back = returned[:, rows:].reshape(requests, -1)[:, : 3 * local_heads * rows]
        cache_lse = join_three(lse_back.reshape(requests, 3, local_heads, rows))
        cache_weight = jnp.transpose(cache_lse, (0, 2, 1))[..., None]
        tree_weight = tree_lse[:, low : low + rows]
        larger = jnp.maximum(cache_weight, tree_weight)
        cache_share = jnp.exp(cache_weight - larger)
        tree_share = jnp.exp(tree_weight - larger)
        blended = (
            cache_share * cache_part.astype(jnp.float32).reshape(requests, rows, local_heads, HD)
            + tree_share * tree_part[:, low : low + rows]
        ) / (cache_share + tree_share)
        attended = blended.astype(jnp.bfloat16).reshape(requests * rows, width)
        if chunk > 0:
            attended, attention_sums[-1] = lax.optimization_barrier(
                (attended, attention_sums[-1])
            )
        attention_terms.append(jnp.dot(attended, w_out, preferred_element_type=jnp.float32))
    attention_sums.append(lax.psum(attention_terms[-1].astype(jnp.bfloat16), "head"))
    mixed_parts = []
    for chunk in range(CHUNKS):
        low = chunk * rows
        attention_sum = attention_sums[chunk].astype(jnp.float32)
        residual = shaped_hidden[:, low : low + rows].reshape(requests * rows, model_width)
        first_normed = normalize(
            attention_sum + b_out + residual.astype(jnp.float32), first_gain, first_shift
        ).astype(jnp.bfloat16)
        inner = jax.nn.gelu(
            jnp.dot(first_normed, w_up, preferred_element_type=jnp.float32) + b_up,
            approximate=True,
        ).astype(jnp.bfloat16)
        down_share = lax.psum_scatter(
            jnp.dot(inner, w_down, preferred_element_type=jnp.float32).astype(jnp.bfloat16),
            "head",
            scatter_dimension=1,
            tiled=True,
        ).astype(jnp.float32)
        mixed_parts.append(
            down_share + columns(b_down) + columns(first_normed).astype(jnp.float32)
        )
    row_sums = []
    for chunk in range(CHUNKS):
        second_mixed = mixed_parts[chunk]
        if chunk > 0:
            second_mixed, row_sums[-1] = lax.optimization_barrier((second_mixed, row_sums[-1]))
            mixed_parts[chunk] = second_mixed
        row_sums.append(
            lax.psum(
                jnp.stack(
                    [jnp.sum(second_mixed, axis=1), jnp.sum(second_mixed * second_mixed, axis=1)]
                ),
                "head",
            )
        )
    outputs = []
    for chunk in range(CHUNKS):
        layer_part = normalize_shared(
            mixed_parts[chunk],
            row_sums[chunk],
            columns(second_gain),
            columns(second_shift),
            model_width,
        ).astype(jnp.bfloat16)
        outputs.append(layer_part.reshape(requests, rows, feature))
    layer_out = jnp.concatenate(outputs, axis=1).reshape(requests * draft, feature)
    return (layer_out, new_keys, new_values)


def solution(mesh):
    placed = (
        P("dp", None),
        P("dp", None),
        P(),
        P("dp"),
        P("dp", None),
        P("dp"),
        P("dp", None, "head"),
        P("dp", None, "head"),
        P(None, "head"),
        P("head"),
        P(None, "head"),
        P(None, "head"),
        P("head"),
        P("head", None),
        P(),
        P(),
        P(),
        P(None, "head"),
        P("head"),
        P("head", None),
        P(),
        P(),
        P(),
    )
    return jax.shard_map(
        local,
        mesh=mesh,
        in_specs=placed,
        out_specs=(P("dp", "head"), P("dp", None, "head"), P("dp", None, "head")),
        check_vma=False,
    )
```

```python
import math

import jax
import jax.numpy as jnp
from jax import lax
from jax.sharding import PartitionSpec as P

HD = 128
PEER_MOST = 2


EPSILON = 1e-05


def ancestry(parent_row, draft):
    nodes = jnp.arange(draft, dtype=jnp.int32)
    reach = (parent_row[:, None] == nodes[None, :]).astype(jnp.float32) + jnp.eye(
        draft, dtype=jnp.float32
    )
    for turn in range(max(1, draft.bit_length())):
        reach = jnp.minimum(jnp.dot(reach, reach, precision=lax.Precision.HIGHEST), 1.0)
    return reach > 0.5


def normalize(mixed, gain, shift):
    center = jnp.mean(mixed, axis=-1, keepdims=True)
    square = jnp.mean(mixed * mixed, axis=-1, keepdims=True)
    return (mixed - center) * lax.rsqrt(square - center * center + EPSILON) * gain + shift


def normalize_shared(mixed, sums, gain, shift, model_width):
    center = (sums[0] / model_width)[:, None]
    square = (sums[1] / model_width)[:, None]
    return (mixed - center) * lax.rsqrt(square - center * center + EPSILON) * gain + shift


def split_three(values):
    high = values.astype(jnp.bfloat16)
    rest = values - high.astype(jnp.float32)
    middle = rest.astype(jnp.bfloat16)
    low = (rest - middle.astype(jnp.float32)).astype(jnp.bfloat16)
    return jnp.stack([high, middle, low], axis=1)


def join_three(pieces):
    wide = pieces.astype(jnp.float32)
    return wide[:, 0] + (wide[:, 1] + wide[:, 2])


def local(
    hidden,
    parents,
    owner_slot,
    slot_lengths,
    accepted_path,
    accepted_count,
    cache_keys,
    cache_values,
    w_query,
    b_query,
    w_key,
    w_value,
    b_value,
    w_out,
    b_out,
    first_gain,
    first_shift,
    w_up,
    b_up,
    w_down,
    b_down,
    second_gain,
    second_shift,
):
    requests = parents.shape[0]
    draft = parents.shape[1]
    tokens = hidden.shape[0]
    model_width = hidden.shape[1]
    width = w_query.shape[1]
    local_heads = width // HD
    capacity = cache_keys.shape[1]
    block = min(capacity, 256)
    shards = lax.axis_size("dp")
    myself = lax.axis_index("dp")
    scale = 1.0 / math.sqrt(HD)
    queries = (jnp.dot(hidden, w_query, preferred_element_type=jnp.float32) + b_query).astype(
        jnp.bfloat16
    )
    key_rows = jnp.dot(hidden, w_key, preferred_element_type=jnp.float32).astype(jnp.bfloat16)
    value_rows = (jnp.dot(hidden, w_value, preferred_element_type=jnp.float32) + b_value).astype(
        jnp.bfloat16
    )
    local_ids = jnp.arange(requests, dtype=jnp.int32)
    levels = jnp.arange(accepted_path.shape[1], dtype=jnp.int32)
    chosen = local_ids[:, None] * draft + accepted_path
    usable = (levels[None, :] < accepted_count[:, None])[..., None]
    kept_keys = jnp.where(usable, key_rows[chosen], jnp.zeros((), jnp.bfloat16))
    kept_values = jnp.where(usable, value_rows[chosen], jnp.zeros((), jnp.bfloat16))
    tree_queries = queries.reshape(requests, draft, local_heads, HD)
    tree_keys = key_rows.reshape(requests, draft, local_heads, HD)
    tree_values = value_rows.reshape(requests, draft, local_heads, HD)
    lineage = jax.vmap(lambda parent_row: ancestry(parent_row, draft))(parents)
    tree_scores = (
        jnp.einsum("rqhd,rkhd->rhqk", tree_queries, tree_keys, preferred_element_type=jnp.float32)
        * scale
    )
    tree_scores = jnp.where(lineage[:, None], tree_scores, -jnp.inf)
    tree_top = jnp.max(tree_scores, axis=3, keepdims=True)
    tree_exp = jnp.exp(tree_scores - tree_top)
    tree_total = jnp.sum(tree_exp, axis=3, keepdims=True)
    tree_probs = tree_exp.astype(jnp.bfloat16)
    tree_part = jnp.einsum(
        "rhqk,rkhd->rqhd", tree_probs, tree_values, preferred_element_type=jnp.float32
    ) / jnp.transpose(tree_total, (0, 2, 1, 3))
    tree_lse = jnp.transpose((tree_top + jnp.log(tree_total))[..., 0], (0, 2, 1))[..., None]
    my_owner = lax.dynamic_slice_in_dim(owner_slot, myself * requests, requests)
    target = my_owner // requests
    earlier = local_ids[None, :] < local_ids[:, None]
    same_target = target[None, :] == target[:, None]
    rank = jnp.sum((earlier & same_target).astype(jnp.int32), axis=1)
    my_slots = myself * requests + local_ids
    every_id = jnp.arange(owner_slot.shape[0], dtype=jnp.int32)
    source_request = jnp.sum(
        jnp.where(owner_slot[None, :] == my_slots[:, None], every_id[None, :], 0), axis=1
    )
    source = source_request // requests
    source_local = source_request % requests
    source_targets = owner_slot.reshape(shards, requests)[source] // requests
    source_rank = jnp.sum(
        ((local_ids[None, :] < source_local[:, None]) & (source_targets == myself)).astype(
            jnp.int32
        ),
        axis=1,
    )

    shaped_queries = queries.reshape(requests, draft, width)
    slots_total = shards * PEER_MOST
    send_index = target * PEER_MOST + rank
    receive_index = source * PEER_MOST + source_rank
    slot_ids = jnp.arange(slots_total, dtype=jnp.int32)

    def spread(values, index):
        placing = (index[None, :] == slot_ids[:, None]).astype(values.dtype)
        flat = values.reshape(values.shape[0], -1)
        placed = jnp.dot(placing, flat, preferred_element_type=jnp.float32).astype(values.dtype)
        return placed.reshape((slots_total,) + values.shape[1:])

    arrived = lax.all_to_all(
        spread(shaped_queries, send_index), "dp", split_axis=0, concat_axis=0, tiled=True
    )
    kept = lax.all_to_all(
        spread(jnp.concatenate([kept_keys, kept_values], axis=1), send_index),
        "dp",
        split_axis=0,
        concat_axis=0,
        tiled=True,
    )[receive_index]
    owned_queries = arrived[receive_index].reshape(requests, draft, local_heads, HD)
    new_keys = kept[:, : kept_keys.shape[1]]
    new_values = kept[:, kept_keys.shape[1] :]
    slot_keys = cache_keys.reshape(requests, capacity, local_heads, HD)
    slot_values = cache_values.reshape(requests, capacity, local_heads, HD)
    scores = (
        jnp.einsum(
            "sqhd,skhd->shqk", owned_queries, slot_keys, preferred_element_type=jnp.float32
        )
        * scale
    )
    living = jnp.arange(capacity, dtype=jnp.int32)[None, :] < slot_lengths[:, None]
    scores = jnp.where(living[:, None, None, :], scores, -jnp.inf)
    cache_top = jnp.max(scores, axis=3, keepdims=True)
    cache_exp = jnp.exp(scores - cache_top)
    cache_total = jnp.sum(cache_exp, axis=3, keepdims=True)
    cache_probs = cache_exp.astype(jnp.bfloat16)
    gathered = jnp.einsum(
        "shqk,skhd->sqhd", cache_probs, slot_values, preferred_element_type=jnp.float32
    )
    owned_part = (
        (gathered / jnp.transpose(cache_total, (0, 2, 1, 3)))
        .astype(jnp.bfloat16)
        .reshape(requests, draft, width)
    )
    owned_lse = (cache_top + jnp.log(cache_total))[..., 0]
    lse_flat = split_three(owned_lse).reshape(requests, -1)
    lse_rows = -(-lse_flat.shape[1] // width)
    lse_flat = jnp.pad(lse_flat, ((0, 0), (0, lse_rows * width - lse_flat.shape[1])))
    back = jnp.concatenate(
        [owned_part, lse_flat.reshape(requests, lse_rows, width)], axis=1
    )
    returned = lax.all_to_all(
        spread(back, receive_index), "dp", split_axis=0, concat_axis=0, tiled=True
    )[send_index]
    cache_part = returned[:, :draft]
    lse_back = returned[:, draft:].reshape(requests, -1)[:, : 3 * local_heads * draft]
    cache_lse = join_three(lse_back.reshape(requests, 3, local_heads, draft))
    cache_weight = jnp.transpose(cache_lse, (0, 2, 1))[..., None]
    larger = jnp.maximum(cache_weight, tree_lse)
    cache_share = jnp.exp(cache_weight - larger)
    tree_share = jnp.exp(tree_lse - larger)
    blended = (
        cache_share * cache_part.astype(jnp.float32).reshape(requests, draft, local_heads, HD)
        + tree_share * tree_part
    ) / (cache_share + tree_share)
    attended = blended.astype(jnp.bfloat16).reshape(tokens, width)
    attention_term = jnp.dot(attended, w_out, preferred_element_type=jnp.float32)
    feature = model_width // lax.axis_size("head")
    offset = lax.axis_index("head") * feature

    def columns(values):
        return lax.dynamic_slice_in_dim(values, offset, feature, values.ndim - 1)

    attention_sum = lax.psum(attention_term.astype(jnp.bfloat16), "head").astype(jnp.float32)
    first_normed = normalize(
        attention_sum + b_out + hidden.astype(jnp.float32), first_gain, first_shift
    ).astype(jnp.bfloat16)
    inner = jax.nn.gelu(
        jnp.dot(first_normed, w_up, preferred_element_type=jnp.float32) + b_up, approximate=True
    ).astype(jnp.bfloat16)
    down_share = lax.psum_scatter(
        jnp.dot(inner, w_down, preferred_element_type=jnp.float32).astype(jnp.bfloat16),
        "head",
        scatter_dimension=1,
        tiled=True,
    ).astype(jnp.float32)
    second_mixed = down_share + columns(b_down) + columns(first_normed).astype(jnp.float32)
    heads_along = lax.axis_size("head")
    own_sums = jnp.stack(
        [jnp.sum(second_mixed, axis=1), jnp.sum(second_mixed * second_mixed, axis=1)]
    )
    second_sums = jnp.sum(
        lax.all_to_all(
            jnp.broadcast_to(own_sums[None], (heads_along,) + own_sums.shape),
            "head",
            0,
            0,
            tiled=False,
        ),
        axis=0,
    )
    layer_out = normalize_shared(
        second_mixed, second_sums, columns(second_gain), columns(second_shift), model_width
    ).astype(jnp.bfloat16)
    return (layer_out, new_keys, new_values)


def solution(mesh):
    placed = (
        P("dp", None),
        P("dp", None),
        P(),
        P("dp"),
        P("dp", None),
        P("dp"),
        P("dp", None, "head"),
        P("dp", None, "head"),
        P(None, "head"),
        P("head"),
        P(None, "head"),
        P(None, "head"),
        P("head"),
        P("head", None),
        P(),
        P(),
        P(),
        P(None, "head"),
        P("head"),
        P("head", None),
        P(),
        P(),
        P(),
    )
    return jax.shard_map(
        local,
        mesh=mesh,
        in_specs=placed,
        out_specs=(P("dp", "head"), P("dp", None, "head"), P("dp", None, "head")),
        check_vma=False,
    )
```

```python
import math

import jax
import jax.numpy as jnp
from jax import lax
from jax.sharding import PartitionSpec as P

HD = 128
PEER_MOST = 2


EPSILON = 1e-05


def ancestry(parent_row, draft):
    nodes = jnp.arange(draft, dtype=jnp.int32)
    reach = (parent_row[:, None] == nodes[None, :]).astype(jnp.float32) + jnp.eye(
        draft, dtype=jnp.float32
    )
    for turn in range(max(1, draft.bit_length())):
        reach = jnp.minimum(jnp.dot(reach, reach, precision=lax.Precision.HIGHEST), 1.0)
    return reach > 0.5


def normalize(mixed, gain, shift):
    center = jnp.mean(mixed, axis=-1, keepdims=True)
    square = jnp.mean(mixed * mixed, axis=-1, keepdims=True)
    return (mixed - center) * lax.rsqrt(square - center * center + EPSILON) * gain + shift


def normalize_shared(mixed, sums, gain, shift, model_width):
    center = (sums[0] / model_width)[:, None]
    square = (sums[1] / model_width)[:, None]
    return (mixed - center) * lax.rsqrt(square - center * center + EPSILON) * gain + shift


def split_three(values):
    high = values.astype(jnp.bfloat16)
    rest = values - high.astype(jnp.float32)
    middle = rest.astype(jnp.bfloat16)
    low = (rest - middle.astype(jnp.float32)).astype(jnp.bfloat16)
    return jnp.stack([high, middle, low], axis=1)


def join_three(pieces):
    wide = pieces.astype(jnp.float32)
    return wide[:, 0] + (wide[:, 1] + wide[:, 2])


def local(
    hidden,
    parents,
    owner_slot,
    slot_lengths,
    accepted_path,
    accepted_count,
    cache_keys,
    cache_values,
    w_query,
    b_query,
    w_key,
    w_value,
    b_value,
    w_out,
    b_out,
    first_gain,
    first_shift,
    w_up,
    b_up,
    w_down,
    b_down,
    second_gain,
    second_shift,
):
    requests = parents.shape[0]
    draft = parents.shape[1]
    tokens = hidden.shape[0]
    model_width = hidden.shape[1]
    width = w_query.shape[1]
    local_heads = width // HD
    capacity = cache_keys.shape[1]
    block = min(capacity, 256)
    shards = lax.axis_size("dp")
    myself = lax.axis_index("dp")
    scale = 1.0 / math.sqrt(HD)
    queries = (jnp.dot(hidden, w_query, preferred_element_type=jnp.float32) + b_query).astype(
        jnp.bfloat16
    )
    key_rows = jnp.dot(hidden, w_key, preferred_element_type=jnp.float32).astype(jnp.bfloat16)
    value_rows = (jnp.dot(hidden, w_value, preferred_element_type=jnp.float32) + b_value).astype(
        jnp.bfloat16
    )
    local_ids = jnp.arange(requests, dtype=jnp.int32)
    levels = jnp.arange(accepted_path.shape[1], dtype=jnp.int32)
    chosen = local_ids[:, None] * draft + accepted_path
    usable = (levels[None, :] < accepted_count[:, None])[..., None]
    kept_keys = jnp.where(usable, key_rows[chosen], jnp.zeros((), jnp.bfloat16))
    kept_values = jnp.where(usable, value_rows[chosen], jnp.zeros((), jnp.bfloat16))
    tree_queries = queries.reshape(requests, draft, local_heads, HD)
    tree_keys = key_rows.reshape(requests, draft, local_heads, HD)
    tree_values = value_rows.reshape(requests, draft, local_heads, HD)
    lineage = jax.vmap(lambda parent_row: ancestry(parent_row, draft))(parents)
    tree_scores = (
        jnp.einsum("rqhd,rkhd->rhqk", tree_queries, tree_keys, preferred_element_type=jnp.float32)
        * scale
    )
    tree_scores = jnp.where(lineage[:, None], tree_scores, -jnp.inf)
    tree_top = jnp.max(tree_scores, axis=3, keepdims=True)
    tree_exp = jnp.exp(tree_scores - tree_top)
    tree_total = jnp.sum(tree_exp, axis=3, keepdims=True)
    tree_probs = tree_exp.astype(jnp.bfloat16)
    tree_part = jnp.einsum(
        "rhqk,rkhd->rqhd", tree_probs, tree_values, preferred_element_type=jnp.float32
    ) / jnp.transpose(tree_total, (0, 2, 1, 3))
    tree_lse = jnp.transpose((tree_top + jnp.log(tree_total))[..., 0], (0, 2, 1))[..., None]
    my_owner = lax.dynamic_slice_in_dim(owner_slot, myself * requests, requests)
    target = my_owner // requests
    earlier = local_ids[None, :] < local_ids[:, None]
    same_target = target[None, :] == target[:, None]
    rank = jnp.sum((earlier & same_target).astype(jnp.int32), axis=1)
    my_slots = myself * requests + local_ids
    every_id = jnp.arange(owner_slot.shape[0], dtype=jnp.int32)
    source_request = jnp.sum(
        jnp.where(owner_slot[None, :] == my_slots[:, None], every_id[None, :], 0), axis=1
    )
    source = source_request // requests
    source_local = source_request % requests
    source_targets = owner_slot.reshape(shards, requests)[source] // requests
    source_rank = jnp.sum(
        ((local_ids[None, :] < source_local[:, None]) & (source_targets == myself)).astype(
            jnp.int32
        ),
        axis=1,
    )

    shaped_queries = queries.reshape(requests, draft, width)
    slots_total = shards * PEER_MOST
    send_index = target * PEER_MOST + rank
    receive_index = source * PEER_MOST + source_rank
    slot_ids = jnp.arange(slots_total, dtype=jnp.int32)

    def spread(values, index):
        placing = (index[None, :] == slot_ids[:, None]).astype(values.dtype)
        flat = values.reshape(values.shape[0], -1)
        placed = jnp.dot(placing, flat, preferred_element_type=jnp.float32).astype(values.dtype)
        return placed.reshape((slots_total,) + values.shape[1:])

    arrived = lax.all_to_all(
        spread(shaped_queries, send_index), "dp", split_axis=0, concat_axis=0, tiled=True
    )
    kept = lax.all_to_all(
        spread(jnp.concatenate([kept_keys, kept_values], axis=1), send_index),
        "dp",
        split_axis=0,
        concat_axis=0,
        tiled=True,
    )[receive_index]
    owned_queries = arrived[receive_index].reshape(requests, draft, local_heads, HD)
    new_keys = kept[:, : kept_keys.shape[1]]
    new_values = kept[:, kept_keys.shape[1] :]
    slot_keys = cache_keys.reshape(requests, capacity, local_heads, HD)
    slot_values = cache_values.reshape(requests, capacity, local_heads, HD)
    scores = (
        jnp.einsum(
            "sqhd,skhd->shqk", owned_queries, slot_keys, preferred_element_type=jnp.float32
        )
        * scale
    )
    living = jnp.arange(capacity, dtype=jnp.int32)[None, :] < slot_lengths[:, None]
    scores = jnp.where(living[:, None, None, :], scores, -jnp.inf)
    cache_top = jnp.max(scores, axis=3, keepdims=True)
    cache_exp = jnp.exp(scores - cache_top)
    cache_total = jnp.sum(cache_exp, axis=3, keepdims=True)
    cache_probs = cache_exp.astype(jnp.bfloat16)
    gathered = jnp.einsum(
        "shqk,skhd->sqhd", cache_probs, slot_values, preferred_element_type=jnp.float32
    )
    owned_part = (
        (gathered / jnp.transpose(cache_total, (0, 2, 1, 3)))
        .astype(jnp.bfloat16)
        .reshape(requests, draft, width)
    )
    owned_lse = (cache_top + jnp.log(cache_total))[..., 0]
    lse_flat = split_three(owned_lse).reshape(requests, -1)
    lse_rows = -(-lse_flat.shape[1] // width)
    lse_flat = jnp.pad(lse_flat, ((0, 0), (0, lse_rows * width - lse_flat.shape[1])))
    back = jnp.concatenate(
        [
            spread(owned_part, receive_index),
            spread(lse_flat, receive_index).reshape(slots_total, lse_rows, width),
        ],
        axis=1,
    )
    returned = lax.all_to_all(back, "dp", split_axis=0, concat_axis=0, tiled=True)[send_index]
    cache_part = returned[:, :draft]
    lse_back = returned[:, draft:].reshape(requests, -1)[:, : 3 * local_heads * draft]
    cache_lse = join_three(lse_back.reshape(requests, 3, local_heads, draft))
    cache_weight = jnp.transpose(cache_lse, (0, 2, 1))[..., None]
    larger = jnp.maximum(cache_weight, tree_lse)
    cache_share = jnp.exp(cache_weight - larger)
    tree_share = jnp.exp(tree_lse - larger)
    blended = (
        cache_share * cache_part.astype(jnp.float32).reshape(requests, draft, local_heads, HD)
        + tree_share * tree_part
    ) / (cache_share + tree_share)
    attended = blended.astype(jnp.bfloat16).reshape(tokens, width)
    attention_term = jnp.dot(attended, w_out, preferred_element_type=jnp.float32)
    feature = model_width // lax.axis_size("head")
    offset = lax.axis_index("head") * feature

    def columns(values):
        return lax.dynamic_slice_in_dim(values, offset, feature, values.ndim - 1)

    attention_sum = lax.psum(attention_term.astype(jnp.bfloat16), "head").astype(jnp.float32)
    first_normed = normalize(
        attention_sum + b_out + hidden.astype(jnp.float32), first_gain, first_shift
    ).astype(jnp.bfloat16)
    inner = jax.nn.gelu(
        jnp.dot(first_normed, w_up, preferred_element_type=jnp.float32) + b_up, approximate=True
    ).astype(jnp.bfloat16)
    down_share = lax.psum_scatter(
        jnp.dot(inner, w_down, preferred_element_type=jnp.float32).astype(jnp.bfloat16),
        "head",
        scatter_dimension=1,
        tiled=True,
    ).astype(jnp.float32)
    second_mixed = down_share + columns(b_down) + columns(first_normed).astype(jnp.float32)
    heads_along = lax.axis_size("head")
    own_sums = jnp.stack(
        [jnp.sum(second_mixed, axis=1), jnp.sum(second_mixed * second_mixed, axis=1)]
    )
    second_sums = jnp.sum(
        lax.all_to_all(
            jnp.broadcast_to(own_sums[None], (heads_along,) + own_sums.shape),
            "head",
            0,
            0,
            tiled=False,
        ),
        axis=0,
    )
    layer_out = normalize_shared(
        second_mixed, second_sums, columns(second_gain), columns(second_shift), model_width
    ).astype(jnp.bfloat16)
    return (layer_out, new_keys, new_values)


def solution(mesh):
    placed = (
        P("dp", None),
        P("dp", None),
        P(),
        P("dp"),
        P("dp", None),
        P("dp"),
        P("dp", None, "head"),
        P("dp", None, "head"),
        P(None, "head"),
        P("head"),
        P(None, "head"),
        P(None, "head"),
        P("head"),
        P("head", None),
        P(),
        P(),
        P(),
        P(None, "head"),
        P("head"),
        P("head", None),
        P(),
        P(),
        P(),
    )
    return jax.shard_map(
        local,
        mesh=mesh,
        in_specs=placed,
        out_specs=(P("dp", "head"), P("dp", None, "head"), P("dp", None, "head")),
        check_vma=False,
    )
```

```python
import math

import jax
import jax.numpy as jnp
from jax import lax
from jax.experimental import pallas as pl
from jax.sharding import PartitionSpec as P

HD = 128
PEER_MOST = 2


EPSILON = 1e-05


def ancestry(parent_row, draft):
    nodes = jnp.arange(draft, dtype=jnp.int32)
    reach = (parent_row[:, None] == nodes[None, :]).astype(jnp.float32) + jnp.eye(
        draft, dtype=jnp.float32
    )
    for turn in range(max(1, draft.bit_length())):
        reach = jnp.minimum(jnp.dot(reach, reach, precision=lax.Precision.HIGHEST), 1.0)
    return reach > 0.5


def normalize(mixed, gain, shift):
    center = jnp.mean(mixed, axis=-1, keepdims=True)
    square = jnp.mean(mixed * mixed, axis=-1, keepdims=True)
    return (mixed - center) * lax.rsqrt(square - center * center + EPSILON) * gain + shift


def normalize_shared(mixed, sums, gain, shift, model_width):
    center = (sums[0] / model_width)[:, None]
    square = (sums[1] / model_width)[:, None]
    return (mixed - center) * lax.rsqrt(square - center * center + EPSILON) * gain + shift


def split_three(values):
    high = values.astype(jnp.bfloat16)
    rest = values - high.astype(jnp.float32)
    middle = rest.astype(jnp.bfloat16)
    low = (rest - middle.astype(jnp.float32)).astype(jnp.bfloat16)
    return jnp.stack([high, middle, low], axis=1)


def join_three(pieces):
    wide = pieces.astype(jnp.float32)
    return wide[:, 0] + (wide[:, 1] + wide[:, 2])


def ffn_block(attn_ref, hid_ref, bout_ref, gain_ref, shift_ref, wup_ref, bup_ref, wdown_ref, normed_ref, down_ref):
    mixed = attn_ref[...].astype(jnp.float32) + bout_ref[...] + hid_ref[...].astype(jnp.float32)
    center = jnp.mean(mixed, axis=-1, keepdims=True)
    square = jnp.mean(mixed * mixed, axis=-1, keepdims=True)
    normed = ((mixed - center) * lax.rsqrt(square - center * center + EPSILON) * gain_ref[...] + shift_ref[...]).astype(jnp.bfloat16)
    normed_ref[...] = normed
    raised = jnp.dot(normed, wup_ref[...], preferred_element_type=jnp.float32) + bup_ref[...]
    inner = jax.nn.gelu(raised, approximate=True).astype(jnp.bfloat16)
    down_ref[...] = jnp.dot(inner, wdown_ref[...], preferred_element_type=jnp.float32).astype(jnp.bfloat16)

def feed_forward(attn, hidden, b_out, gain, shift, w_up, b_up, w_down, block=128):
    tokens, model = hidden.shape
    units = w_up.shape[1]
    row = lambda i: (i, 0)
    fixed = lambda i: (0, 0)
    return pl.pallas_call(
        ffn_block,
        grid=(tokens // block,),
        in_specs=[
            pl.BlockSpec((block, model), row),
            pl.BlockSpec((block, model), row),
            pl.BlockSpec((1, model), fixed),
            pl.BlockSpec((1, model), fixed),
            pl.BlockSpec((1, model), fixed),
            pl.BlockSpec((model, units), fixed),
            pl.BlockSpec((1, units), fixed),
            pl.BlockSpec((units, model), fixed),
        ],
        out_specs=[pl.BlockSpec((block, model), row), pl.BlockSpec((block, model), row)],
        out_shape=[jax.ShapeDtypeStruct((tokens, model), jnp.bfloat16)] * 2,
        cost_estimate=pl.CostEstimate(flops=4 * tokens * model * units, transcendentals=tokens * units, bytes_accessed=2 * (4 * tokens * model + 2 * model * units)),
    )(attn, hidden, b_out.reshape(1, -1), gain.reshape(1, -1), shift.reshape(1, -1), w_up, b_up.reshape(1, -1), w_down)


def local(
    hidden,
    parents,
    owner_slot,
    slot_lengths,
    accepted_path,
    accepted_count,
    cache_keys,
    cache_values,
    w_query,
    b_query,
    w_key,
    w_value,
    b_value,
    w_out,
    b_out,
    first_gain,
    first_shift,
    w_up,
    b_up,
    w_down,
    b_down,
    second_gain,
    second_shift,
):
    requests = parents.shape[0]
    draft = parents.shape[1]
    tokens = hidden.shape[0]
    model_width = hidden.shape[1]
    width = w_query.shape[1]
    local_heads = width // HD
    capacity = cache_keys.shape[1]
    block = min(capacity, 256)
    shards = lax.axis_size("dp")
    myself = lax.axis_index("dp")
    scale = 1.0 / math.sqrt(HD)
    queries = (jnp.dot(hidden, w_query, preferred_element_type=jnp.float32) + b_query).astype(
        jnp.bfloat16
    )
    key_rows = jnp.dot(hidden, w_key, preferred_element_type=jnp.float32).astype(jnp.bfloat16)
    value_rows = (jnp.dot(hidden, w_value, preferred_element_type=jnp.float32) + b_value).astype(
        jnp.bfloat16
    )
    local_ids = jnp.arange(requests, dtype=jnp.int32)
    levels = jnp.arange(accepted_path.shape[1], dtype=jnp.int32)
    chosen = local_ids[:, None] * draft + accepted_path
    usable = (levels[None, :] < accepted_count[:, None])[..., None]
    kept_keys = jnp.where(usable, key_rows[chosen], jnp.zeros((), jnp.bfloat16))
    kept_values = jnp.where(usable, value_rows[chosen], jnp.zeros((), jnp.bfloat16))
    tree_queries = queries.reshape(requests, draft, local_heads, HD)
    tree_keys = key_rows.reshape(requests, draft, local_heads, HD)
    tree_values = value_rows.reshape(requests, draft, local_heads, HD)
    lineage = jax.vmap(lambda parent_row: ancestry(parent_row, draft))(parents)
    tree_scores = (
        jnp.einsum("rqhd,rkhd->rhqk", tree_queries, tree_keys, preferred_element_type=jnp.float32)
        * scale
    )
    tree_scores = jnp.where(lineage[:, None], tree_scores, -jnp.inf)
    tree_top = jnp.max(tree_scores, axis=3, keepdims=True)
    tree_exp = jnp.exp(tree_scores - tree_top)
    tree_total = jnp.sum(tree_exp, axis=3, keepdims=True)
    tree_probs = tree_exp.astype(jnp.bfloat16)
    tree_part = jnp.einsum(
        "rhqk,rkhd->rqhd", tree_probs, tree_values, preferred_element_type=jnp.float32
    ) / jnp.transpose(tree_total, (0, 2, 1, 3))
    tree_lse = jnp.transpose((tree_top + jnp.log(tree_total))[..., 0], (0, 2, 1))[..., None]
    my_owner = lax.dynamic_slice_in_dim(owner_slot, myself * requests, requests)
    target = my_owner // requests
    earlier = local_ids[None, :] < local_ids[:, None]
    same_target = target[None, :] == target[:, None]
    rank = jnp.sum((earlier & same_target).astype(jnp.int32), axis=1)
    my_slots = myself * requests + local_ids
    every_id = jnp.arange(owner_slot.shape[0], dtype=jnp.int32)
    source_request = jnp.sum(
        jnp.where(owner_slot[None, :] == my_slots[:, None], every_id[None, :], 0), axis=1
    )
    source = source_request // requests
    source_local = source_request % requests
    source_targets = owner_slot.reshape(shards, requests)[source] // requests
    source_rank = jnp.sum(
        ((local_ids[None, :] < source_local[:, None]) & (source_targets == myself)).astype(
            jnp.int32
        ),
        axis=1,
    )

    shaped_queries = queries.reshape(requests, draft, width)
    slots_total = shards * PEER_MOST
    send_index = target * PEER_MOST + rank
    receive_index = source * PEER_MOST + source_rank
    slot_ids = jnp.arange(slots_total, dtype=jnp.int32)

    def spread(values, index):
        placing = (index[None, :] == slot_ids[:, None]).astype(values.dtype)
        flat = values.reshape(values.shape[0], -1)
        placed = jnp.dot(placing, flat, preferred_element_type=jnp.float32).astype(values.dtype)
        return placed.reshape((slots_total,) + values.shape[1:])

    arrived = lax.all_to_all(
        spread(shaped_queries, send_index), "dp", split_axis=0, concat_axis=0, tiled=True
    )
    kept = lax.all_to_all(
        spread(jnp.concatenate([kept_keys, kept_values], axis=1), send_index),
        "dp",
        split_axis=0,
        concat_axis=0,
        tiled=True,
    )[receive_index]
    owned_queries = arrived[receive_index].reshape(requests, draft, local_heads, HD)
    new_keys = kept[:, : kept_keys.shape[1]]
    new_values = kept[:, kept_keys.shape[1] :]
    slot_keys = cache_keys.reshape(requests, capacity, local_heads, HD)
    slot_values = cache_values.reshape(requests, capacity, local_heads, HD)
    scores = (
        jnp.einsum(
            "sqhd,skhd->shqk", owned_queries, slot_keys, preferred_element_type=jnp.float32
        )
        * scale
    )
    living = jnp.arange(capacity, dtype=jnp.int32)[None, :] < slot_lengths[:, None]
    scores = jnp.where(living[:, None, None, :], scores, -jnp.inf)
    cache_top = jnp.max(scores, axis=3, keepdims=True)
    cache_exp = jnp.exp(scores - cache_top)
    cache_total = jnp.sum(cache_exp, axis=3, keepdims=True)
    cache_probs = cache_exp.astype(jnp.bfloat16)
    gathered = jnp.einsum(
        "shqk,skhd->sqhd", cache_probs, slot_values, preferred_element_type=jnp.float32
    )
    owned_part = (
        (gathered / jnp.transpose(cache_total, (0, 2, 1, 3)))
        .astype(jnp.bfloat16)
        .reshape(requests, draft, width)
    )
    owned_lse = (cache_top + jnp.log(cache_total))[..., 0]
    lse_flat = split_three(owned_lse).reshape(requests, -1)
    lse_rows = -(-lse_flat.shape[1] // width)
    lse_flat = jnp.pad(lse_flat, ((0, 0), (0, lse_rows * width - lse_flat.shape[1])))
    back = jnp.concatenate(
        [
            spread(owned_part, receive_index),
            spread(lse_flat, receive_index).reshape(slots_total, lse_rows, width),
        ],
        axis=1,
    )
    returned = lax.all_to_all(back, "dp", split_axis=0, concat_axis=0, tiled=True)[send_index]
    cache_part = returned[:, :draft]
    lse_back = returned[:, draft:].reshape(requests, -1)[:, : 3 * local_heads * draft]
    cache_lse = join_three(lse_back.reshape(requests, 3, local_heads, draft))
    cache_weight = jnp.transpose(cache_lse, (0, 2, 1))[..., None]
    larger = jnp.maximum(cache_weight, tree_lse)
    cache_share = jnp.exp(cache_weight - larger)
    tree_share = jnp.exp(tree_lse - larger)
    blended = (
        cache_share * cache_part.astype(jnp.float32).reshape(requests, draft, local_heads, HD)
        + tree_share * tree_part
    ) / (cache_share + tree_share)
    attended = blended.astype(jnp.bfloat16).reshape(tokens, width)
    attention_term = jnp.dot(attended, w_out, preferred_element_type=jnp.float32)
    feature = model_width // lax.axis_size("head")
    offset = lax.axis_index("head") * feature

    def columns(values):
        return lax.dynamic_slice_in_dim(values, offset, feature, values.ndim - 1)

    attention_sum = lax.psum(attention_term.astype(jnp.bfloat16), "head")
    first_normed, down_part = feed_forward(
        attention_sum, hidden, b_out, first_gain, first_shift, w_up, b_up, w_down
    )
    down_share = lax.psum_scatter(
        down_part, "head", scatter_dimension=1, tiled=True
    ).astype(jnp.float32)
    second_mixed = down_share + columns(b_down) + columns(first_normed).astype(jnp.float32)
    heads_along = lax.axis_size("head")
    own_sums = jnp.stack(
        [jnp.sum(second_mixed, axis=1), jnp.sum(second_mixed * second_mixed, axis=1)]
    )
    second_sums = jnp.sum(
        lax.all_to_all(
            jnp.broadcast_to(own_sums[None], (heads_along,) + own_sums.shape),
            "head",
            0,
            0,
            tiled=False,
        ),
        axis=0,
    )
    layer_out = normalize_shared(
        second_mixed, second_sums, columns(second_gain), columns(second_shift), model_width
    ).astype(jnp.bfloat16)
    return (layer_out, new_keys, new_values)


def solution(mesh):
    placed = (
        P("dp", None),
        P("dp", None),
        P(),
        P("dp"),
        P("dp", None),
        P("dp"),
        P("dp", None, "head"),
        P("dp", None, "head"),
        P(None, "head"),
        P("head"),
        P(None, "head"),
        P(None, "head"),
        P("head"),
        P("head", None),
        P(),
        P(),
        P(),
        P(None, "head"),
        P("head"),
        P("head", None),
        P(),
        P(),
        P(),
    )
    return jax.shard_map(
        local,
        mesh=mesh,
        in_specs=placed,
        out_specs=(P("dp", "head"), P("dp", None, "head"), P("dp", None, "head")),
        check_vma=False,
    )
```

```python
import math

import jax
import jax.numpy as jnp
from jax import lax
from jax.experimental import pallas as pl
from jax.experimental.pallas import tpu as pltpu
from jax.sharding import PartitionSpec as P

HD = 128
PEER_MOST = 2


EPSILON = 1e-05


def ancestry(parent_row, draft):
    nodes = jnp.arange(draft, dtype=jnp.int32)
    reach = (parent_row[:, None] == nodes[None, :]).astype(jnp.float32) + jnp.eye(
        draft, dtype=jnp.float32
    )
    for turn in range(max(1, draft.bit_length())):
        reach = jnp.minimum(jnp.dot(reach, reach, precision=lax.Precision.HIGHEST), 1.0)
    return reach > 0.5


def normalize(mixed, gain, shift):
    center = jnp.mean(mixed, axis=-1, keepdims=True)
    square = jnp.mean(mixed * mixed, axis=-1, keepdims=True)
    return (mixed - center) * lax.rsqrt(square - center * center + EPSILON) * gain + shift


def normalize_shared(mixed, sums, gain, shift, model_width):
    center = (sums[0] / model_width)[:, None]
    square = (sums[1] / model_width)[:, None]
    return (mixed - center) * lax.rsqrt(square - center * center + EPSILON) * gain + shift


def ffn_block(attn_ref, hid_ref, bout_ref, gain_ref, shift_ref, wup_ref, bup_ref, wdown_ref, normed_ref, down_ref):
    mixed = attn_ref[...].astype(jnp.float32) + bout_ref[...] + hid_ref[...].astype(jnp.float32)
    center = jnp.mean(mixed, axis=-1, keepdims=True)
    square = jnp.mean(mixed * mixed, axis=-1, keepdims=True)
    normed = ((mixed - center) * lax.rsqrt(square - center * center + EPSILON) * gain_ref[...] + shift_ref[...]).astype(jnp.bfloat16)
    normed_ref[...] = normed
    raised = jnp.dot(normed, wup_ref[...], preferred_element_type=jnp.float32) + bup_ref[...]
    inner = jax.nn.gelu(raised, approximate=True).astype(jnp.bfloat16)
    down_ref[...] = jnp.dot(inner, wdown_ref[...], preferred_element_type=jnp.float32).astype(jnp.bfloat16)

def feed_forward(attn, hidden, b_out, gain, shift, w_up, b_up, w_down, block=128):
    tokens, model = hidden.shape
    units = w_up.shape[1]
    row = lambda i: (i, 0)
    fixed = lambda i: (0, 0)
    return pl.pallas_call(
        ffn_block,
        grid=(tokens // block,),
        in_specs=[
            pl.BlockSpec((block, model), row),
            pl.BlockSpec((block, model), row),
            pl.BlockSpec((1, model), fixed),
            pl.BlockSpec((1, model), fixed),
            pl.BlockSpec((1, model), fixed),
            pl.BlockSpec((model, units), fixed),
            pl.BlockSpec((1, units), fixed),
            pl.BlockSpec((units, model), fixed),
        ],
        out_specs=[pl.BlockSpec((block, model), row), pl.BlockSpec((block, model), row)],
        out_shape=[jax.ShapeDtypeStruct((tokens, model), jnp.bfloat16)] * 2,
        cost_estimate=pl.CostEstimate(flops=4 * tokens * model * units, transcendentals=tokens * units, bytes_accessed=2 * (4 * tokens * model + 2 * model * units)),
    )(attn, hidden, b_out.reshape(1, -1), gain.reshape(1, -1), shift.reshape(1, -1), w_up, b_up.reshape(1, -1), w_down)


def attend_block(where_ref, length_ref, query_ref, key_ref, value_ref, back_ref):
    slot = pl.program_id(0)
    length = length_ref[slot]
    draft = query_ref.shape[1]
    heads = query_ref.shape[2] // HD
    width = query_ref.shape[2]
    capacity = key_ref.shape[1]
    living = lax.broadcasted_iota(jnp.int32, (draft, capacity), 1) < length
    back_ref[0, draft:, :] = jnp.zeros((back_ref.shape[1] - draft, width), back_ref.dtype)
    for head in range(heads):
        cols = slice(head * HD, (head + 1) * HD)
        query = query_ref[0, :, cols]
        scores = lax.dot_general(
            query, key_ref[0, :, cols], (((1,), (1,)), ((), ())), preferred_element_type=jnp.float32
        ) * (1.0 / math.sqrt(HD))
        scores = jnp.where(living, scores, -jnp.inf)
        top = jnp.max(scores, axis=1, keepdims=True)
        weights = jnp.exp(scores - top)
        total = jnp.sum(weights, axis=1, keepdims=True)
        mixed = jnp.dot(weights.astype(jnp.bfloat16), value_ref[0, :, cols], preferred_element_type=jnp.float32)
        back_ref[0, :draft, cols] = (mixed / total).astype(back_ref.dtype)
        lse = jnp.broadcast_to(top + jnp.log(total), (draft, 128)).T[0:1, :draft]
        high = lse.astype(jnp.bfloat16)
        rest = lse - high.astype(jnp.float32)
        middle = rest.astype(jnp.bfloat16)
        low = (rest - middle.astype(jnp.float32)).astype(jnp.bfloat16)
        back_ref[0, draft + head : draft + head + 1, 0:draft] = high
        back_ref[0, draft + head : draft + head + 1, draft : 2 * draft] = middle
        back_ref[0, draft + head : draft + head + 1, 2 * draft : 3 * draft] = low

def attend(arrived, where, lengths, keys, values):
    positions, draft, width = arrived.shape
    slots, capacity, _ = keys.shape
    heads = width // HD
    rows = draft + heads
    grid_spec = pltpu.PrefetchScalarGridSpec(
        num_scalar_prefetch=2,
        grid=(slots,),
        in_specs=[
            pl.BlockSpec((1, draft, width), lambda s, w, n: (w[s], 0, 0)),
            pl.BlockSpec((1, capacity, width), lambda s, w, n: (s, 0, 0)),
            pl.BlockSpec((1, capacity, width), lambda s, w, n: (s, 0, 0)),
        ],
        out_specs=pl.BlockSpec((1, rows, width), lambda s, w, n: (w[s], 0, 0)),
    )
    return pl.pallas_call(
        attend_block,
        grid_spec=grid_spec,
        out_shape=jax.ShapeDtypeStruct((positions, rows, width), arrived.dtype),
    )(where, lengths, arrived, keys, values)


def local(
    hidden,
    parents,
    owner_slot,
    slot_lengths,
    accepted_path,
    accepted_count,
    cache_keys,
    cache_values,
    w_query,
    b_query,
    w_key,
    w_value,
    b_value,
    w_out,
    b_out,
    first_gain,
    first_shift,
    w_up,
    b_up,
    w_down,
    b_down,
    second_gain,
    second_shift,
):
    requests = parents.shape[0]
    draft = parents.shape[1]
    tokens = hidden.shape[0]
    model_width = hidden.shape[1]
    width = w_query.shape[1]
    local_heads = width // HD
    capacity = cache_keys.shape[1]
    block = min(capacity, 256)
    shards = lax.axis_size("dp")
    myself = lax.axis_index("dp")
    scale = 1.0 / math.sqrt(HD)
    queries = (jnp.dot(hidden, w_query, preferred_element_type=jnp.float32) + b_query).astype(
        jnp.bfloat16
    )
    key_rows = jnp.dot(hidden, w_key, preferred_element_type=jnp.float32).astype(jnp.bfloat16)
    value_rows = (jnp.dot(hidden, w_value, preferred_element_type=jnp.float32) + b_value).astype(
        jnp.bfloat16
    )
    local_ids = jnp.arange(requests, dtype=jnp.int32)
    levels = jnp.arange(accepted_path.shape[1], dtype=jnp.int32)
    chosen = local_ids[:, None] * draft + accepted_path
    usable = (levels[None, :] < accepted_count[:, None])[..., None]
    kept_keys = jnp.where(usable, key_rows[chosen], jnp.zeros((), jnp.bfloat16))
    kept_values = jnp.where(usable, value_rows[chosen], jnp.zeros((), jnp.bfloat16))
    tree_queries = queries.reshape(requests, draft, local_heads, HD)
    tree_keys = key_rows.reshape(requests, draft, local_heads, HD)
    tree_values = value_rows.reshape(requests, draft, local_heads, HD)
    lineage = jax.vmap(lambda parent_row: ancestry(parent_row, draft))(parents)
    tree_scores = (
        jnp.einsum("rqhd,rkhd->rhqk", tree_queries, tree_keys, preferred_element_type=jnp.float32)
        * scale
    )
    tree_scores = jnp.where(lineage[:, None], tree_scores, -jnp.inf)
    tree_top = jnp.max(tree_scores, axis=3, keepdims=True)
    tree_exp = jnp.exp(tree_scores - tree_top)
    tree_total = jnp.sum(tree_exp, axis=3, keepdims=True)
    tree_probs = tree_exp.astype(jnp.bfloat16)
    tree_part = jnp.einsum(
        "rhqk,rkhd->rqhd", tree_probs, tree_values, preferred_element_type=jnp.float32
    ) / jnp.transpose(tree_total, (0, 2, 1, 3))
    tree_lse = jnp.transpose((tree_top + jnp.log(tree_total))[..., 0], (0, 2, 1))[..., None]
    my_owner = lax.dynamic_slice_in_dim(owner_slot, myself * requests, requests)
    target = my_owner // requests
    earlier = local_ids[None, :] < local_ids[:, None]
    same_target = target[None, :] == target[:, None]
    rank = jnp.sum((earlier & same_target).astype(jnp.int32), axis=1)
    my_slots = myself * requests + local_ids
    every_id = jnp.arange(owner_slot.shape[0], dtype=jnp.int32)
    source_request = jnp.sum(
        jnp.where(owner_slot[None, :] == my_slots[:, None], every_id[None, :], 0), axis=1
    )
    source = source_request // requests
    source_local = source_request % requests
    source_targets = owner_slot.reshape(shards, requests)[source] // requests
    source_rank = jnp.sum(
        ((local_ids[None, :] < source_local[:, None]) & (source_targets == myself)).astype(
            jnp.int32
        ),
        axis=1,
    )

    shaped_queries = queries.reshape(requests, draft, width)
    slots_total = shards * PEER_MOST
    send_index = target * PEER_MOST + rank
    receive_index = source * PEER_MOST + source_rank
    slot_ids = jnp.arange(slots_total, dtype=jnp.int32)

    def spread(values, index):
        placing = (index[None, :] == slot_ids[:, None]).astype(values.dtype)
        flat = values.reshape(values.shape[0], -1)
        placed = jnp.dot(placing, flat, preferred_element_type=jnp.float32).astype(values.dtype)
        return placed.reshape((slots_total,) + values.shape[1:])

    arrived = lax.all_to_all(
        spread(shaped_queries, send_index), "dp", split_axis=0, concat_axis=0, tiled=True
    )
    kept = lax.all_to_all(
        spread(jnp.concatenate([kept_keys, kept_values], axis=1), send_index),
        "dp",
        split_axis=0,
        concat_axis=0,
        tiled=True,
    )[receive_index]
    new_keys = kept[:, : kept_keys.shape[1]]
    new_values = kept[:, kept_keys.shape[1] :]
    back = attend(arrived, receive_index, slot_lengths, cache_keys, cache_values)
    returned = lax.all_to_all(back, "dp", split_axis=0, concat_axis=0, tiled=True)[send_index]
    cache_part = returned[:, :draft]
    lse_rows = returned[:, draft : draft + local_heads].astype(jnp.float32)
    cache_lse = lse_rows[..., :draft] + (
        lse_rows[..., draft : 2 * draft] + lse_rows[..., 2 * draft : 3 * draft]
    )
    cache_weight = jnp.transpose(cache_lse, (0, 2, 1))[..., None]
    larger = jnp.maximum(cache_weight, tree_lse)
    cache_share = jnp.exp(cache_weight - larger)
    tree_share = jnp.exp(tree_lse - larger)
    blended = (
        cache_share * cache_part.astype(jnp.float32).reshape(requests, draft, local_heads, HD)
        + tree_share * tree_part
    ) / (cache_share + tree_share)
    attended = blended.astype(jnp.bfloat16).reshape(tokens, width)
    attention_term = jnp.dot(attended, w_out, preferred_element_type=jnp.float32)
    feature = model_width // lax.axis_size("head")
    offset = lax.axis_index("head") * feature

    def columns(values):
        return lax.dynamic_slice_in_dim(values, offset, feature, values.ndim - 1)

    attention_sum = lax.psum(attention_term.astype(jnp.bfloat16), "head")
    first_normed, down_part = feed_forward(
        attention_sum, hidden, b_out, first_gain, first_shift, w_up, b_up, w_down
    )
    down_share = lax.psum_scatter(
        down_part, "head", scatter_dimension=1, tiled=True
    ).astype(jnp.float32)
    second_mixed = down_share + columns(b_down) + columns(first_normed).astype(jnp.float32)
    heads_along = lax.axis_size("head")
    own_sums = jnp.stack(
        [jnp.sum(second_mixed, axis=1), jnp.sum(second_mixed * second_mixed, axis=1)]
    )
    second_sums = jnp.sum(
        lax.all_to_all(
            jnp.broadcast_to(own_sums[None], (heads_along,) + own_sums.shape),
            "head",
            0,
            0,
            tiled=False,
        ),
        axis=0,
    )
    layer_out = normalize_shared(
        second_mixed, second_sums, columns(second_gain), columns(second_shift), model_width
    ).astype(jnp.bfloat16)
    return (layer_out, new_keys, new_values)


def solution(mesh):
    placed = (
        P("dp", None),
        P("dp", None),
        P(),
        P("dp"),
        P("dp", None),
        P("dp"),
        P("dp", None, "head"),
        P("dp", None, "head"),
        P(None, "head"),
        P("head"),
        P(None, "head"),
        P(None, "head"),
        P("head"),
        P("head", None),
        P(),
        P(),
        P(),
        P(None, "head"),
        P("head"),
        P("head", None),
        P(),
        P(),
        P(),
    )
    return jax.shard_map(
        local,
        mesh=mesh,
        in_specs=placed,
        out_specs=(P("dp", "head"), P("dp", None, "head"), P("dp", None, "head")),
        check_vma=False,
    )
```

```python
import math

import jax
import jax.numpy as jnp
from jax import lax
from jax.experimental import pallas as pl
from jax.experimental.pallas import tpu as pltpu
from jax.sharding import PartitionSpec as P

HD = 128
PEER_MOST = 2


EPSILON = 1e-05


def ancestry(parent_row, draft):
    nodes = jnp.arange(draft, dtype=jnp.int32)
    reach = (parent_row[:, None] == nodes[None, :]).astype(jnp.float32) + jnp.eye(
        draft, dtype=jnp.float32
    )
    for turn in range(max(1, draft.bit_length())):
        reach = jnp.minimum(jnp.dot(reach, reach, precision=lax.Precision.HIGHEST), 1.0)
    return reach > 0.5


def normalize(mixed, gain, shift):
    center = jnp.mean(mixed, axis=-1, keepdims=True)
    square = jnp.mean(mixed * mixed, axis=-1, keepdims=True)
    return (mixed - center) * lax.rsqrt(square - center * center + EPSILON) * gain + shift


def normalize_shared(mixed, sums, gain, shift, model_width):
    center = (sums[0] / model_width)[:, None]
    square = (sums[1] / model_width)[:, None]
    return (mixed - center) * lax.rsqrt(square - center * center + EPSILON) * gain + shift


def ffn_block(attn_ref, hid_ref, bout_ref, gain_ref, shift_ref, wup_ref, bup_ref, wdown_ref, normed_ref, down_ref):
    mixed = attn_ref[...].astype(jnp.float32) + bout_ref[...] + hid_ref[...].astype(jnp.float32)
    center = jnp.mean(mixed, axis=-1, keepdims=True)
    square = jnp.mean(mixed * mixed, axis=-1, keepdims=True)
    normed = ((mixed - center) * lax.rsqrt(square - center * center + EPSILON) * gain_ref[...] + shift_ref[...]).astype(jnp.bfloat16)
    normed_ref[...] = normed
    raised = jnp.dot(normed, wup_ref[...], preferred_element_type=jnp.float32) + bup_ref[...]
    inner = jax.nn.gelu(raised, approximate=True).astype(jnp.bfloat16)
    down_ref[...] = jnp.dot(inner, wdown_ref[...], preferred_element_type=jnp.float32).astype(jnp.bfloat16)

def feed_forward(attn, hidden, b_out, gain, shift, w_up, b_up, w_down, block=128):
    tokens, model = hidden.shape
    units = w_up.shape[1]
    row = lambda i: (i, 0)
    fixed = lambda i: (0, 0)
    return pl.pallas_call(
        ffn_block,
        grid=(tokens // block,),
        in_specs=[
            pl.BlockSpec((block, model), row),
            pl.BlockSpec((block, model), row),
            pl.BlockSpec((1, model), fixed),
            pl.BlockSpec((1, model), fixed),
            pl.BlockSpec((1, model), fixed),
            pl.BlockSpec((model, units), fixed),
            pl.BlockSpec((1, units), fixed),
            pl.BlockSpec((units, model), fixed),
        ],
        out_specs=[pl.BlockSpec((block, model), row), pl.BlockSpec((block, model), row)],
        out_shape=[jax.ShapeDtypeStruct((tokens, model), jnp.bfloat16)] * 2,
        cost_estimate=pl.CostEstimate(flops=4 * tokens * model * units, transcendentals=tokens * units, bytes_accessed=2 * (4 * tokens * model + 2 * model * units)),
    )(attn, hidden, b_out.reshape(1, -1), gain.reshape(1, -1), shift.reshape(1, -1), w_up, b_up.reshape(1, -1), w_down)


def attend_block(where_ref, length_ref, query_ref, key_ref, value_ref, back_ref):
    slot = pl.program_id(0)
    length = length_ref[slot]
    draft = query_ref.shape[1]
    heads = query_ref.shape[2] // HD
    width = query_ref.shape[2]
    capacity = key_ref.shape[1]
    living = lax.broadcasted_iota(jnp.int32, (draft, capacity), 1) < length
    back_ref[0, draft:, :] = jnp.zeros((back_ref.shape[1] - draft, width), back_ref.dtype)
    for head in range(heads):
        cols = slice(head * HD, (head + 1) * HD)
        query = query_ref[0, :, cols]
        scores = lax.dot_general(
            query, key_ref[0, :, cols], (((1,), (1,)), ((), ())), preferred_element_type=jnp.float32
        ) * (1.0 / math.sqrt(HD))
        scores = jnp.where(living, scores, -jnp.inf)
        top = jnp.max(scores, axis=1, keepdims=True)
        weights = jnp.exp(scores - top)
        total = jnp.sum(weights, axis=1, keepdims=True)
        mixed = jnp.dot(weights.astype(jnp.bfloat16), value_ref[0, :, cols], preferred_element_type=jnp.float32)
        back_ref[0, :draft, cols] = (mixed / total).astype(back_ref.dtype)
        lse = jnp.broadcast_to(top + jnp.log(total), (draft, 128)).T[0:1, :draft]
        high = lse.astype(jnp.bfloat16)
        rest = lse - high.astype(jnp.float32)
        middle = rest.astype(jnp.bfloat16)
        low = (rest - middle.astype(jnp.float32)).astype(jnp.bfloat16)
        back_ref[0, draft + head : draft + head + 1, 0:draft] = high
        back_ref[0, draft + head : draft + head + 1, draft : 2 * draft] = middle
        back_ref[0, draft + head : draft + head + 1, 2 * draft : 3 * draft] = low

def attend(arrived, where, lengths, keys, values):
    positions, draft, width = arrived.shape
    slots, capacity, _ = keys.shape
    heads = width // HD
    rows = draft + heads
    grid_spec = pltpu.PrefetchScalarGridSpec(
        num_scalar_prefetch=2,
        grid=(slots,),
        in_specs=[
            pl.BlockSpec((1, draft, width), lambda s, w, n: (w[s], 0, 0)),
            pl.BlockSpec((1, capacity, width), lambda s, w, n: (s, 0, 0)),
            pl.BlockSpec((1, capacity, width), lambda s, w, n: (s, 0, 0)),
        ],
        out_specs=pl.BlockSpec((1, rows, width), lambda s, w, n: (w[s], 0, 0)),
    )
    return pl.pallas_call(
        attend_block,
        grid_spec=grid_spec,
        out_shape=jax.ShapeDtypeStruct((positions, rows, width), arrived.dtype),
    )(where, lengths, arrived, keys, values)


def project_block(where_ref, hidden_ref, weight_ref, bias_ref, query_ref, placed_ref):
    rows = (
        jnp.dot(hidden_ref[...], weight_ref[...], preferred_element_type=jnp.float32)
        + bias_ref[...]
    ).astype(query_ref.dtype)
    query_ref[...] = rows
    placed_ref[0] = rows


def project(hidden, weight, bias, where, positions, draft):
    tokens, model = hidden.shape
    width = weight.shape[1]
    grid_spec = pltpu.PrefetchScalarGridSpec(
        num_scalar_prefetch=1,
        grid=(tokens // draft,),
        in_specs=[
            pl.BlockSpec((draft, model), lambda r, w: (r, 0)),
            pl.BlockSpec((model, width), lambda r, w: (0, 0)),
            pl.BlockSpec((1, width), lambda r, w: (0, 0)),
        ],
        out_specs=[
            pl.BlockSpec((draft, width), lambda r, w: (r, 0)),
            pl.BlockSpec((1, draft, width), lambda r, w: (w[r], 0, 0)),
        ],
    )
    return pl.pallas_call(
        project_block,
        grid_spec=grid_spec,
        out_shape=[
            jax.ShapeDtypeStruct((tokens, width), jnp.bfloat16),
            jax.ShapeDtypeStruct((positions, draft, width), jnp.bfloat16),
        ],
    )(where, hidden, weight, bias.reshape(1, -1))


def local(
    hidden,
    parents,
    owner_slot,
    slot_lengths,
    accepted_path,
    accepted_count,
    cache_keys,
    cache_values,
    w_query,
    b_query,
    w_key,
    w_value,
    b_value,
    w_out,
    b_out,
    first_gain,
    first_shift,
    w_up,
    b_up,
    w_down,
    b_down,
    second_gain,
    second_shift,
):
    requests = parents.shape[0]
    draft = parents.shape[1]
    tokens = hidden.shape[0]
    model_width = hidden.shape[1]
    width = w_query.shape[1]
    local_heads = width // HD
    capacity = cache_keys.shape[1]
    block = min(capacity, 256)
    shards = lax.axis_size("dp")
    myself = lax.axis_index("dp")
    scale = 1.0 / math.sqrt(HD)
    local_ids = jnp.arange(requests, dtype=jnp.int32)
    my_owner = lax.dynamic_slice_in_dim(owner_slot, myself * requests, requests)
    target = my_owner // requests
    earlier = local_ids[None, :] < local_ids[:, None]
    same_target = target[None, :] == target[:, None]
    rank = jnp.sum((earlier & same_target).astype(jnp.int32), axis=1)
    my_slots = myself * requests + local_ids
    every_id = jnp.arange(owner_slot.shape[0], dtype=jnp.int32)
    source_request = jnp.sum(
        jnp.where(owner_slot[None, :] == my_slots[:, None], every_id[None, :], 0), axis=1
    )
    source = source_request // requests
    source_local = source_request % requests
    source_targets = owner_slot.reshape(shards, requests)[source] // requests
    source_rank = jnp.sum(
        ((local_ids[None, :] < source_local[:, None]) & (source_targets == myself)).astype(
            jnp.int32
        ),
        axis=1,
    )
    slots_total = shards * PEER_MOST
    send_index = target * PEER_MOST + rank
    receive_index = source * PEER_MOST + source_rank
    queries, placed_queries = project(hidden, w_query, b_query, send_index, slots_total, draft)
    key_rows = jnp.dot(hidden, w_key, preferred_element_type=jnp.float32).astype(jnp.bfloat16)
    value_rows = (jnp.dot(hidden, w_value, preferred_element_type=jnp.float32) + b_value).astype(
        jnp.bfloat16
    )
    levels = jnp.arange(accepted_path.shape[1], dtype=jnp.int32)
    chosen = local_ids[:, None] * draft + accepted_path
    usable = (levels[None, :] < accepted_count[:, None])[..., None]
    kept_keys = jnp.where(usable, key_rows[chosen], jnp.zeros((), jnp.bfloat16))
    kept_values = jnp.where(usable, value_rows[chosen], jnp.zeros((), jnp.bfloat16))
    tree_queries = queries.reshape(requests, draft, local_heads, HD)
    tree_keys = key_rows.reshape(requests, draft, local_heads, HD)
    tree_values = value_rows.reshape(requests, draft, local_heads, HD)
    lineage = jax.vmap(lambda parent_row: ancestry(parent_row, draft))(parents)
    tree_scores = (
        jnp.einsum("rqhd,rkhd->rhqk", tree_queries, tree_keys, preferred_element_type=jnp.float32)
        * scale
    )
    tree_scores = jnp.where(lineage[:, None], tree_scores, -jnp.inf)
    tree_top = jnp.max(tree_scores, axis=3, keepdims=True)
    tree_exp = jnp.exp(tree_scores - tree_top)
    tree_total = jnp.sum(tree_exp, axis=3, keepdims=True)
    tree_probs = tree_exp.astype(jnp.bfloat16)
    tree_part = jnp.einsum(
        "rhqk,rkhd->rqhd", tree_probs, tree_values, preferred_element_type=jnp.float32
    ) / jnp.transpose(tree_total, (0, 2, 1, 3))
    tree_lse = jnp.transpose((tree_top + jnp.log(tree_total))[..., 0], (0, 2, 1))[..., None]
    slot_ids = jnp.arange(slots_total, dtype=jnp.int32)

    def spread(values, index):
        placing = (index[None, :] == slot_ids[:, None]).astype(values.dtype)
        flat = values.reshape(values.shape[0], -1)
        placed = jnp.dot(placing, flat, preferred_element_type=jnp.float32).astype(values.dtype)
        return placed.reshape((slots_total,) + values.shape[1:])

    arrived = lax.all_to_all(placed_queries, "dp", split_axis=0, concat_axis=0, tiled=True)
    kept = lax.all_to_all(
        spread(jnp.concatenate([kept_keys, kept_values], axis=1), send_index),
        "dp",
        split_axis=0,
        concat_axis=0,
        tiled=True,
    )[receive_index]
    new_keys = kept[:, : kept_keys.shape[1]]
    new_values = kept[:, kept_keys.shape[1] :]
    back = attend(arrived, receive_index, slot_lengths, cache_keys, cache_values)
    returned = lax.all_to_all(back, "dp", split_axis=0, concat_axis=0, tiled=True)[send_index]
    cache_part = returned[:, :draft]
    lse_rows = returned[:, draft : draft + local_heads].astype(jnp.float32)
    cache_lse = lse_rows[..., :draft] + (
        lse_rows[..., draft : 2 * draft] + lse_rows[..., 2 * draft : 3 * draft]
    )
    cache_weight = jnp.transpose(cache_lse, (0, 2, 1))[..., None]
    larger = jnp.maximum(cache_weight, tree_lse)
    cache_share = jnp.exp(cache_weight - larger)
    tree_share = jnp.exp(tree_lse - larger)
    blended = (
        cache_share * cache_part.astype(jnp.float32).reshape(requests, draft, local_heads, HD)
        + tree_share * tree_part
    ) / (cache_share + tree_share)
    attended = blended.astype(jnp.bfloat16).reshape(tokens, width)
    attention_term = jnp.dot(attended, w_out, preferred_element_type=jnp.float32)
    feature = model_width // lax.axis_size("head")
    offset = lax.axis_index("head") * feature

    def columns(values):
        return lax.dynamic_slice_in_dim(values, offset, feature, values.ndim - 1)

    attention_sum = lax.psum(attention_term.astype(jnp.bfloat16), "head")
    first_normed, down_part = feed_forward(
        attention_sum, hidden, b_out, first_gain, first_shift, w_up, b_up, w_down
    )
    down_share = lax.psum_scatter(
        down_part, "head", scatter_dimension=1, tiled=True
    ).astype(jnp.float32)
    second_mixed = down_share + columns(b_down) + columns(first_normed).astype(jnp.float32)
    heads_along = lax.axis_size("head")
    own_sums = jnp.stack(
        [jnp.sum(second_mixed, axis=1), jnp.sum(second_mixed * second_mixed, axis=1)]
    )
    second_sums = jnp.sum(
        lax.all_to_all(
            jnp.broadcast_to(own_sums[None], (heads_along,) + own_sums.shape),
            "head",
            0,
            0,
            tiled=False,
        ),
        axis=0,
    )
    layer_out = normalize_shared(
        second_mixed, second_sums, columns(second_gain), columns(second_shift), model_width
    ).astype(jnp.bfloat16)
    return (layer_out, new_keys, new_values)


def solution(mesh):
    placed = (
        P("dp", None),
        P("dp", None),
        P(),
        P("dp"),
        P("dp", None),
        P("dp"),
        P("dp", None, "head"),
        P("dp", None, "head"),
        P(None, "head"),
        P("head"),
        P(None, "head"),
        P(None, "head"),
        P("head"),
        P("head", None),
        P(),
        P(),
        P(),
        P(None, "head"),
        P("head"),
        P("head", None),
        P(),
        P(),
        P(),
    )
    return jax.shard_map(
        local,
        mesh=mesh,
        in_specs=placed,
        out_specs=(P("dp", "head"), P("dp", None, "head"), P("dp", None, "head")),
        check_vma=False,
    )
```

```python
import math

import jax
import jax.numpy as jnp
from jax import lax
from jax.experimental import pallas as pl
from jax.experimental.pallas import tpu as pltpu
from jax.sharding import PartitionSpec as P

HD = 128
PEER_MOST = 2


EPSILON = 1e-05


def ancestry(parent_row, draft):
    nodes = jnp.arange(draft, dtype=jnp.int32)
    reach = (parent_row[:, None] == nodes[None, :]).astype(jnp.float32) + jnp.eye(
        draft, dtype=jnp.float32
    )
    for turn in range(max(1, draft.bit_length())):
        reach = jnp.minimum(jnp.dot(reach, reach, precision=lax.Precision.HIGHEST), 1.0)
    return reach > 0.5


def normalize(mixed, gain, shift):
    center = jnp.mean(mixed, axis=-1, keepdims=True)
    square = jnp.mean(mixed * mixed, axis=-1, keepdims=True)
    return (mixed - center) * lax.rsqrt(square - center * center + EPSILON) * gain + shift


def normalize_shared(mixed, sums, gain, shift, model_width):
    center = (sums[0] / model_width)[:, None]
    square = (sums[1] / model_width)[:, None]
    return (mixed - center) * lax.rsqrt(square - center * center + EPSILON) * gain + shift


def ffn_block(attn_ref, hid_ref, bout_ref, gain_ref, shift_ref, wup_ref, bup_ref, wdown_ref, normed_ref, down_ref):
    mixed = attn_ref[...].astype(jnp.float32) + bout_ref[...] + hid_ref[...].astype(jnp.float32)
    center = jnp.mean(mixed, axis=-1, keepdims=True)
    square = jnp.mean(mixed * mixed, axis=-1, keepdims=True)
    normed = ((mixed - center) * lax.rsqrt(square - center * center + EPSILON) * gain_ref[...] + shift_ref[...]).astype(jnp.bfloat16)
    normed_ref[...] = normed
    raised = jnp.dot(normed, wup_ref[...], preferred_element_type=jnp.float32) + bup_ref[...]
    inner = jax.nn.gelu(raised, approximate=True).astype(jnp.bfloat16)
    down_ref[...] = jnp.dot(inner, wdown_ref[...], preferred_element_type=jnp.float32).astype(jnp.bfloat16)

def feed_forward(attn, hidden, b_out, gain, shift, w_up, b_up, w_down, block=128):
    tokens, model = hidden.shape
    units = w_up.shape[1]
    row = lambda i: (i, 0)
    fixed = lambda i: (0, 0)
    return pl.pallas_call(
        ffn_block,
        grid=(tokens // block,),
        in_specs=[
            pl.BlockSpec((block, model), row),
            pl.BlockSpec((block, model), row),
            pl.BlockSpec((1, model), fixed),
            pl.BlockSpec((1, model), fixed),
            pl.BlockSpec((1, model), fixed),
            pl.BlockSpec((model, units), fixed),
            pl.BlockSpec((1, units), fixed),
            pl.BlockSpec((units, model), fixed),
        ],
        out_specs=[pl.BlockSpec((block, model), row), pl.BlockSpec((block, model), row)],
        out_shape=[jax.ShapeDtypeStruct((tokens, model), jnp.bfloat16)] * 2,
        cost_estimate=pl.CostEstimate(flops=4 * tokens * model * units, transcendentals=tokens * units, bytes_accessed=2 * (4 * tokens * model + 2 * model * units)),
    )(attn, hidden, b_out.reshape(1, -1), gain.reshape(1, -1), shift.reshape(1, -1), w_up, b_up.reshape(1, -1), w_down)


def attend_block(where_ref, length_ref, query_ref, key_ref, value_ref, back_ref):
    slot = pl.program_id(0)
    length = length_ref[slot]
    draft = query_ref.shape[1]
    heads = query_ref.shape[2] // HD
    width = query_ref.shape[2]
    capacity = key_ref.shape[1]
    living = lax.broadcasted_iota(jnp.int32, (draft, capacity), 1) < length
    back_ref[0, draft:, :] = jnp.zeros((back_ref.shape[1] - draft, width), back_ref.dtype)
    for head in range(heads):
        cols = slice(head * HD, (head + 1) * HD)
        query = query_ref[0, :, cols]
        scores = lax.dot_general(
            query, key_ref[0, :, cols], (((1,), (1,)), ((), ())), preferred_element_type=jnp.float32
        ) * (1.0 / math.sqrt(HD))
        scores = jnp.where(living, scores, -jnp.inf)
        top = jnp.max(scores, axis=1, keepdims=True)
        weights = jnp.exp(scores - top)
        total = jnp.sum(weights, axis=1, keepdims=True)
        mixed = jnp.dot(weights.astype(jnp.bfloat16), value_ref[0, :, cols], preferred_element_type=jnp.float32)
        back_ref[0, :draft, cols] = (mixed / total).astype(back_ref.dtype)
        lse = jnp.broadcast_to(top + jnp.log(total), (draft, 128)).T[0:1, :draft]
        high = lse.astype(jnp.bfloat16)
        rest = lse - high.astype(jnp.float32)
        middle = rest.astype(jnp.bfloat16)
        low = (rest - middle.astype(jnp.float32)).astype(jnp.bfloat16)
        back_ref[0, draft + head : draft + head + 1, 0:draft] = high
        back_ref[0, draft + head : draft + head + 1, draft : 2 * draft] = middle
        back_ref[0, draft + head : draft + head + 1, 2 * draft : 3 * draft] = low

def attend(arrived, where, lengths, keys, values):
    positions, draft, width = arrived.shape
    slots, capacity, _ = keys.shape
    heads = width // HD
    rows = draft + heads
    grid_spec = pltpu.PrefetchScalarGridSpec(
        num_scalar_prefetch=2,
        grid=(slots,),
        in_specs=[
            pl.BlockSpec((1, draft, width), lambda s, w, n: (w[s], 0, 0)),
            pl.BlockSpec((1, capacity, width), lambda s, w, n: (s, 0, 0)),
            pl.BlockSpec((1, capacity, width), lambda s, w, n: (s, 0, 0)),
        ],
        out_specs=pl.BlockSpec((1, rows, width), lambda s, w, n: (w[s], 0, 0)),
    )
    return pl.pallas_call(
        attend_block,
        grid_spec=grid_spec,
        out_shape=jax.ShapeDtypeStruct((positions, rows, width), arrived.dtype),
    )(where, lengths, arrived, keys, values)


def project_block(where_ref, hidden_ref, weight_ref, bias_ref, query_ref, placed_ref):
    draft = placed_ref.shape[1]
    rows = (
        jnp.dot(hidden_ref[...], weight_ref[...], preferred_element_type=jnp.float32)
        + bias_ref[...]
    ).astype(query_ref.dtype)
    query_ref[...] = rows
    for request in range(query_ref.shape[0] // draft):
        placed_ref[where_ref[request]] = rows[request * draft : (request + 1) * draft]


def project(hidden, weight, bias, where, positions, draft):
    tokens, model = hidden.shape
    width = weight.shape[1]
    grid_spec = pltpu.PrefetchScalarGridSpec(
        num_scalar_prefetch=1,
        grid=(1,),
        in_specs=[
            pl.BlockSpec((tokens, model), lambda r, w: (0, 0)),
            pl.BlockSpec((model, width), lambda r, w: (0, 0)),
            pl.BlockSpec((1, width), lambda r, w: (0, 0)),
        ],
        out_specs=[
            pl.BlockSpec((tokens, width), lambda r, w: (0, 0)),
            pl.BlockSpec((positions, draft, width), lambda r, w: (0, 0, 0)),
        ],
    )
    return pl.pallas_call(
        project_block,
        grid_spec=grid_spec,
        out_shape=[
            jax.ShapeDtypeStruct((tokens, width), jnp.bfloat16),
            jax.ShapeDtypeStruct((positions, draft, width), jnp.bfloat16),
        ],
    )(where, hidden, weight, bias.reshape(1, -1))


def local(
    hidden,
    parents,
    owner_slot,
    slot_lengths,
    accepted_path,
    accepted_count,
    cache_keys,
    cache_values,
    w_query,
    b_query,
    w_key,
    w_value,
    b_value,
    w_out,
    b_out,
    first_gain,
    first_shift,
    w_up,
    b_up,
    w_down,
    b_down,
    second_gain,
    second_shift,
):
    requests = parents.shape[0]
    draft = parents.shape[1]
    tokens = hidden.shape[0]
    model_width = hidden.shape[1]
    width = w_query.shape[1]
    local_heads = width // HD
    capacity = cache_keys.shape[1]
    block = min(capacity, 256)
    shards = lax.axis_size("dp")
    myself = lax.axis_index("dp")
    scale = 1.0 / math.sqrt(HD)
    local_ids = jnp.arange(requests, dtype=jnp.int32)
    my_owner = lax.dynamic_slice_in_dim(owner_slot, myself * requests, requests)
    target = my_owner // requests
    earlier = local_ids[None, :] < local_ids[:, None]
    same_target = target[None, :] == target[:, None]
    rank = jnp.sum((earlier & same_target).astype(jnp.int32), axis=1)
    my_slots = myself * requests + local_ids
    every_id = jnp.arange(owner_slot.shape[0], dtype=jnp.int32)
    source_request = jnp.sum(
        jnp.where(owner_slot[None, :] == my_slots[:, None], every_id[None, :], 0), axis=1
    )
    source = source_request // requests
    source_local = source_request % requests
    source_targets = owner_slot.reshape(shards, requests)[source] // requests
    source_rank = jnp.sum(
        ((local_ids[None, :] < source_local[:, None]) & (source_targets == myself)).astype(
            jnp.int32
        ),
        axis=1,
    )
    slots_total = shards * PEER_MOST
    send_index = target * PEER_MOST + rank
    receive_index = source * PEER_MOST + source_rank
    queries, placed_queries = project(hidden, w_query, b_query, send_index, slots_total, draft)
    key_rows = jnp.dot(hidden, w_key, preferred_element_type=jnp.float32).astype(jnp.bfloat16)
    value_rows = (jnp.dot(hidden, w_value, preferred_element_type=jnp.float32) + b_value).astype(
        jnp.bfloat16
    )
    levels = jnp.arange(accepted_path.shape[1], dtype=jnp.int32)
    chosen = local_ids[:, None] * draft + accepted_path
    usable = (levels[None, :] < accepted_count[:, None])[..., None]
    kept_keys = jnp.where(usable, key_rows[chosen], jnp.zeros((), jnp.bfloat16))
    kept_values = jnp.where(usable, value_rows[chosen], jnp.zeros((), jnp.bfloat16))
    tree_queries = queries.reshape(requests, draft, local_heads, HD)
    tree_keys = key_rows.reshape(requests, draft, local_heads, HD)
    tree_values = value_rows.reshape(requests, draft, local_heads, HD)
    lineage = jax.vmap(lambda parent_row: ancestry(parent_row, draft))(parents)
    tree_scores = (
        jnp.einsum("rqhd,rkhd->rhqk", tree_queries, tree_keys, preferred_element_type=jnp.float32)
        * scale
    )
    tree_scores = jnp.where(lineage[:, None], tree_scores, -jnp.inf)
    tree_top = jnp.max(tree_scores, axis=3, keepdims=True)
    tree_exp = jnp.exp(tree_scores - tree_top)
    tree_total = jnp.sum(tree_exp, axis=3, keepdims=True)
    tree_probs = tree_exp.astype(jnp.bfloat16)
    tree_part = jnp.einsum(
        "rhqk,rkhd->rqhd", tree_probs, tree_values, preferred_element_type=jnp.float32
    ) / jnp.transpose(tree_total, (0, 2, 1, 3))
    tree_lse = jnp.transpose((tree_top + jnp.log(tree_total))[..., 0], (0, 2, 1))[..., None]
    slot_ids = jnp.arange(slots_total, dtype=jnp.int32)

    def spread(values, index):
        placing = (index[None, :] == slot_ids[:, None]).astype(values.dtype)
        flat = values.reshape(values.shape[0], -1)
        placed = jnp.dot(placing, flat, preferred_element_type=jnp.float32).astype(values.dtype)
        return placed.reshape((slots_total,) + values.shape[1:])

    arrived = lax.all_to_all(placed_queries, "dp", split_axis=0, concat_axis=0, tiled=True)
    kept = lax.all_to_all(
        spread(jnp.concatenate([kept_keys, kept_values], axis=1), send_index),
        "dp",
        split_axis=0,
        concat_axis=0,
        tiled=True,
    )[receive_index]
    new_keys = kept[:, : kept_keys.shape[1]]
    new_values = kept[:, kept_keys.shape[1] :]
    back = attend(arrived, receive_index, slot_lengths, cache_keys, cache_values)
    returned = lax.all_to_all(back, "dp", split_axis=0, concat_axis=0, tiled=True)[send_index]
    cache_part = returned[:, :draft]
    lse_rows = returned[:, draft : draft + local_heads].astype(jnp.float32)
    cache_lse = lse_rows[..., :draft] + (
        lse_rows[..., draft : 2 * draft] + lse_rows[..., 2 * draft : 3 * draft]
    )
    cache_weight = jnp.transpose(cache_lse, (0, 2, 1))[..., None]
    larger = jnp.maximum(cache_weight, tree_lse)
    cache_share = jnp.exp(cache_weight - larger)
    tree_share = jnp.exp(tree_lse - larger)
    blended = (
        cache_share * cache_part.astype(jnp.float32).reshape(requests, draft, local_heads, HD)
        + tree_share * tree_part
    ) / (cache_share + tree_share)
    attended = blended.astype(jnp.bfloat16).reshape(tokens, width)
    attention_term = jnp.dot(attended, w_out, preferred_element_type=jnp.float32)
    feature = model_width // lax.axis_size("head")
    offset = lax.axis_index("head") * feature

    def columns(values):
        return lax.dynamic_slice_in_dim(values, offset, feature, values.ndim - 1)

    attention_sum = lax.psum(attention_term.astype(jnp.bfloat16), "head")
    first_normed, down_part = feed_forward(
        attention_sum, hidden, b_out, first_gain, first_shift, w_up, b_up, w_down
    )
    down_share = lax.psum_scatter(
        down_part, "head", scatter_dimension=1, tiled=True
    ).astype(jnp.float32)
    second_mixed = down_share + columns(b_down) + columns(first_normed).astype(jnp.float32)
    heads_along = lax.axis_size("head")
    own_sums = jnp.stack(
        [jnp.sum(second_mixed, axis=1), jnp.sum(second_mixed * second_mixed, axis=1)]
    )
    second_sums = jnp.sum(
        lax.all_to_all(
            jnp.broadcast_to(own_sums[None], (heads_along,) + own_sums.shape),
            "head",
            0,
            0,
            tiled=False,
        ),
        axis=0,
    )
    layer_out = normalize_shared(
        second_mixed, second_sums, columns(second_gain), columns(second_shift), model_width
    ).astype(jnp.bfloat16)
    return (layer_out, new_keys, new_values)


def solution(mesh):
    placed = (
        P("dp", None),
        P("dp", None),
        P(),
        P("dp"),
        P("dp", None),
        P("dp"),
        P("dp", None, "head"),
        P("dp", None, "head"),
        P(None, "head"),
        P("head"),
        P(None, "head"),
        P(None, "head"),
        P("head"),
        P("head", None),
        P(),
        P(),
        P(),
        P(None, "head"),
        P("head"),
        P("head", None),
        P(),
        P(),
        P(),
    )
    return jax.shard_map(
        local,
        mesh=mesh,
        in_specs=placed,
        out_specs=(P("dp", "head"), P("dp", None, "head"), P("dp", None, "head")),
        check_vma=False,
    )
```

```python
import math

import jax
import jax.numpy as jnp
from jax import lax
from jax.experimental import pallas as pl
from jax.experimental.pallas import tpu as pltpu
from jax.sharding import PartitionSpec as P

HD = 128
PEER_MOST = 2


EPSILON = 1e-05


def ancestry(parent_row, draft):
    nodes = jnp.arange(draft, dtype=jnp.int32)
    reach = (parent_row[:, None] == nodes[None, :]).astype(jnp.float32) + jnp.eye(
        draft, dtype=jnp.float32
    )
    for turn in range(max(1, draft.bit_length())):
        reach = jnp.minimum(jnp.dot(reach, reach, precision=lax.Precision.HIGHEST), 1.0)
    return reach > 0.5


def normalize(mixed, gain, shift):
    center = jnp.mean(mixed, axis=-1, keepdims=True)
    square = jnp.mean(mixed * mixed, axis=-1, keepdims=True)
    return (mixed - center) * lax.rsqrt(square - center * center + EPSILON) * gain + shift


def normalize_shared(mixed, sums, gain, shift, model_width):
    center = (sums[0] / model_width)[:, None]
    square = (sums[1] / model_width)[:, None]
    return (mixed - center) * lax.rsqrt(square - center * center + EPSILON) * gain + shift


def ffn_block(attn_ref, hid_ref, bout_ref, gain_ref, shift_ref, wup_ref, bup_ref, wdown_ref, normed_ref, down_ref):
    mixed = attn_ref[...].astype(jnp.float32) + bout_ref[...] + hid_ref[...].astype(jnp.float32)
    center = jnp.mean(mixed, axis=-1, keepdims=True)
    square = jnp.mean(mixed * mixed, axis=-1, keepdims=True)
    normed = ((mixed - center) * lax.rsqrt(square - center * center + EPSILON) * gain_ref[...] + shift_ref[...]).astype(jnp.bfloat16)
    normed_ref[...] = normed
    raised = jnp.dot(normed, wup_ref[...], preferred_element_type=jnp.float32) + bup_ref[...]
    inner = jax.nn.gelu(raised, approximate=True).astype(jnp.bfloat16)
    down_ref[...] = jnp.dot(inner, wdown_ref[...], preferred_element_type=jnp.float32).astype(jnp.bfloat16)

def feed_forward(attn, hidden, b_out, gain, shift, w_up, b_up, w_down, block=256):
    tokens, model = hidden.shape
    units = w_up.shape[1]
    row = lambda i: (i, 0)
    fixed = lambda i: (0, 0)
    return pl.pallas_call(
        ffn_block,
        grid=(tokens // block,),
        in_specs=[
            pl.BlockSpec((block, model), row),
            pl.BlockSpec((block, model), row),
            pl.BlockSpec((1, model), fixed),
            pl.BlockSpec((1, model), fixed),
            pl.BlockSpec((1, model), fixed),
            pl.BlockSpec((model, units), fixed),
            pl.BlockSpec((1, units), fixed),
            pl.BlockSpec((units, model), fixed),
        ],
        out_specs=[pl.BlockSpec((block, model), row), pl.BlockSpec((block, model), row)],
        out_shape=[jax.ShapeDtypeStruct((tokens, model), jnp.bfloat16)] * 2,
        cost_estimate=pl.CostEstimate(flops=4 * tokens * model * units, transcendentals=tokens * units, bytes_accessed=2 * (4 * tokens * model + 2 * model * units)),
    )(attn, hidden, b_out.reshape(1, -1), gain.reshape(1, -1), shift.reshape(1, -1), w_up, b_up.reshape(1, -1), w_down)


def attend_block(where_ref, length_ref, query_ref, key_ref, value_ref, back_ref):
    slot = pl.program_id(0)
    length = length_ref[slot]
    draft = query_ref.shape[1]
    heads = query_ref.shape[2] // HD
    width = query_ref.shape[2]
    capacity = key_ref.shape[1]
    living = lax.broadcasted_iota(jnp.int32, (draft, capacity), 1) < length
    back_ref[0, draft:, :] = jnp.zeros((back_ref.shape[1] - draft, width), back_ref.dtype)
    for head in range(heads):
        cols = slice(head * HD, (head + 1) * HD)
        query = query_ref[0, :, cols]
        scores = lax.dot_general(
            query, key_ref[0, :, cols], (((1,), (1,)), ((), ())), preferred_element_type=jnp.float32
        ) * (1.0 / math.sqrt(HD))
        scores = jnp.where(living, scores, -jnp.inf)
        top = jnp.max(scores, axis=1, keepdims=True)
        weights = jnp.exp(scores - top)
        total = jnp.sum(weights, axis=1, keepdims=True)
        mixed = jnp.dot(weights.astype(jnp.bfloat16), value_ref[0, :, cols], preferred_element_type=jnp.float32)
        back_ref[0, :draft, cols] = (mixed / total).astype(back_ref.dtype)
        lse = jnp.broadcast_to(top + jnp.log(total), (draft, 128)).T[0:1, :draft]
        high = lse.astype(jnp.bfloat16)
        rest = lse - high.astype(jnp.float32)
        middle = rest.astype(jnp.bfloat16)
        low = (rest - middle.astype(jnp.float32)).astype(jnp.bfloat16)
        back_ref[0, draft + head : draft + head + 1, 0:draft] = high
        back_ref[0, draft + head : draft + head + 1, draft : 2 * draft] = middle
        back_ref[0, draft + head : draft + head + 1, 2 * draft : 3 * draft] = low

def attend(arrived, where, lengths, keys, values):
    positions, draft, width = arrived.shape
    slots, capacity, _ = keys.shape
    heads = width // HD
    rows = draft + heads
    grid_spec = pltpu.PrefetchScalarGridSpec(
        num_scalar_prefetch=2,
        grid=(slots,),
        in_specs=[
            pl.BlockSpec((1, draft, width), lambda s, w, n: (w[s], 0, 0)),
            pl.BlockSpec((1, capacity, width), lambda s, w, n: (s, 0, 0)),
            pl.BlockSpec((1, capacity, width), lambda s, w, n: (s, 0, 0)),
        ],
        out_specs=pl.BlockSpec((1, rows, width), lambda s, w, n: (w[s], 0, 0)),
    )
    return pl.pallas_call(
        attend_block,
        grid_spec=grid_spec,
        out_shape=jax.ShapeDtypeStruct((positions, rows, width), arrived.dtype),
    )(where, lengths, arrived, keys, values)


def project_block(where_ref, hidden_ref, weight_ref, bias_ref, query_ref, placed_ref):
    draft = placed_ref.shape[1]
    rows = (
        jnp.dot(hidden_ref[...], weight_ref[...], preferred_element_type=jnp.float32)
        + bias_ref[...]
    ).astype(query_ref.dtype)
    query_ref[...] = rows
    for request in range(query_ref.shape[0] // draft):
        placed_ref[where_ref[request]] = rows[request * draft : (request + 1) * draft]


def project(hidden, weight, bias, where, positions, draft):
    tokens, model = hidden.shape
    width = weight.shape[1]
    grid_spec = pltpu.PrefetchScalarGridSpec(
        num_scalar_prefetch=1,
        grid=(1,),
        in_specs=[
            pl.BlockSpec((tokens, model), lambda r, w: (0, 0)),
            pl.BlockSpec((model, width), lambda r, w: (0, 0)),
            pl.BlockSpec((1, width), lambda r, w: (0, 0)),
        ],
        out_specs=[
            pl.BlockSpec((tokens, width), lambda r, w: (0, 0)),
            pl.BlockSpec((positions, draft, width), lambda r, w: (0, 0, 0)),
        ],
    )
    return pl.pallas_call(
        project_block,
        grid_spec=grid_spec,
        out_shape=[
            jax.ShapeDtypeStruct((tokens, width), jnp.bfloat16),
            jax.ShapeDtypeStruct((positions, draft, width), jnp.bfloat16),
        ],
    )(where, hidden, weight, bias.reshape(1, -1))


def local(
    hidden,
    parents,
    owner_slot,
    slot_lengths,
    accepted_path,
    accepted_count,
    cache_keys,
    cache_values,
    w_query,
    b_query,
    w_key,
    w_value,
    b_value,
    w_out,
    b_out,
    first_gain,
    first_shift,
    w_up,
    b_up,
    w_down,
    b_down,
    second_gain,
    second_shift,
):
    requests = parents.shape[0]
    draft = parents.shape[1]
    tokens = hidden.shape[0]
    model_width = hidden.shape[1]
    width = w_query.shape[1]
    local_heads = width // HD
    capacity = cache_keys.shape[1]
    block = min(capacity, 256)
    shards = lax.axis_size("dp")
    myself = lax.axis_index("dp")
    scale = 1.0 / math.sqrt(HD)
    local_ids = jnp.arange(requests, dtype=jnp.int32)
    my_owner = lax.dynamic_slice_in_dim(owner_slot, myself * requests, requests)
    target = my_owner // requests
    earlier = local_ids[None, :] < local_ids[:, None]
    same_target = target[None, :] == target[:, None]
    rank = jnp.sum((earlier & same_target).astype(jnp.int32), axis=1)
    my_slots = myself * requests + local_ids
    every_id = jnp.arange(owner_slot.shape[0], dtype=jnp.int32)
    source_request = jnp.sum(
        jnp.where(owner_slot[None, :] == my_slots[:, None], every_id[None, :], 0), axis=1
    )
    source = source_request // requests
    source_local = source_request % requests
    source_targets = owner_slot.reshape(shards, requests)[source] // requests
    source_rank = jnp.sum(
        ((local_ids[None, :] < source_local[:, None]) & (source_targets == myself)).astype(
            jnp.int32
        ),
        axis=1,
    )
    slots_total = shards * PEER_MOST
    send_index = target * PEER_MOST + rank
    receive_index = source * PEER_MOST + source_rank
    queries, placed_queries = project(hidden, w_query, b_query, send_index, slots_total, draft)
    key_rows = jnp.dot(hidden, w_key, preferred_element_type=jnp.float32).astype(jnp.bfloat16)
    value_rows = (jnp.dot(hidden, w_value, preferred_element_type=jnp.float32) + b_value).astype(
        jnp.bfloat16
    )
    levels = jnp.arange(accepted_path.shape[1], dtype=jnp.int32)
    chosen = local_ids[:, None] * draft + accepted_path
    usable = (levels[None, :] < accepted_count[:, None])[..., None]
    kept_keys = jnp.where(usable, key_rows[chosen], jnp.zeros((), jnp.bfloat16))
    kept_values = jnp.where(usable, value_rows[chosen], jnp.zeros((), jnp.bfloat16))
    tree_queries = queries.reshape(requests, draft, local_heads, HD)
    tree_keys = key_rows.reshape(requests, draft, local_heads, HD)
    tree_values = value_rows.reshape(requests, draft, local_heads, HD)
    lineage = jax.vmap(lambda parent_row: ancestry(parent_row, draft))(parents)
    tree_scores = (
        jnp.einsum("rqhd,rkhd->rhqk", tree_queries, tree_keys, preferred_element_type=jnp.float32)
        * scale
    )
    tree_scores = jnp.where(lineage[:, None], tree_scores, -jnp.inf)
    tree_top = jnp.max(tree_scores, axis=3, keepdims=True)
    tree_exp = jnp.exp(tree_scores - tree_top)
    tree_total = jnp.sum(tree_exp, axis=3, keepdims=True)
    tree_probs = tree_exp.astype(jnp.bfloat16)
    tree_part = jnp.einsum(
        "rhqk,rkhd->rqhd", tree_probs, tree_values, preferred_element_type=jnp.float32
    ) / jnp.transpose(tree_total, (0, 2, 1, 3))
    tree_lse = jnp.transpose((tree_top + jnp.log(tree_total))[..., 0], (0, 2, 1))[..., None]
    slot_ids = jnp.arange(slots_total, dtype=jnp.int32)

    def spread(values, index):
        placing = (index[None, :] == slot_ids[:, None]).astype(values.dtype)
        flat = values.reshape(values.shape[0], -1)
        placed = jnp.dot(placing, flat, preferred_element_type=jnp.float32).astype(values.dtype)
        return placed.reshape((slots_total,) + values.shape[1:])

    arrived = lax.all_to_all(placed_queries, "dp", split_axis=0, concat_axis=0, tiled=True)
    kept = lax.all_to_all(
        spread(jnp.concatenate([kept_keys, kept_values], axis=1), send_index),
        "dp",
        split_axis=0,
        concat_axis=0,
        tiled=True,
    )[receive_index]
    new_keys = kept[:, : kept_keys.shape[1]]
    new_values = kept[:, kept_keys.shape[1] :]
    back = attend(arrived, receive_index, slot_lengths, cache_keys, cache_values)
    returned = lax.all_to_all(back, "dp", split_axis=0, concat_axis=0, tiled=True)[send_index]
    cache_part = returned[:, :draft]
    lse_rows = returned[:, draft : draft + local_heads].astype(jnp.float32)
    cache_lse = lse_rows[..., :draft] + (
        lse_rows[..., draft : 2 * draft] + lse_rows[..., 2 * draft : 3 * draft]
    )
    cache_weight = jnp.transpose(cache_lse, (0, 2, 1))[..., None]
    larger = jnp.maximum(cache_weight, tree_lse)
    cache_share = jnp.exp(cache_weight - larger)
    tree_share = jnp.exp(tree_lse - larger)
    blended = (
        cache_share * cache_part.astype(jnp.float32).reshape(requests, draft, local_heads, HD)
        + tree_share * tree_part
    ) / (cache_share + tree_share)
    attended = blended.astype(jnp.bfloat16).reshape(tokens, width)
    attention_term = jnp.dot(attended, w_out, preferred_element_type=jnp.float32)
    feature = model_width // lax.axis_size("head")
    offset = lax.axis_index("head") * feature

    def columns(values):
        return lax.dynamic_slice_in_dim(values, offset, feature, values.ndim - 1)

    attention_sum = lax.psum(attention_term.astype(jnp.bfloat16), "head")
    first_normed, down_part = feed_forward(
        attention_sum, hidden, b_out, first_gain, first_shift, w_up, b_up, w_down
    )
    down_share = lax.psum_scatter(
        down_part, "head", scatter_dimension=1, tiled=True
    ).astype(jnp.float32)
    second_mixed = down_share + columns(b_down) + columns(first_normed).astype(jnp.float32)
    heads_along = lax.axis_size("head")
    own_sums = jnp.stack(
        [jnp.sum(second_mixed, axis=1), jnp.sum(second_mixed * second_mixed, axis=1)]
    )
    second_sums = jnp.sum(
        lax.all_to_all(
            jnp.broadcast_to(own_sums[None], (heads_along,) + own_sums.shape),
            "head",
            0,
            0,
            tiled=False,
        ),
        axis=0,
    )
    layer_out = normalize_shared(
        second_mixed, second_sums, columns(second_gain), columns(second_shift), model_width
    ).astype(jnp.bfloat16)
    return (layer_out, new_keys, new_values)


def solution(mesh):
    placed = (
        P("dp", None),
        P("dp", None),
        P(),
        P("dp"),
        P("dp", None),
        P("dp"),
        P("dp", None, "head"),
        P("dp", None, "head"),
        P(None, "head"),
        P("head"),
        P(None, "head"),
        P(None, "head"),
        P("head"),
        P("head", None),
        P(),
        P(),
        P(),
        P(None, "head"),
        P("head"),
        P("head", None),
        P(),
        P(),
        P(),
    )
    return jax.shard_map(
        local,
        mesh=mesh,
        in_specs=placed,
        out_specs=(P("dp", "head"), P("dp", None, "head"), P("dp", None, "head")),
        check_vma=False,
    )
```

```python
import math

import jax
import jax.numpy as jnp
from jax import lax
from jax.experimental import pallas as pl
from jax.experimental.pallas import tpu as pltpu
from jax.sharding import PartitionSpec as P

HD = 128
PEER_MOST = 2


EPSILON = 1e-05


def ancestry(parent_row, draft):
    nodes = jnp.arange(draft, dtype=jnp.int32)
    reach = (parent_row[:, None] == nodes[None, :]).astype(jnp.float32) + jnp.eye(
        draft, dtype=jnp.float32
    )
    for turn in range(max(1, draft.bit_length())):
        reach = jnp.minimum(jnp.dot(reach, reach, precision=lax.Precision.HIGHEST), 1.0)
    return reach > 0.5


def normalize(mixed, gain, shift):
    center = jnp.mean(mixed, axis=-1, keepdims=True)
    square = jnp.mean(mixed * mixed, axis=-1, keepdims=True)
    return (mixed - center) * lax.rsqrt(square - center * center + EPSILON) * gain + shift


def normalize_shared(mixed, sums, gain, shift, model_width):
    center = (sums[0] / model_width)[:, None]
    square = (sums[1] / model_width)[:, None]
    return (mixed - center) * lax.rsqrt(square - center * center + EPSILON) * gain + shift


def ffn_block(attn_ref, hid_ref, bout_ref, gain_ref, shift_ref, wup_ref, bup_ref, wdown_ref, normed_ref, down_ref):
    mixed = attn_ref[...].astype(jnp.float32) + bout_ref[...] + hid_ref[...].astype(jnp.float32)
    center = jnp.mean(mixed, axis=-1, keepdims=True)
    square = jnp.mean(mixed * mixed, axis=-1, keepdims=True)
    normed = ((mixed - center) * lax.rsqrt(square - center * center + EPSILON) * gain_ref[...] + shift_ref[...]).astype(jnp.bfloat16)
    normed_ref[...] = normed
    raised = jnp.dot(normed, wup_ref[...], preferred_element_type=jnp.float32) + bup_ref[...]
    inner = jax.nn.gelu(raised, approximate=True).astype(jnp.bfloat16)
    down_ref[...] = jnp.dot(inner, wdown_ref[...], preferred_element_type=jnp.float32).astype(jnp.bfloat16)

def feed_forward(attn, hidden, b_out, gain, shift, w_up, b_up, w_down, block=256):
    tokens, model = hidden.shape
    units = w_up.shape[1]
    row = lambda i: (i, 0)
    fixed = lambda i: (0, 0)
    return pl.pallas_call(
        ffn_block,
        grid=(tokens // block,),
        in_specs=[
            pl.BlockSpec((block, model), row),
            pl.BlockSpec((block, model), row),
            pl.BlockSpec((1, model), fixed),
            pl.BlockSpec((1, model), fixed),
            pl.BlockSpec((1, model), fixed),
            pl.BlockSpec((model, units), fixed),
            pl.BlockSpec((1, units), fixed),
            pl.BlockSpec((units, model), fixed),
        ],
        out_specs=[pl.BlockSpec((block, model), row), pl.BlockSpec((block, model), row)],
        out_shape=[jax.ShapeDtypeStruct((tokens, model), jnp.bfloat16)] * 2,
        cost_estimate=pl.CostEstimate(flops=4 * tokens * model * units, transcendentals=tokens * units, bytes_accessed=2 * (4 * tokens * model + 2 * model * units)),
    )(attn, hidden, b_out.reshape(1, -1), gain.reshape(1, -1), shift.reshape(1, -1), w_up, b_up.reshape(1, -1), w_down)


def attend_block(where_ref, length_ref, query_ref, key_ref, value_ref, back_ref):
    slot = pl.program_id(0)
    length = length_ref[slot]
    draft = query_ref.shape[1]
    heads = query_ref.shape[2] // HD
    width = query_ref.shape[2]
    capacity = key_ref.shape[1]
    living = lax.broadcasted_iota(jnp.int32, (draft, capacity), 1) < length
    back_ref[0, draft:, :] = jnp.zeros((back_ref.shape[1] - draft, width), back_ref.dtype)
    for head in range(heads):
        cols = slice(head * HD, (head + 1) * HD)
        query = query_ref[0, :, cols]
        scores = lax.dot_general(
            query, key_ref[0, :, cols], (((1,), (1,)), ((), ())), preferred_element_type=jnp.float32
        ) * (1.0 / math.sqrt(HD))
        scores = jnp.where(living, scores, -jnp.inf)
        top = jnp.max(scores, axis=1, keepdims=True)
        weights = jnp.exp(scores - top)
        total = jnp.sum(weights, axis=1, keepdims=True)
        mixed = jnp.dot(weights.astype(jnp.bfloat16), value_ref[0, :, cols], preferred_element_type=jnp.float32)
        back_ref[0, :draft, cols] = (mixed / total).astype(back_ref.dtype)
        lse = jnp.broadcast_to(top + jnp.log(total), (draft, 128)).T[0:1, :draft]
        high = lse.astype(jnp.bfloat16)
        rest = lse - high.astype(jnp.float32)
        middle = rest.astype(jnp.bfloat16)
        low = (rest - middle.astype(jnp.float32)).astype(jnp.bfloat16)
        back_ref[0, draft + head : draft + head + 1, 0:draft] = high
        back_ref[0, draft + head : draft + head + 1, draft : 2 * draft] = middle
        back_ref[0, draft + head : draft + head + 1, 2 * draft : 3 * draft] = low

def attend(arrived, where, lengths, keys, values):
    positions, draft, width = arrived.shape
    slots, capacity, _ = keys.shape
    heads = width // HD
    rows = draft + heads
    grid_spec = pltpu.PrefetchScalarGridSpec(
        num_scalar_prefetch=2,
        grid=(slots,),
        in_specs=[
            pl.BlockSpec((1, draft, width), lambda s, w, n: (w[s], 0, 0)),
            pl.BlockSpec((1, capacity, width), lambda s, w, n: (s, 0, 0)),
            pl.BlockSpec((1, capacity, width), lambda s, w, n: (s, 0, 0)),
        ],
        out_specs=pl.BlockSpec((1, rows, width), lambda s, w, n: (w[s], 0, 0)),
    )
    return pl.pallas_call(
        attend_block,
        grid_spec=grid_spec,
        out_shape=jax.ShapeDtypeStruct((positions, rows, width), arrived.dtype),
    )(where, lengths, arrived, keys, values)


def project_block(where_ref, hidden_ref, weight_ref, bias_ref, query_ref, placed_ref):
    draft = placed_ref.shape[1]
    rows = (
        jnp.dot(hidden_ref[...], weight_ref[...], preferred_element_type=jnp.float32)
        + bias_ref[...]
    ).astype(query_ref.dtype)
    query_ref[...] = rows
    for request in range(query_ref.shape[0] // draft):
        placed_ref[where_ref[request]] = rows[request * draft : (request + 1) * draft]


def project(hidden, weight, bias, where, positions, draft):
    tokens, model = hidden.shape
    width = weight.shape[1]
    grid_spec = pltpu.PrefetchScalarGridSpec(
        num_scalar_prefetch=1,
        grid=(1,),
        in_specs=[
            pl.BlockSpec((tokens, model), lambda r, w: (0, 0)),
            pl.BlockSpec((model, width), lambda r, w: (0, 0)),
            pl.BlockSpec((1, width), lambda r, w: (0, 0)),
        ],
        out_specs=[
            pl.BlockSpec((tokens, width), lambda r, w: (0, 0)),
            pl.BlockSpec((positions, draft, width), lambda r, w: (0, 0, 0)),
        ],
    )
    return pl.pallas_call(
        project_block,
        grid_spec=grid_spec,
        out_shape=[
            jax.ShapeDtypeStruct((tokens, width), jnp.bfloat16),
            jax.ShapeDtypeStruct((positions, draft, width), jnp.bfloat16),
        ],
    )(where, hidden, weight, bias.reshape(1, -1))


def blend_block(
    where_ref, received_ref, tree_ref, cache_share_ref, tree_share_ref, weight_ref, out_ref, mixed_ref
):
    draft = tree_ref.shape[0] // where_ref.shape[0]
    heads = cache_share_ref.shape[1]
    for request in range(where_ref.shape[0]):
        rows = slice(request * draft, (request + 1) * draft)
        part = received_ref[where_ref[request], :draft, :].astype(jnp.float32)
        tree = tree_ref[rows, :]
        cache_share = cache_share_ref[rows, :]
        tree_share = tree_share_ref[rows, :]
        for head in range(heads):
            cols = slice(head * HD, (head + 1) * HD)
            ours = cache_share[:, head : head + 1]
            theirs = tree_share[:, head : head + 1]
            mixed_ref[rows, cols] = (
                (ours * part[:, cols] + theirs * tree[:, cols]) / (ours + theirs)
            ).astype(mixed_ref.dtype)
    out_ref[...] = jnp.dot(
        mixed_ref[...], weight_ref[...], preferred_element_type=jnp.float32
    ).astype(out_ref.dtype)


def blend_out(received, where, tree_part, cache_share, tree_share, weight):
    tokens, width = tree_part.shape
    model = weight.shape[1]
    whole = lambda r, w: (0, 0)
    grid_spec = pltpu.PrefetchScalarGridSpec(
        num_scalar_prefetch=1,
        grid=(1,),
        in_specs=[
            pl.BlockSpec(received.shape, lambda r, w: (0, 0, 0)),
            pl.BlockSpec(tree_part.shape, whole),
            pl.BlockSpec(cache_share.shape, whole),
            pl.BlockSpec(tree_share.shape, whole),
            pl.BlockSpec(weight.shape, whole),
        ],
        out_specs=pl.BlockSpec((tokens, model), whole),
        scratch_shapes=[pltpu.VMEM((tokens, width), jnp.bfloat16)],
    )
    return pl.pallas_call(
        blend_block,
        grid_spec=grid_spec,
        out_shape=jax.ShapeDtypeStruct((tokens, model), jnp.bfloat16),
    )(where, received, tree_part, cache_share, tree_share, weight)


def local(
    hidden,
    parents,
    owner_slot,
    slot_lengths,
    accepted_path,
    accepted_count,
    cache_keys,
    cache_values,
    w_query,
    b_query,
    w_key,
    w_value,
    b_value,
    w_out,
    b_out,
    first_gain,
    first_shift,
    w_up,
    b_up,
    w_down,
    b_down,
    second_gain,
    second_shift,
):
    requests = parents.shape[0]
    draft = parents.shape[1]
    tokens = hidden.shape[0]
    model_width = hidden.shape[1]
    width = w_query.shape[1]
    local_heads = width // HD
    capacity = cache_keys.shape[1]
    block = min(capacity, 256)
    shards = lax.axis_size("dp")
    myself = lax.axis_index("dp")
    scale = 1.0 / math.sqrt(HD)
    local_ids = jnp.arange(requests, dtype=jnp.int32)
    my_owner = lax.dynamic_slice_in_dim(owner_slot, myself * requests, requests)
    target = my_owner // requests
    earlier = local_ids[None, :] < local_ids[:, None]
    same_target = target[None, :] == target[:, None]
    rank = jnp.sum((earlier & same_target).astype(jnp.int32), axis=1)
    my_slots = myself * requests + local_ids
    every_id = jnp.arange(owner_slot.shape[0], dtype=jnp.int32)
    source_request = jnp.sum(
        jnp.where(owner_slot[None, :] == my_slots[:, None], every_id[None, :], 0), axis=1
    )
    source = source_request // requests
    source_local = source_request % requests
    source_targets = owner_slot.reshape(shards, requests)[source] // requests
    source_rank = jnp.sum(
        ((local_ids[None, :] < source_local[:, None]) & (source_targets == myself)).astype(
            jnp.int32
        ),
        axis=1,
    )
    slots_total = shards * PEER_MOST
    send_index = target * PEER_MOST + rank
    receive_index = source * PEER_MOST + source_rank
    queries, placed_queries = project(hidden, w_query, b_query, send_index, slots_total, draft)
    key_rows = jnp.dot(hidden, w_key, preferred_element_type=jnp.float32).astype(jnp.bfloat16)
    value_rows = (jnp.dot(hidden, w_value, preferred_element_type=jnp.float32) + b_value).astype(
        jnp.bfloat16
    )
    levels = jnp.arange(accepted_path.shape[1], dtype=jnp.int32)
    chosen = local_ids[:, None] * draft + accepted_path
    usable = (levels[None, :] < accepted_count[:, None])[..., None]
    kept_keys = jnp.where(usable, key_rows[chosen], jnp.zeros((), jnp.bfloat16))
    kept_values = jnp.where(usable, value_rows[chosen], jnp.zeros((), jnp.bfloat16))
    tree_queries = queries.reshape(requests, draft, local_heads, HD)
    tree_keys = key_rows.reshape(requests, draft, local_heads, HD)
    tree_values = value_rows.reshape(requests, draft, local_heads, HD)
    lineage = jax.vmap(lambda parent_row: ancestry(parent_row, draft))(parents)
    tree_scores = (
        jnp.einsum("rqhd,rkhd->rhqk", tree_queries, tree_keys, preferred_element_type=jnp.float32)
        * scale
    )
    tree_scores = jnp.where(lineage[:, None], tree_scores, -jnp.inf)
    tree_top = jnp.max(tree_scores, axis=3, keepdims=True)
    tree_exp = jnp.exp(tree_scores - tree_top)
    tree_total = jnp.sum(tree_exp, axis=3, keepdims=True)
    tree_probs = tree_exp.astype(jnp.bfloat16)
    tree_part = jnp.einsum(
        "rhqk,rkhd->rqhd", tree_probs, tree_values, preferred_element_type=jnp.float32
    ) / jnp.transpose(tree_total, (0, 2, 1, 3))
    tree_lse = jnp.transpose((tree_top + jnp.log(tree_total))[..., 0], (0, 2, 1))[..., None]
    slot_ids = jnp.arange(slots_total, dtype=jnp.int32)

    def spread(values, index):
        placing = (index[None, :] == slot_ids[:, None]).astype(values.dtype)
        flat = values.reshape(values.shape[0], -1)
        placed = jnp.dot(placing, flat, preferred_element_type=jnp.float32).astype(values.dtype)
        return placed.reshape((slots_total,) + values.shape[1:])

    arrived = lax.all_to_all(placed_queries, "dp", split_axis=0, concat_axis=0, tiled=True)
    kept = lax.all_to_all(
        spread(jnp.concatenate([kept_keys, kept_values], axis=1), send_index),
        "dp",
        split_axis=0,
        concat_axis=0,
        tiled=True,
    )[receive_index]
    new_keys = kept[:, : kept_keys.shape[1]]
    new_values = kept[:, kept_keys.shape[1] :]
    back = attend(arrived, receive_index, slot_lengths, cache_keys, cache_values)
    received = lax.all_to_all(back, "dp", split_axis=0, concat_axis=0, tiled=True)
    lse_rows = received[send_index, draft : draft + local_heads].astype(jnp.float32)
    cache_lse = lse_rows[..., :draft] + (
        lse_rows[..., draft : 2 * draft] + lse_rows[..., 2 * draft : 3 * draft]
    )
    cache_weight = jnp.transpose(cache_lse, (0, 2, 1))[..., None]
    larger = jnp.maximum(cache_weight, tree_lse)
    cache_share = jnp.exp(cache_weight - larger)
    tree_share = jnp.exp(tree_lse - larger)
    attention_term = blend_out(
        received,
        send_index,
        tree_part.reshape(tokens, width),
        cache_share.reshape(tokens, local_heads),
        tree_share.reshape(tokens, local_heads),
        w_out,
    )
    feature = model_width // lax.axis_size("head")
    offset = lax.axis_index("head") * feature

    def columns(values):
        return lax.dynamic_slice_in_dim(values, offset, feature, values.ndim - 1)

    attention_sum = lax.psum(attention_term, "head")
    first_normed, down_part = feed_forward(
        attention_sum, hidden, b_out, first_gain, first_shift, w_up, b_up, w_down
    )
    down_share = lax.psum_scatter(
        down_part, "head", scatter_dimension=1, tiled=True
    ).astype(jnp.float32)
    second_mixed = down_share + columns(b_down) + columns(first_normed).astype(jnp.float32)
    heads_along = lax.axis_size("head")
    own_sums = jnp.stack(
        [jnp.sum(second_mixed, axis=1), jnp.sum(second_mixed * second_mixed, axis=1)]
    )
    second_sums = jnp.sum(
        lax.all_to_all(
            jnp.broadcast_to(own_sums[None], (heads_along,) + own_sums.shape),
            "head",
            0,
            0,
            tiled=False,
        ),
        axis=0,
    )
    layer_out = normalize_shared(
        second_mixed, second_sums, columns(second_gain), columns(second_shift), model_width
    ).astype(jnp.bfloat16)
    return (layer_out, new_keys, new_values)


def solution(mesh):
    placed = (
        P("dp", None),
        P("dp", None),
        P(),
        P("dp"),
        P("dp", None),
        P("dp"),
        P("dp", None, "head"),
        P("dp", None, "head"),
        P(None, "head"),
        P("head"),
        P(None, "head"),
        P(None, "head"),
        P("head"),
        P("head", None),
        P(),
        P(),
        P(),
        P(None, "head"),
        P("head"),
        P("head", None),
        P(),
        P(),
        P(),
    )
    return jax.shard_map(
        local,
        mesh=mesh,
        in_specs=placed,
        out_specs=(P("dp", "head"), P("dp", None, "head"), P("dp", None, "head")),
        check_vma=False,
    )
```

```python
import math

import jax
import jax.numpy as jnp
from jax import lax
from jax.experimental import pallas as pl
from jax.experimental.pallas import tpu as pltpu
from jax.sharding import PartitionSpec as P

HD = 128
PEER_MOST = 2


EPSILON = 1e-05


def ancestry(parent_row, draft):
    nodes = jnp.arange(draft, dtype=jnp.int32)
    reach = (parent_row[:, None] == nodes[None, :]).astype(jnp.float32) + jnp.eye(
        draft, dtype=jnp.float32
    )
    for turn in range(max(1, draft.bit_length())):
        reach = jnp.minimum(jnp.dot(reach, reach, precision=lax.Precision.HIGHEST), 1.0)
    return reach > 0.5


def normalize(mixed, gain, shift):
    center = jnp.mean(mixed, axis=-1, keepdims=True)
    square = jnp.mean(mixed * mixed, axis=-1, keepdims=True)
    return (mixed - center) * lax.rsqrt(square - center * center + EPSILON) * gain + shift


def normalize_shared(mixed, sums, gain, shift, model_width):
    center = (sums[0] / model_width)[:, None]
    square = (sums[1] / model_width)[:, None]
    return (mixed - center) * lax.rsqrt(square - center * center + EPSILON) * gain + shift


def ffn_block(
    column_ref, attn_ref, hid_ref, bout_ref, gain_ref, shift_ref, wup_ref, bup_ref, wdown_ref,
    normed_ref, down_ref,
):
    mixed = attn_ref[...].astype(jnp.float32) + bout_ref[...] + hid_ref[...].astype(jnp.float32)
    center = jnp.mean(mixed, axis=-1, keepdims=True)
    square = jnp.mean(mixed * mixed, axis=-1, keepdims=True)
    scale = lax.rsqrt(square - center * center + EPSILON)
    normed = ((mixed - center) * scale * gain_ref[...] + shift_ref[...]).astype(jnp.bfloat16)
    feature = normed_ref.shape[1]
    start = pl.multiple_of(column_ref[0] * feature, feature)
    cols = pl.ds(start, feature)
    own = (
        attn_ref[:, cols].astype(jnp.float32) + bout_ref[:, cols] + hid_ref[:, cols].astype(jnp.float32)
    )
    normed_ref[...] = ((own - center) * scale * gain_ref[:, cols] + shift_ref[:, cols]).astype(
        normed_ref.dtype
    )
    raised = jnp.dot(normed, wup_ref[...], preferred_element_type=jnp.float32) + bup_ref[...]
    inner = jax.nn.gelu(raised, approximate=True).astype(jnp.bfloat16)
    down_ref[...] = jnp.dot(inner, wdown_ref[...], preferred_element_type=jnp.float32).astype(
        jnp.bfloat16
    )


def feed_forward(attn, hidden, b_out, gain, shift, w_up, b_up, w_down, column, feature, block=256):
    tokens, model = hidden.shape
    units = w_up.shape[1]
    row = lambda i, c: (i, 0)
    fixed = lambda i, c: (0, 0)
    grid_spec = pltpu.PrefetchScalarGridSpec(
        num_scalar_prefetch=1,
        grid=(tokens // block,),
        in_specs=[
            pl.BlockSpec((block, model), row),
            pl.BlockSpec((block, model), row),
            pl.BlockSpec((1, model), fixed),
            pl.BlockSpec((1, model), fixed),
            pl.BlockSpec((1, model), fixed),
            pl.BlockSpec((model, units), fixed),
            pl.BlockSpec((1, units), fixed),
            pl.BlockSpec((units, model), fixed),
        ],
        out_specs=[
            pl.BlockSpec((block, feature), lambda i, c: (i, 0)),
            pl.BlockSpec((block, model), row),
        ],
    )
    return pl.pallas_call(
        ffn_block,
        grid_spec=grid_spec,
        out_shape=[
            jax.ShapeDtypeStruct((tokens, feature), jnp.bfloat16),
            jax.ShapeDtypeStruct((tokens, model), jnp.bfloat16),
        ],
    )(
        column,
        attn,
        hidden,
        b_out.reshape(1, -1),
        gain.reshape(1, -1),
        shift.reshape(1, -1),
        w_up,
        b_up.reshape(1, -1),
        w_down,
    )


def attend_block(where_ref, length_ref, query_ref, key_ref, value_ref, back_ref):
    slot = pl.program_id(0)
    length = length_ref[slot]
    draft = query_ref.shape[1]
    heads = query_ref.shape[2] // HD
    width = query_ref.shape[2]
    capacity = key_ref.shape[1]
    living = lax.broadcasted_iota(jnp.int32, (draft, capacity), 1) < length
    back_ref[0, draft:, :] = jnp.zeros((back_ref.shape[1] - draft, width), back_ref.dtype)
    for head in range(heads):
        cols = slice(head * HD, (head + 1) * HD)
        query = query_ref[0, :, cols]
        scores = lax.dot_general(
            query, key_ref[0, :, cols], (((1,), (1,)), ((), ())), preferred_element_type=jnp.float32
        ) * (1.0 / math.sqrt(HD))
        scores = jnp.where(living, scores, -jnp.inf)
        top = jnp.max(scores, axis=1, keepdims=True)
        weights = jnp.exp(scores - top)
        total = jnp.sum(weights, axis=1, keepdims=True)
        mixed = jnp.dot(weights.astype(jnp.bfloat16), value_ref[0, :, cols], preferred_element_type=jnp.float32)
        back_ref[0, :draft, cols] = (mixed / total).astype(back_ref.dtype)
        lse = jnp.broadcast_to(top + jnp.log(total), (draft, 128)).T[0:1, :draft]
        high = lse.astype(jnp.bfloat16)
        rest = lse - high.astype(jnp.float32)
        middle = rest.astype(jnp.bfloat16)
        low = (rest - middle.astype(jnp.float32)).astype(jnp.bfloat16)
        back_ref[0, draft + head : draft + head + 1, 0:draft] = high
        back_ref[0, draft + head : draft + head + 1, draft : 2 * draft] = middle
        back_ref[0, draft + head : draft + head + 1, 2 * draft : 3 * draft] = low

def attend(arrived, where, lengths, keys, values):
    positions, draft, width = arrived.shape
    slots, capacity, _ = keys.shape
    heads = width // HD
    rows = draft + heads
    grid_spec = pltpu.PrefetchScalarGridSpec(
        num_scalar_prefetch=2,
        grid=(slots,),
        in_specs=[
            pl.BlockSpec((1, draft, width), lambda s, w, n: (w[s], 0, 0)),
            pl.BlockSpec((1, capacity, width), lambda s, w, n: (s, 0, 0)),
            pl.BlockSpec((1, capacity, width), lambda s, w, n: (s, 0, 0)),
        ],
        out_specs=pl.BlockSpec((1, rows, width), lambda s, w, n: (w[s], 0, 0)),
    )
    return pl.pallas_call(
        attend_block,
        grid_spec=grid_spec,
        out_shape=jax.ShapeDtypeStruct((positions, rows, width), arrived.dtype),
    )(where, lengths, arrived, keys, values)


def project_block(where_ref, hidden_ref, weight_ref, bias_ref, query_ref, placed_ref):
    draft = placed_ref.shape[1]
    rows = (
        jnp.dot(hidden_ref[...], weight_ref[...], preferred_element_type=jnp.float32)
        + bias_ref[...]
    ).astype(query_ref.dtype)
    query_ref[...] = rows
    for request in range(query_ref.shape[0] // draft):
        placed_ref[where_ref[request]] = rows[request * draft : (request + 1) * draft]


def project(hidden, weight, bias, where, positions, draft):
    tokens, model = hidden.shape
    width = weight.shape[1]
    grid_spec = pltpu.PrefetchScalarGridSpec(
        num_scalar_prefetch=1,
        grid=(1,),
        in_specs=[
            pl.BlockSpec((tokens, model), lambda r, w: (0, 0)),
            pl.BlockSpec((model, width), lambda r, w: (0, 0)),
            pl.BlockSpec((1, width), lambda r, w: (0, 0)),
        ],
        out_specs=[
            pl.BlockSpec((tokens, width), lambda r, w: (0, 0)),
            pl.BlockSpec((positions, draft, width), lambda r, w: (0, 0, 0)),
        ],
    )
    return pl.pallas_call(
        project_block,
        grid_spec=grid_spec,
        out_shape=[
            jax.ShapeDtypeStruct((tokens, width), jnp.bfloat16),
            jax.ShapeDtypeStruct((positions, draft, width), jnp.bfloat16),
        ],
    )(where, hidden, weight, bias.reshape(1, -1))


def local(
    hidden,
    parents,
    owner_slot,
    slot_lengths,
    accepted_path,
    accepted_count,
    cache_keys,
    cache_values,
    w_query,
    b_query,
    w_key,
    w_value,
    b_value,
    w_out,
    b_out,
    first_gain,
    first_shift,
    w_up,
    b_up,
    w_down,
    b_down,
    second_gain,
    second_shift,
):
    requests = parents.shape[0]
    draft = parents.shape[1]
    tokens = hidden.shape[0]
    model_width = hidden.shape[1]
    width = w_query.shape[1]
    local_heads = width // HD
    capacity = cache_keys.shape[1]
    block = min(capacity, 256)
    shards = lax.axis_size("dp")
    myself = lax.axis_index("dp")
    scale = 1.0 / math.sqrt(HD)
    local_ids = jnp.arange(requests, dtype=jnp.int32)
    my_owner = lax.dynamic_slice_in_dim(owner_slot, myself * requests, requests)
    target = my_owner // requests
    earlier = local_ids[None, :] < local_ids[:, None]
    same_target = target[None, :] == target[:, None]
    rank = jnp.sum((earlier & same_target).astype(jnp.int32), axis=1)
    my_slots = myself * requests + local_ids
    every_id = jnp.arange(owner_slot.shape[0], dtype=jnp.int32)
    source_request = jnp.sum(
        jnp.where(owner_slot[None, :] == my_slots[:, None], every_id[None, :], 0), axis=1
    )
    source = source_request // requests
    source_local = source_request % requests
    source_targets = owner_slot.reshape(shards, requests)[source] // requests
    source_rank = jnp.sum(
        ((local_ids[None, :] < source_local[:, None]) & (source_targets == myself)).astype(
            jnp.int32
        ),
        axis=1,
    )
    slots_total = shards * PEER_MOST
    send_index = target * PEER_MOST + rank
    receive_index = source * PEER_MOST + source_rank
    queries, placed_queries = project(hidden, w_query, b_query, send_index, slots_total, draft)
    key_rows = jnp.dot(hidden, w_key, preferred_element_type=jnp.float32).astype(jnp.bfloat16)
    value_rows = (jnp.dot(hidden, w_value, preferred_element_type=jnp.float32) + b_value).astype(
        jnp.bfloat16
    )
    levels = jnp.arange(accepted_path.shape[1], dtype=jnp.int32)
    chosen = local_ids[:, None] * draft + accepted_path
    usable = (levels[None, :] < accepted_count[:, None])[..., None]
    kept_keys = jnp.where(usable, key_rows[chosen], jnp.zeros((), jnp.bfloat16))
    kept_values = jnp.where(usable, value_rows[chosen], jnp.zeros((), jnp.bfloat16))
    tree_queries = queries.reshape(requests, draft, local_heads, HD)
    tree_keys = key_rows.reshape(requests, draft, local_heads, HD)
    tree_values = value_rows.reshape(requests, draft, local_heads, HD)
    lineage = jax.vmap(lambda parent_row: ancestry(parent_row, draft))(parents)
    tree_scores = (
        jnp.einsum("rqhd,rkhd->rhqk", tree_queries, tree_keys, preferred_element_type=jnp.float32)
        * scale
    )
    tree_scores = jnp.where(lineage[:, None], tree_scores, -jnp.inf)
    tree_top = jnp.max(tree_scores, axis=3, keepdims=True)
    tree_exp = jnp.exp(tree_scores - tree_top)
    tree_total = jnp.sum(tree_exp, axis=3, keepdims=True)
    tree_probs = tree_exp.astype(jnp.bfloat16)
    tree_part = jnp.einsum(
        "rhqk,rkhd->rqhd", tree_probs, tree_values, preferred_element_type=jnp.float32
    ) / jnp.transpose(tree_total, (0, 2, 1, 3))
    tree_lse = jnp.transpose((tree_top + jnp.log(tree_total))[..., 0], (0, 2, 1))[..., None]
    slot_ids = jnp.arange(slots_total, dtype=jnp.int32)

    def spread(values, index):
        placing = (index[None, :] == slot_ids[:, None]).astype(values.dtype)
        flat = values.reshape(values.shape[0], -1)
        placed = jnp.dot(placing, flat, preferred_element_type=jnp.float32).astype(values.dtype)
        return placed.reshape((slots_total,) + values.shape[1:])

    arrived = lax.all_to_all(placed_queries, "dp", split_axis=0, concat_axis=0, tiled=True)
    kept = lax.all_to_all(
        spread(jnp.concatenate([kept_keys, kept_values], axis=1), send_index),
        "dp",
        split_axis=0,
        concat_axis=0,
        tiled=True,
    )[receive_index]
    new_keys = kept[:, : kept_keys.shape[1]]
    new_values = kept[:, kept_keys.shape[1] :]
    back = attend(arrived, receive_index, slot_lengths, cache_keys, cache_values)
    returned = lax.all_to_all(back, "dp", split_axis=0, concat_axis=0, tiled=True)[send_index]
    cache_part = returned[:, :draft]
    lse_rows = returned[:, draft : draft + local_heads].astype(jnp.float32)
    cache_lse = lse_rows[..., :draft] + (
        lse_rows[..., draft : 2 * draft] + lse_rows[..., 2 * draft : 3 * draft]
    )
    cache_weight = jnp.transpose(cache_lse, (0, 2, 1))[..., None]
    larger = jnp.maximum(cache_weight, tree_lse)
    cache_share = jnp.exp(cache_weight - larger)
    tree_share = jnp.exp(tree_lse - larger)
    blended = (
        cache_share * cache_part.astype(jnp.float32).reshape(requests, draft, local_heads, HD)
        + tree_share * tree_part
    ) / (cache_share + tree_share)
    attended = blended.astype(jnp.bfloat16).reshape(tokens, width)
    attention_term = jnp.dot(attended, w_out, preferred_element_type=jnp.float32)
    feature = model_width // lax.axis_size("head")
    offset = lax.axis_index("head") * feature

    def columns(values):
        return lax.dynamic_slice_in_dim(values, offset, feature, values.ndim - 1)

    attention_sum = lax.psum(attention_term.astype(jnp.bfloat16), "head")
    own_normed, down_part = feed_forward(
        attention_sum,
        hidden,
        b_out,
        first_gain,
        first_shift,
        w_up,
        b_up,
        w_down,
        lax.axis_index("head").reshape(1).astype(jnp.int32),
        feature,
    )
    down_share = lax.psum_scatter(
        down_part, "head", scatter_dimension=1, tiled=True
    ).astype(jnp.float32)
    second_mixed = down_share + columns(b_down) + own_normed.astype(jnp.float32)
    heads_along = lax.axis_size("head")
    own_sums = jnp.stack(
        [jnp.sum(second_mixed, axis=1), jnp.sum(second_mixed * second_mixed, axis=1)]
    )
    second_sums = jnp.sum(
        lax.all_to_all(
            jnp.broadcast_to(own_sums[None], (heads_along,) + own_sums.shape),
            "head",
            0,
            0,
            tiled=False,
        ),
        axis=0,
    )
    layer_out = normalize_shared(
        second_mixed, second_sums, columns(second_gain), columns(second_shift), model_width
    ).astype(jnp.bfloat16)
    return (layer_out, new_keys, new_values)


def solution(mesh):
    placed = (
        P("dp", None),
        P("dp", None),
        P(),
        P("dp"),
        P("dp", None),
        P("dp"),
        P("dp", None, "head"),
        P("dp", None, "head"),
        P(None, "head"),
        P("head"),
        P(None, "head"),
        P(None, "head"),
        P("head"),
        P("head", None),
        P(),
        P(),
        P(),
        P(None, "head"),
        P("head"),
        P("head", None),
        P(),
        P(),
        P(),
    )
    return jax.shard_map(
        local,
        mesh=mesh,
        in_specs=placed,
        out_specs=(P("dp", "head"), P("dp", None, "head"), P("dp", None, "head")),
        check_vma=False,
    )
```

```python
import math

import jax
import jax.numpy as jnp
from jax import lax
from jax.experimental import pallas as pl
from jax.experimental.pallas import tpu as pltpu
from jax.sharding import PartitionSpec as P

HD = 128
PEER_MOST = 2


EPSILON = 1e-05


def ancestry(parent_row, draft):
    nodes = jnp.arange(draft, dtype=jnp.int32)
    reach = (parent_row[:, None] == nodes[None, :]).astype(jnp.float32) + jnp.eye(
        draft, dtype=jnp.float32
    )
    for turn in range(max(1, draft.bit_length())):
        reach = jnp.minimum(jnp.dot(reach, reach, precision=lax.Precision.HIGHEST), 1.0)
    return reach > 0.5


def normalize(mixed, gain, shift):
    center = jnp.mean(mixed, axis=-1, keepdims=True)
    square = jnp.mean(mixed * mixed, axis=-1, keepdims=True)
    return (mixed - center) * lax.rsqrt(square - center * center + EPSILON) * gain + shift


def normalize_shared(mixed, sums, gain, shift, model_width):
    center = (sums[0] / model_width)[:, None]
    square = (sums[1] / model_width)[:, None]
    return (mixed - center) * lax.rsqrt(square - center * center + EPSILON) * gain + shift


def ffn_block(
    column_ref, attn_ref, hid_ref, bout_ref, gain_ref, shift_ref, wup_ref, bup_ref, wdown_ref,
    normed_ref, down_ref,
):
    mixed = attn_ref[...].astype(jnp.float32) + bout_ref[...] + hid_ref[...].astype(jnp.float32)
    center = jnp.mean(mixed, axis=-1, keepdims=True)
    square = jnp.mean(mixed * mixed, axis=-1, keepdims=True)
    scale = lax.rsqrt(square - center * center + EPSILON)
    normed = ((mixed - center) * scale * gain_ref[...] + shift_ref[...]).astype(jnp.bfloat16)
    feature = normed_ref.shape[1]
    start = pl.multiple_of(column_ref[0] * feature, feature)
    cols = pl.ds(start, feature)
    own = (
        attn_ref[:, cols].astype(jnp.float32) + bout_ref[:, cols] + hid_ref[:, cols].astype(jnp.float32)
    )
    normed_ref[...] = ((own - center) * scale * gain_ref[:, cols] + shift_ref[:, cols]).astype(
        normed_ref.dtype
    )
    raised = jnp.dot(normed, wup_ref[...], preferred_element_type=jnp.float32) + bup_ref[...]
    inner = jax.nn.gelu(raised, approximate=True).astype(jnp.bfloat16)
    down_ref[...] = jnp.dot(inner, wdown_ref[...], preferred_element_type=jnp.float32).astype(
        jnp.bfloat16
    )


def feed_forward(attn, hidden, b_out, gain, shift, w_up, b_up, w_down, column, feature, block=512):
    tokens, model = hidden.shape
    units = w_up.shape[1]
    row = lambda i, c: (i, 0)
    fixed = lambda i, c: (0, 0)
    grid_spec = pltpu.PrefetchScalarGridSpec(
        num_scalar_prefetch=1,
        grid=(tokens // block,),
        in_specs=[
            pl.BlockSpec((block, model), row),
            pl.BlockSpec((block, model), row),
            pl.BlockSpec((1, model), fixed),
            pl.BlockSpec((1, model), fixed),
            pl.BlockSpec((1, model), fixed),
            pl.BlockSpec((model, units), fixed),
            pl.BlockSpec((1, units), fixed),
            pl.BlockSpec((units, model), fixed),
        ],
        out_specs=[
            pl.BlockSpec((block, feature), lambda i, c: (i, 0)),
            pl.BlockSpec((block, model), row),
        ],
    )
    return pl.pallas_call(
        ffn_block,
        grid_spec=grid_spec,
        out_shape=[
            jax.ShapeDtypeStruct((tokens, feature), jnp.bfloat16),
            jax.ShapeDtypeStruct((tokens, model), jnp.bfloat16),
        ],
    )(
        column,
        attn,
        hidden,
        b_out.reshape(1, -1),
        gain.reshape(1, -1),
        shift.reshape(1, -1),
        w_up,
        b_up.reshape(1, -1),
        w_down,
    )


def attend_block(where_ref, length_ref, query_ref, key_ref, value_ref, back_ref):
    slot = pl.program_id(0)
    length = length_ref[slot]
    draft = query_ref.shape[1]
    heads = query_ref.shape[2] // HD
    width = query_ref.shape[2]
    capacity = key_ref.shape[1]
    living = lax.broadcasted_iota(jnp.int32, (draft, capacity), 1) < length
    back_ref[0, draft:, :] = jnp.zeros((back_ref.shape[1] - draft, width), back_ref.dtype)
    for head in range(heads):
        cols = slice(head * HD, (head + 1) * HD)
        query = query_ref[0, :, cols]
        scores = lax.dot_general(
            query, key_ref[0, :, cols], (((1,), (1,)), ((), ())), preferred_element_type=jnp.float32
        ) * (1.0 / math.sqrt(HD))
        scores = jnp.where(living, scores, -jnp.inf)
        top = jnp.max(scores, axis=1, keepdims=True)
        weights = jnp.exp(scores - top)
        total = jnp.sum(weights, axis=1, keepdims=True)
        mixed = jnp.dot(weights.astype(jnp.bfloat16), value_ref[0, :, cols], preferred_element_type=jnp.float32)
        back_ref[0, :draft, cols] = (mixed / total).astype(back_ref.dtype)
        lse = jnp.broadcast_to(top + jnp.log(total), (draft, 128)).T[0:1, :draft]
        high = lse.astype(jnp.bfloat16)
        rest = lse - high.astype(jnp.float32)
        middle = rest.astype(jnp.bfloat16)
        low = (rest - middle.astype(jnp.float32)).astype(jnp.bfloat16)
        back_ref[0, draft + head : draft + head + 1, 0:draft] = high
        back_ref[0, draft + head : draft + head + 1, draft : 2 * draft] = middle
        back_ref[0, draft + head : draft + head + 1, 2 * draft : 3 * draft] = low

def attend(arrived, where, lengths, keys, values):
    positions, draft, width = arrived.shape
    slots, capacity, _ = keys.shape
    heads = width // HD
    rows = draft + heads
    grid_spec = pltpu.PrefetchScalarGridSpec(
        num_scalar_prefetch=2,
        grid=(slots,),
        in_specs=[
            pl.BlockSpec((1, draft, width), lambda s, w, n: (w[s], 0, 0)),
            pl.BlockSpec((1, capacity, width), lambda s, w, n: (s, 0, 0)),
            pl.BlockSpec((1, capacity, width), lambda s, w, n: (s, 0, 0)),
        ],
        out_specs=pl.BlockSpec((1, rows, width), lambda s, w, n: (w[s], 0, 0)),
    )
    return pl.pallas_call(
        attend_block,
        grid_spec=grid_spec,
        out_shape=jax.ShapeDtypeStruct((positions, rows, width), arrived.dtype),
    )(where, lengths, arrived, keys, values)


def project_block(where_ref, hidden_ref, weight_ref, bias_ref, query_ref, placed_ref):
    draft = placed_ref.shape[1]
    rows = (
        jnp.dot(hidden_ref[...], weight_ref[...], preferred_element_type=jnp.float32)
        + bias_ref[...]
    ).astype(query_ref.dtype)
    query_ref[...] = rows
    for request in range(query_ref.shape[0] // draft):
        placed_ref[where_ref[request]] = rows[request * draft : (request + 1) * draft]


def project(hidden, weight, bias, where, positions, draft):
    tokens, model = hidden.shape
    width = weight.shape[1]
    grid_spec = pltpu.PrefetchScalarGridSpec(
        num_scalar_prefetch=1,
        grid=(1,),
        in_specs=[
            pl.BlockSpec((tokens, model), lambda r, w: (0, 0)),
            pl.BlockSpec((model, width), lambda r, w: (0, 0)),
            pl.BlockSpec((1, width), lambda r, w: (0, 0)),
        ],
        out_specs=[
            pl.BlockSpec((tokens, width), lambda r, w: (0, 0)),
            pl.BlockSpec((positions, draft, width), lambda r, w: (0, 0, 0)),
        ],
    )
    return pl.pallas_call(
        project_block,
        grid_spec=grid_spec,
        out_shape=[
            jax.ShapeDtypeStruct((tokens, width), jnp.bfloat16),
            jax.ShapeDtypeStruct((positions, draft, width), jnp.bfloat16),
        ],
    )(where, hidden, weight, bias.reshape(1, -1))


def local(
    hidden,
    parents,
    owner_slot,
    slot_lengths,
    accepted_path,
    accepted_count,
    cache_keys,
    cache_values,
    w_query,
    b_query,
    w_key,
    w_value,
    b_value,
    w_out,
    b_out,
    first_gain,
    first_shift,
    w_up,
    b_up,
    w_down,
    b_down,
    second_gain,
    second_shift,
):
    requests = parents.shape[0]
    draft = parents.shape[1]
    tokens = hidden.shape[0]
    model_width = hidden.shape[1]
    width = w_query.shape[1]
    local_heads = width // HD
    capacity = cache_keys.shape[1]
    block = min(capacity, 256)
    shards = lax.axis_size("dp")
    myself = lax.axis_index("dp")
    scale = 1.0 / math.sqrt(HD)
    local_ids = jnp.arange(requests, dtype=jnp.int32)
    my_owner = lax.dynamic_slice_in_dim(owner_slot, myself * requests, requests)
    target = my_owner // requests
    earlier = local_ids[None, :] < local_ids[:, None]
    same_target = target[None, :] == target[:, None]
    rank = jnp.sum((earlier & same_target).astype(jnp.int32), axis=1)
    my_slots = myself * requests + local_ids
    every_id = jnp.arange(owner_slot.shape[0], dtype=jnp.int32)
    source_request = jnp.sum(
        jnp.where(owner_slot[None, :] == my_slots[:, None], every_id[None, :], 0), axis=1
    )
    source = source_request // requests
    source_local = source_request % requests
    source_targets = owner_slot.reshape(shards, requests)[source] // requests
    source_rank = jnp.sum(
        ((local_ids[None, :] < source_local[:, None]) & (source_targets == myself)).astype(
            jnp.int32
        ),
        axis=1,
    )
    slots_total = shards * PEER_MOST
    send_index = target * PEER_MOST + rank
    receive_index = source * PEER_MOST + source_rank
    queries, placed_queries = project(hidden, w_query, b_query, send_index, slots_total, draft)
    key_rows = jnp.dot(hidden, w_key, preferred_element_type=jnp.float32).astype(jnp.bfloat16)
    value_rows = (jnp.dot(hidden, w_value, preferred_element_type=jnp.float32) + b_value).astype(
        jnp.bfloat16
    )
    levels = jnp.arange(accepted_path.shape[1], dtype=jnp.int32)
    chosen = local_ids[:, None] * draft + accepted_path
    usable = (levels[None, :] < accepted_count[:, None])[..., None]
    kept_keys = jnp.where(usable, key_rows[chosen], jnp.zeros((), jnp.bfloat16))
    kept_values = jnp.where(usable, value_rows[chosen], jnp.zeros((), jnp.bfloat16))
    tree_queries = queries.reshape(requests, draft, local_heads, HD)
    tree_keys = key_rows.reshape(requests, draft, local_heads, HD)
    tree_values = value_rows.reshape(requests, draft, local_heads, HD)
    lineage = jax.vmap(lambda parent_row: ancestry(parent_row, draft))(parents)
    tree_scores = (
        jnp.einsum("rqhd,rkhd->rhqk", tree_queries, tree_keys, preferred_element_type=jnp.float32)
        * scale
    )
    tree_scores = jnp.where(lineage[:, None], tree_scores, -jnp.inf)
    tree_top = jnp.max(tree_scores, axis=3, keepdims=True)
    tree_exp = jnp.exp(tree_scores - tree_top)
    tree_total = jnp.sum(tree_exp, axis=3, keepdims=True)
    tree_probs = tree_exp.astype(jnp.bfloat16)
    tree_part = jnp.einsum(
        "rhqk,rkhd->rqhd", tree_probs, tree_values, preferred_element_type=jnp.float32
    ) / jnp.transpose(tree_total, (0, 2, 1, 3))
    tree_lse = jnp.transpose((tree_top + jnp.log(tree_total))[..., 0], (0, 2, 1))[..., None]
    slot_ids = jnp.arange(slots_total, dtype=jnp.int32)

    def spread(values, index):
        placing = (index[None, :] == slot_ids[:, None]).astype(values.dtype)
        flat = values.reshape(values.shape[0], -1)
        placed = jnp.dot(placing, flat, preferred_element_type=jnp.float32).astype(values.dtype)
        return placed.reshape((slots_total,) + values.shape[1:])

    arrived = lax.all_to_all(placed_queries, "dp", split_axis=0, concat_axis=0, tiled=True)
    kept = lax.all_to_all(
        spread(jnp.concatenate([kept_keys, kept_values], axis=1), send_index),
        "dp",
        split_axis=0,
        concat_axis=0,
        tiled=True,
    )[receive_index]
    new_keys = kept[:, : kept_keys.shape[1]]
    new_values = kept[:, kept_keys.shape[1] :]
    back = attend(arrived, receive_index, slot_lengths, cache_keys, cache_values)
    returned = lax.all_to_all(back, "dp", split_axis=0, concat_axis=0, tiled=True)[send_index]
    cache_part = returned[:, :draft]
    lse_rows = returned[:, draft : draft + local_heads].astype(jnp.float32)
    cache_lse = lse_rows[..., :draft] + (
        lse_rows[..., draft : 2 * draft] + lse_rows[..., 2 * draft : 3 * draft]
    )
    cache_weight = jnp.transpose(cache_lse, (0, 2, 1))[..., None]
    larger = jnp.maximum(cache_weight, tree_lse)
    cache_share = jnp.exp(cache_weight - larger)
    tree_share = jnp.exp(tree_lse - larger)
    blended = (
        cache_share * cache_part.astype(jnp.float32).reshape(requests, draft, local_heads, HD)
        + tree_share * tree_part
    ) / (cache_share + tree_share)
    attended = blended.astype(jnp.bfloat16).reshape(tokens, width)
    attention_term = jnp.dot(attended, w_out, preferred_element_type=jnp.float32)
    feature = model_width // lax.axis_size("head")
    offset = lax.axis_index("head") * feature

    def columns(values):
        return lax.dynamic_slice_in_dim(values, offset, feature, values.ndim - 1)

    attention_sum = lax.psum(attention_term.astype(jnp.bfloat16), "head")
    own_normed, down_part = feed_forward(
        attention_sum,
        hidden,
        b_out,
        first_gain,
        first_shift,
        w_up,
        b_up,
        w_down,
        lax.axis_index("head").reshape(1).astype(jnp.int32),
        feature,
    )
    down_share = lax.psum_scatter(
        down_part, "head", scatter_dimension=1, tiled=True
    ).astype(jnp.float32)
    second_mixed = down_share + columns(b_down) + own_normed.astype(jnp.float32)
    heads_along = lax.axis_size("head")
    own_sums = jnp.stack(
        [jnp.sum(second_mixed, axis=1), jnp.sum(second_mixed * second_mixed, axis=1)]
    )
    second_sums = jnp.sum(
        lax.all_to_all(
            jnp.broadcast_to(own_sums[None], (heads_along,) + own_sums.shape),
            "head",
            0,
            0,
            tiled=False,
        ),
        axis=0,
    )
    layer_out = normalize_shared(
        second_mixed, second_sums, columns(second_gain), columns(second_shift), model_width
    ).astype(jnp.bfloat16)
    return (layer_out, new_keys, new_values)


def solution(mesh):
    placed = (
        P("dp", None),
        P("dp", None),
        P(),
        P("dp"),
        P("dp", None),
        P("dp"),
        P("dp", None, "head"),
        P("dp", None, "head"),
        P(None, "head"),
        P("head"),
        P(None, "head"),
        P(None, "head"),
        P("head"),
        P("head", None),
        P(),
        P(),
        P(),
        P(None, "head"),
        P("head"),
        P("head", None),
        P(),
        P(),
        P(),
    )
    return jax.shard_map(
        local,
        mesh=mesh,
        in_specs=placed,
        out_specs=(P("dp", "head"), P("dp", None, "head"), P("dp", None, "head")),
        check_vma=False,
    )
```

```python
import math

import jax
import jax.numpy as jnp
from jax import lax
from jax.experimental import pallas as pl
from jax.experimental.pallas import tpu as pltpu
from jax.sharding import PartitionSpec as P

HD = 128
PEER_MOST = 2


EPSILON = 1e-05


def ancestry(parent_row, draft):
    nodes = jnp.arange(draft, dtype=jnp.int32)
    reach = (parent_row[:, None] == nodes[None, :]).astype(jnp.float32) + jnp.eye(
        draft, dtype=jnp.float32
    )
    for turn in range(max(1, draft.bit_length())):
        reach = jnp.minimum(jnp.dot(reach, reach, precision=lax.Precision.HIGHEST), 1.0)
    return reach > 0.5


def normalize(mixed, gain, shift):
    center = jnp.mean(mixed, axis=-1, keepdims=True)
    square = jnp.mean(mixed * mixed, axis=-1, keepdims=True)
    return (mixed - center) * lax.rsqrt(square - center * center + EPSILON) * gain + shift


def normalize_shared(mixed, sums, gain, shift, model_width):
    center = (sums[0] / model_width)[:, None]
    square = (sums[1] / model_width)[:, None]
    return (mixed - center) * lax.rsqrt(square - center * center + EPSILON) * gain + shift


def ffn_block(
    column_ref, attn_ref, hid_ref, bout_ref, gain_ref, shift_ref, wup_ref, bup_ref, wdown_ref,
    normed_ref, down_ref,
):
    mixed = attn_ref[...].astype(jnp.float32) + bout_ref[...] + hid_ref[...].astype(jnp.float32)
    center = jnp.mean(mixed, axis=-1, keepdims=True)
    square = jnp.mean(mixed * mixed, axis=-1, keepdims=True)
    scale = lax.rsqrt(square - center * center + EPSILON)
    normed = ((mixed - center) * scale * gain_ref[...] + shift_ref[...]).astype(jnp.bfloat16)
    feature = normed_ref.shape[1]
    start = pl.multiple_of(column_ref[0] * feature, feature)
    cols = pl.ds(start, feature)
    own = (
        attn_ref[:, cols].astype(jnp.float32) + bout_ref[:, cols] + hid_ref[:, cols].astype(jnp.float32)
    )
    normed_ref[...] = ((own - center) * scale * gain_ref[:, cols] + shift_ref[:, cols]).astype(
        normed_ref.dtype
    )
    raised = jnp.dot(normed, wup_ref[...], preferred_element_type=jnp.float32) + bup_ref[...]
    inner = jax.nn.gelu(raised, approximate=True).astype(jnp.bfloat16)
    down_ref[...] = jnp.dot(inner, wdown_ref[...], preferred_element_type=jnp.float32).astype(
        jnp.bfloat16
    )


def feed_forward(attn, hidden, b_out, gain, shift, w_up, b_up, w_down, column, feature, block=128):
    tokens, model = hidden.shape
    units = w_up.shape[1]
    row = lambda i, c: (i, 0)
    fixed = lambda i, c: (0, 0)
    grid_spec = pltpu.PrefetchScalarGridSpec(
        num_scalar_prefetch=1,
        grid=(tokens // block,),
        in_specs=[
            pl.BlockSpec((block, model), row),
            pl.BlockSpec((block, model), row),
            pl.BlockSpec((1, model), fixed),
            pl.BlockSpec((1, model), fixed),
            pl.BlockSpec((1, model), fixed),
            pl.BlockSpec((model, units), fixed),
            pl.BlockSpec((1, units), fixed),
            pl.BlockSpec((units, model), fixed),
        ],
        out_specs=[
            pl.BlockSpec((block, feature), lambda i, c: (i, 0)),
            pl.BlockSpec((block, model), row),
        ],
    )
    return pl.pallas_call(
        ffn_block,
        grid_spec=grid_spec,
        out_shape=[
            jax.ShapeDtypeStruct((tokens, feature), jnp.bfloat16),
            jax.ShapeDtypeStruct((tokens, model), jnp.bfloat16),
        ],
    )(
        column,
        attn,
        hidden,
        b_out.reshape(1, -1),
        gain.reshape(1, -1),
        shift.reshape(1, -1),
        w_up,
        b_up.reshape(1, -1),
        w_down,
    )


def attend_block(where_ref, length_ref, query_ref, key_ref, value_ref, back_ref):
    slot = pl.program_id(0)
    length = length_ref[slot]
    draft = query_ref.shape[1]
    heads = query_ref.shape[2] // HD
    width = query_ref.shape[2]
    capacity = key_ref.shape[1]
    living = lax.broadcasted_iota(jnp.int32, (draft, capacity), 1) < length
    back_ref[0, draft:, :] = jnp.zeros((back_ref.shape[1] - draft, width), back_ref.dtype)
    for head in range(heads):
        cols = slice(head * HD, (head + 1) * HD)
        query = query_ref[0, :, cols]
        scores = lax.dot_general(
            query, key_ref[0, :, cols], (((1,), (1,)), ((), ())), preferred_element_type=jnp.float32
        ) * (1.0 / math.sqrt(HD))
        scores = jnp.where(living, scores, -jnp.inf)
        top = jnp.max(scores, axis=1, keepdims=True)
        weights = jnp.exp(scores - top)
        total = jnp.sum(weights, axis=1, keepdims=True)
        mixed = jnp.dot(weights.astype(jnp.bfloat16), value_ref[0, :, cols], preferred_element_type=jnp.float32)
        back_ref[0, :draft, cols] = (mixed / total).astype(back_ref.dtype)
        lse = jnp.broadcast_to(top + jnp.log(total), (draft, 128)).T[0:1, :draft]
        high = lse.astype(jnp.bfloat16)
        rest = lse - high.astype(jnp.float32)
        middle = rest.astype(jnp.bfloat16)
        low = (rest - middle.astype(jnp.float32)).astype(jnp.bfloat16)
        back_ref[0, draft + head : draft + head + 1, 0:draft] = high
        back_ref[0, draft + head : draft + head + 1, draft : 2 * draft] = middle
        back_ref[0, draft + head : draft + head + 1, 2 * draft : 3 * draft] = low

def attend(arrived, where, lengths, keys, values):
    positions, draft, width = arrived.shape
    slots, capacity, _ = keys.shape
    heads = width // HD
    rows = draft + heads
    grid_spec = pltpu.PrefetchScalarGridSpec(
        num_scalar_prefetch=2,
        grid=(slots,),
        in_specs=[
            pl.BlockSpec((1, draft, width), lambda s, w, n: (w[s], 0, 0)),
            pl.BlockSpec((1, capacity, width), lambda s, w, n: (s, 0, 0)),
            pl.BlockSpec((1, capacity, width), lambda s, w, n: (s, 0, 0)),
        ],
        out_specs=pl.BlockSpec((1, rows, width), lambda s, w, n: (w[s], 0, 0)),
    )
    return pl.pallas_call(
        attend_block,
        grid_spec=grid_spec,
        out_shape=jax.ShapeDtypeStruct((positions, rows, width), arrived.dtype),
    )(where, lengths, arrived, keys, values)


def project_block(where_ref, hidden_ref, weight_ref, bias_ref, query_ref, placed_ref):
    draft = placed_ref.shape[1]
    rows = (
        jnp.dot(hidden_ref[...], weight_ref[...], preferred_element_type=jnp.float32)
        + bias_ref[...]
    ).astype(query_ref.dtype)
    query_ref[...] = rows
    for request in range(query_ref.shape[0] // draft):
        placed_ref[where_ref[request]] = rows[request * draft : (request + 1) * draft]


def project(hidden, weight, bias, where, positions, draft):
    tokens, model = hidden.shape
    width = weight.shape[1]
    grid_spec = pltpu.PrefetchScalarGridSpec(
        num_scalar_prefetch=1,
        grid=(1,),
        in_specs=[
            pl.BlockSpec((tokens, model), lambda r, w: (0, 0)),
            pl.BlockSpec((model, width), lambda r, w: (0, 0)),
            pl.BlockSpec((1, width), lambda r, w: (0, 0)),
        ],
        out_specs=[
            pl.BlockSpec((tokens, width), lambda r, w: (0, 0)),
            pl.BlockSpec((positions, draft, width), lambda r, w: (0, 0, 0)),
        ],
    )
    return pl.pallas_call(
        project_block,
        grid_spec=grid_spec,
        out_shape=[
            jax.ShapeDtypeStruct((tokens, width), jnp.bfloat16),
            jax.ShapeDtypeStruct((positions, draft, width), jnp.bfloat16),
        ],
    )(where, hidden, weight, bias.reshape(1, -1))


def local(
    hidden,
    parents,
    owner_slot,
    slot_lengths,
    accepted_path,
    accepted_count,
    cache_keys,
    cache_values,
    w_query,
    b_query,
    w_key,
    w_value,
    b_value,
    w_out,
    b_out,
    first_gain,
    first_shift,
    w_up,
    b_up,
    w_down,
    b_down,
    second_gain,
    second_shift,
):
    requests = parents.shape[0]
    draft = parents.shape[1]
    tokens = hidden.shape[0]
    model_width = hidden.shape[1]
    width = w_query.shape[1]
    local_heads = width // HD
    capacity = cache_keys.shape[1]
    block = min(capacity, 256)
    shards = lax.axis_size("dp")
    myself = lax.axis_index("dp")
    scale = 1.0 / math.sqrt(HD)
    local_ids = jnp.arange(requests, dtype=jnp.int32)
    my_owner = lax.dynamic_slice_in_dim(owner_slot, myself * requests, requests)
    target = my_owner // requests
    earlier = local_ids[None, :] < local_ids[:, None]
    same_target = target[None, :] == target[:, None]
    rank = jnp.sum((earlier & same_target).astype(jnp.int32), axis=1)
    my_slots = myself * requests + local_ids
    every_id = jnp.arange(owner_slot.shape[0], dtype=jnp.int32)
    source_request = jnp.sum(
        jnp.where(owner_slot[None, :] == my_slots[:, None], every_id[None, :], 0), axis=1
    )
    source = source_request // requests
    source_local = source_request % requests
    source_targets = owner_slot.reshape(shards, requests)[source] // requests
    source_rank = jnp.sum(
        ((local_ids[None, :] < source_local[:, None]) & (source_targets == myself)).astype(
            jnp.int32
        ),
        axis=1,
    )
    slots_total = shards * PEER_MOST
    send_index = target * PEER_MOST + rank
    receive_index = source * PEER_MOST + source_rank
    queries, placed_queries = project(hidden, w_query, b_query, send_index, slots_total, draft)
    key_rows = jnp.dot(hidden, w_key, preferred_element_type=jnp.float32).astype(jnp.bfloat16)
    value_rows = (jnp.dot(hidden, w_value, preferred_element_type=jnp.float32) + b_value).astype(
        jnp.bfloat16
    )
    levels = jnp.arange(accepted_path.shape[1], dtype=jnp.int32)
    chosen = local_ids[:, None] * draft + accepted_path
    usable = (levels[None, :] < accepted_count[:, None])[..., None]
    kept_keys = jnp.where(usable, key_rows[chosen], jnp.zeros((), jnp.bfloat16))
    kept_values = jnp.where(usable, value_rows[chosen], jnp.zeros((), jnp.bfloat16))
    tree_queries = queries.reshape(requests, draft, local_heads, HD)
    tree_keys = key_rows.reshape(requests, draft, local_heads, HD)
    tree_values = value_rows.reshape(requests, draft, local_heads, HD)
    lineage = jax.vmap(lambda parent_row: ancestry(parent_row, draft))(parents)
    tree_scores = (
        jnp.einsum("rqhd,rkhd->rhqk", tree_queries, tree_keys, preferred_element_type=jnp.float32)
        * scale
    )
    tree_scores = jnp.where(lineage[:, None], tree_scores, -jnp.inf)
    tree_top = jnp.max(tree_scores, axis=3, keepdims=True)
    tree_exp = jnp.exp(tree_scores - tree_top)
    tree_total = jnp.sum(tree_exp, axis=3, keepdims=True)
    tree_probs = tree_exp.astype(jnp.bfloat16)
    tree_part = jnp.einsum(
        "rhqk,rkhd->rqhd", tree_probs, tree_values, preferred_element_type=jnp.float32
    ) / jnp.transpose(tree_total, (0, 2, 1, 3))
    tree_lse = jnp.transpose((tree_top + jnp.log(tree_total))[..., 0], (0, 2, 1))[..., None]
    slot_ids = jnp.arange(slots_total, dtype=jnp.int32)

    def spread(values, index):
        placing = (index[None, :] == slot_ids[:, None]).astype(values.dtype)
        flat = values.reshape(values.shape[0], -1)
        placed = jnp.dot(placing, flat, preferred_element_type=jnp.float32).astype(values.dtype)
        return placed.reshape((slots_total,) + values.shape[1:])

    arrived = lax.all_to_all(placed_queries, "dp", split_axis=0, concat_axis=0, tiled=True)
    kept = lax.all_to_all(
        spread(jnp.concatenate([kept_keys, kept_values], axis=1), send_index),
        "dp",
        split_axis=0,
        concat_axis=0,
        tiled=True,
    )[receive_index]
    new_keys = kept[:, : kept_keys.shape[1]]
    new_values = kept[:, kept_keys.shape[1] :]
    back = attend(arrived, receive_index, slot_lengths, cache_keys, cache_values)
    returned = lax.all_to_all(back, "dp", split_axis=0, concat_axis=0, tiled=True)[send_index]
    cache_part = returned[:, :draft]
    lse_rows = returned[:, draft : draft + local_heads].astype(jnp.float32)
    cache_lse = lse_rows[..., :draft] + (
        lse_rows[..., draft : 2 * draft] + lse_rows[..., 2 * draft : 3 * draft]
    )
    cache_weight = jnp.transpose(cache_lse, (0, 2, 1))[..., None]
    larger = jnp.maximum(cache_weight, tree_lse)
    cache_share = jnp.exp(cache_weight - larger)
    tree_share = jnp.exp(tree_lse - larger)
    blended = (
        cache_share * cache_part.astype(jnp.float32).reshape(requests, draft, local_heads, HD)
        + tree_share * tree_part
    ) / (cache_share + tree_share)
    attended = blended.astype(jnp.bfloat16).reshape(tokens, width)
    attention_term = jnp.dot(attended, w_out, preferred_element_type=jnp.float32)
    feature = model_width // lax.axis_size("head")
    offset = lax.axis_index("head") * feature

    def columns(values):
        return lax.dynamic_slice_in_dim(values, offset, feature, values.ndim - 1)

    attention_sum = lax.psum(attention_term.astype(jnp.bfloat16), "head")
    own_normed, down_part = feed_forward(
        attention_sum,
        hidden,
        b_out,
        first_gain,
        first_shift,
        w_up,
        b_up,
        w_down,
        lax.axis_index("head").reshape(1).astype(jnp.int32),
        feature,
    )
    down_share = lax.psum_scatter(
        down_part, "head", scatter_dimension=1, tiled=True
    ).astype(jnp.float32)
    second_mixed = down_share + columns(b_down) + own_normed.astype(jnp.float32)
    heads_along = lax.axis_size("head")
    own_sums = jnp.stack(
        [jnp.sum(second_mixed, axis=1), jnp.sum(second_mixed * second_mixed, axis=1)]
    )
    second_sums = jnp.sum(
        lax.all_to_all(
            jnp.broadcast_to(own_sums[None], (heads_along,) + own_sums.shape),
            "head",
            0,
            0,
            tiled=False,
        ),
        axis=0,
    )
    layer_out = normalize_shared(
        second_mixed, second_sums, columns(second_gain), columns(second_shift), model_width
    ).astype(jnp.bfloat16)
    return (layer_out, new_keys, new_values)


def solution(mesh):
    placed = (
        P("dp", None),
        P("dp", None),
        P(),
        P("dp"),
        P("dp", None),
        P("dp"),
        P("dp", None, "head"),
        P("dp", None, "head"),
        P(None, "head"),
        P("head"),
        P(None, "head"),
        P(None, "head"),
        P("head"),
        P("head", None),
        P(),
        P(),
        P(),
        P(None, "head"),
        P("head"),
        P("head", None),
        P(),
        P(),
        P(),
    )
    return jax.shard_map(
        local,
        mesh=mesh,
        in_specs=placed,
        out_specs=(P("dp", "head"), P("dp", None, "head"), P("dp", None, "head")),
        check_vma=False,
    )
```
